32 devices in a mesh: groups: 2 (over y), lon: 4 (over z), chan: 2 (over x), lat: 2 (over core).
Axes of the slice: x: 2, y: 2, z: 4, core: 2. Of those that a mesh axis runs over, the one named last changes fastest.
Arguments:
- inputs: bfloat16 [256, 64, 512], P('chan', ('groups', 'lat'), 'lon'), parts along dimension 1, may hold values from -6 to 6
- cotangent: bfloat16 [256, 64, 512], P('chan', ('groups', 'lat'), 'lon'), parts along dimension 1, may hold values from -6 to 6
- weight: bfloat16 [3, 3, 256, 256], P(None, None, 'chan'), may hold values from -0.125 to 0.125
- bias_vector: float32 [256], P('chan'), may hold values from -4 to 4
Outputs:
- input_grad: bfloat16 [256, 64, 512], P('chan', ('groups', 'lat'), 'lon'), parts along dimension 1
- weight_grad: float32 [6, 3, 256, 256], P('groups', None, 'chan'), parts along dimension 0
- bias_grad: float32 [512], P(('groups', 'chan')), parts along dimension 0
The draws below stay inside these ranges and needn't reach their ends.
There are 2 independent parts, one for each index of `groups`. The reference program is written for one: setup_inputs(seed, part) draws one part's arguments, and reference() takes and returns one part's arrays. A program takes and returns all parts, laid end to end along the dimension named above; an argument that names none is the same for every part. Nothing has to cross between parts.
All inputs are finite; a program needn't handle non-finite values.
Results may differ from the reference program's by a relative error of at most 0.007.
Values may be sent and summed in bfloat16 or wider, within the bound.
No kernel may reach another device: no remote copies, remote signals or barrier semaphores. Data moves between devices by JAX's collectives and lax.ppermute only.
A program may use at most 64 MiB of HBM per device.

```python
import jax
import jax.numpy as jnp
from jax import lax

C = 256
HEIGHT = 32
WIDTH = 512


def level_of(rng, shape, shards, low, high):
    def one(axis_at, blocks):
        draws = jax.random.uniform(jax.random.fold_in(jax.random.fold_in(rng, 6), axis_at), (blocks,), jnp.float32, low / len(shards), high / len(shards))
        return jnp.repeat(jnp.exp(draws), shape[axis_at] // blocks).reshape((-1,) + (1,) * (len(shape) - axis_at - 1))

    gain = one(*shards[0])
    for cut in shards[1:]:
        gain = gain * one(*cut)
    return gain


def bell_draw(key, extent, scale, bound, cuts=(), held_as=jnp.bfloat16):
    result = jax.random.normal(key, extent, jnp.float32) * scale
    if len(cuts) > 0:
        result = level_of(key, extent, cuts, -0.22, 0.18) * result
    return jnp.clip(result, min=-bound, max=bound).astype(held_as)


def setup_inputs(seed: int = 0, part: int = 0) -> dict:
    key_of = jax.random.split(jax.random.key(seed), 5)
    own_keys = jax.random.split(jax.random.fold_in(key_of[4], part), 5)
    return {
        "inputs": bell_draw(own_keys[0], (C, HEIGHT, WIDTH), 1.0, 6.0, ((0, 2), (1, 2), (2, 4))),
        "cotangent": bell_draw(own_keys[1], (C, HEIGHT, WIDTH), 1.0, 6.0, ((0, 2), (1, 2), (2, 4))),
        "weight": bell_draw(key_of[2], (3, 3, C, C), (9 * C) ** -0.5, 0.125, ((2, 2),)),
        "bias_vector": bell_draw(key_of[3], (C,), 1.0, 4.0, ((0, 2),), jnp.float32),
    }


def pad_field(field):
    wrapped = jnp.concatenate([field[:, :, -1:], field, field[:, :, :1]], axis=2)
    return jnp.pad(wrapped, ((0, 0), (1, 1), (0, 0)))


def gelu_slope(preact):
    normal_cdf = 0.5 * (1.0 + jax.scipy.special.erf(preact * 0.7071067811865476))
    density = jnp.exp(-0.5 * preact * preact) * 0.3989422804014327
    return normal_cdf + preact * density


def reference(inputs, cotangent, weight, bias_vector):
    channels, height, breadth = inputs.shape
    padded = pad_field(inputs).astype(jnp.float32)
    kernel = weight.astype(jnp.float32)
    preact = jnp.zeros((channels, height * breadth), jnp.float32)
    for tap_row in range(3):
        for tap_col in range(3):
            window = padded[:, tap_row:tap_row + height, tap_col:tap_col + breadth].reshape(channels, -1)
            preact = preact + jnp.dot(kernel[tap_row, tap_col], window, precision=lax.Precision.HIGHEST)
    preact = preact + bias_vector[:, None]
    upstream = cotangent.reshape(channels, -1).astype(jnp.float32)
    grad_pre = (upstream * gelu_slope(preact)).astype(jnp.bfloat16)
    grad_wide = grad_pre.astype(jnp.float32)
    bias_grad = jnp.sum(grad_wide, axis=1)
    taps = []
    for tap_row in range(3):
        row_taps = []
        for tap_col in range(3):
            window = padded[:, tap_row:tap_row + height, tap_col:tap_col + breadth].reshape(channels, -1)
            row_taps.append(lax.dot_general(grad_wide, window, (((1,), (1,)), ((), ())), precision=lax.Precision.HIGHEST))
        taps.append(jnp.stack(row_taps))
    weight_grad = jnp.stack(taps)
    grad_padded = pad_field(grad_pre.reshape(channels, height, breadth)).astype(jnp.float32)
    summed = jnp.zeros((channels, height * breadth), jnp.float32)
    for tap_row in range(3):
        for tap_col in range(3):
            window = grad_padded[:, 2 - tap_row:2 - tap_row + height, 2 - tap_col:2 - tap_col + breadth].reshape(channels, -1)
            summed = summed + lax.dot_general(kernel[tap_row, tap_col], window, (((0,), (0,)), ((), ())), precision=lax.Precision.HIGHEST)
    input_grad = summed.astype(jnp.bfloat16).reshape(channels, height, breadth)
    return input_grad, weight_grad, bias_grad
```

```python
import jax
import jax.numpy as jnp
from jax import lax
from jax.sharding import PartitionSpec as P


def padded_2(shard, sides, width):
    for axis, dim in sides:
        devices, length = (lax.axis_size(axis), shard.shape[dim])
        up = [(i, (i + 1) % devices) for i in range(devices)]
        down = [(j, i) for i, j in up]
        last = lax.slice_in_dim(shard, length - width, length, axis=dim)
        initial = lax.slice_in_dim(shard, 0, width, axis=dim)
        before = lax.ppermute(last, axis, up)
        after = lax.ppermute(initial, axis, down)
        shard = jnp.concatenate([before, shard, after], axis=dim)
    return shard


def gelu_slope(preact):
    normal_cdf = 0.5 * (1.0 + jax.scipy.special.erf(preact * 0.7071067811865476))
    density = jnp.exp(-0.5 * preact * preact) * 0.3989422804014327
    return normal_cdf + preact * density


def mask_rims(padded):
    lat_index = lax.axis_index("lat")
    band_count = lax.axis_size("lat")
    row_ids = jnp.arange(padded.shape[1])
    outside = (row_ids == 0) & (lat_index == 0) | (row_ids == padded.shape[1] - 1) & (
        lat_index == band_count - 1
    )
    return jnp.where(outside[None, :, None], jnp.zeros((), padded.dtype), padded)


def window_of(field, first_row, first_col, row_count, column_count):
    return field[
        :, first_row : first_row + row_count, first_col : first_col + column_count
    ].reshape(field.shape[0], -1)


def conv_taps(kernel, field, row_count, column_count, flip):
    total = None
    for tap_row in range(3):
        for tap_col in range(3):
            if flip:
                window = window_of(field, 2 - tap_row, 2 - tap_col, row_count, column_count)
            else:
                window = window_of(field, tap_row, tap_col, row_count, column_count)
            part = jnp.dot(kernel[tap_row, tap_col], window, preferred_element_type=jnp.float32)
            total = part if total is None else total + part
    return total


def local(inputs, cotangent, weight, bias_vector):
    own_channels, row_count, column_count = inputs.shape
    chan_count = lax.axis_size("chan")
    chan_index = lax.axis_index("chan")
    input_pad = mask_rims(padded_2(inputs, (("lon", 2), ("lat", 1)), 1))
    blocks = [input_pad]
    for shift in range(1, chan_count):
        pairs = [(i, (i - shift) % chan_count) for i in range(chan_count)]
        blocks.append(lax.ppermute(input_pad, "chan", pairs))
    kernel_cols = []
    for shift in range(chan_count):
        source = (chan_index + shift) % chan_count
        kernel_cols.append(
            lax.dynamic_slice_in_dim(weight, source * own_channels, own_channels, axis=3)
        )
    preact = None
    for shift in range(chan_count):
        part = conv_taps(kernel_cols[shift], blocks[shift], row_count, column_count, False)
        preact = part if preact is None else preact + part
    preact = preact + bias_vector[:, None]
    upstream = cotangent.reshape(own_channels, -1).astype(jnp.float32)
    grad_pre = (upstream * gelu_slope(preact)).astype(jnp.bfloat16)
    bias_part = jnp.sum(grad_pre.astype(jnp.float32), axis=1)
    input_local = jnp.concatenate(blocks, axis=0)
    taps = []
    for tap_row in range(3):
        row_taps = []
        for tap_col in range(3):
            window = window_of(input_local, tap_row, tap_col, row_count, column_count)
            row_taps.append(
                lax.dot_general(
                    grad_pre, window, (((1,), (1,)), ((), ())), preferred_element_type=jnp.float32
                )
            )
        taps.append(jnp.stack(row_taps))
    weight_part = jnp.stack(taps)
    flat = jnp.concatenate([weight_part.reshape(-1), bias_part])
    flat = lax.psum(flat, ("lon", "lat"))
    weight_local = flat[: weight_part.size].reshape(weight_part.shape)
    bias_grad = flat[weight_part.size :]
    doubled = jnp.concatenate([weight_local, weight_local], axis=3)
    weight_grad = lax.dynamic_slice_in_dim(
        doubled, (chan_count - chan_index) % chan_count * own_channels, chan_count * own_channels, axis=3
    )
    grad_field = grad_pre.reshape(own_channels, row_count, column_count)
    grad_pad = mask_rims(padded_2(grad_field, (("lon", 2), ("lat", 1)), 1))
    received = []
    for shift in range(1, chan_count):
        kernel_t = jnp.swapaxes(kernel_cols[shift], 2, 3)
        part = conv_taps(kernel_t, grad_pad, row_count, column_count, True)
        pairs = [(i, (i + shift) % chan_count) for i in range(chan_count)]
        received.append(lax.ppermute(part.astype(jnp.bfloat16), "chan", pairs))
    own_part = conv_taps(jnp.swapaxes(kernel_cols[0], 2, 3), grad_pad, row_count, column_count, True)
    for piece in received:
        own_part = own_part + piece.astype(jnp.float32)
    input_grad = own_part.astype(jnp.bfloat16).reshape(own_channels, row_count, column_count)
    return (input_grad, weight_grad, bias_grad)


def solution(mesh):
    placed = (
        P("chan", ("groups", "lat"), "lon"),
        P("chan", ("groups", "lat"), "lon"),
        P(None, None, "chan", None),
        P("chan"),
    )
    return jax.shard_map(
        local,
        mesh=mesh,
        in_specs=placed,
        out_specs=(
            P("chan", ("groups", "lat"), "lon"),
            P("groups", None, "chan", None),
            P(("groups", "chan")),
        ),
        check_vma=False,
    )
```

```python
import jax
import jax.numpy as jnp
from jax import lax
from jax.sharding import PartitionSpec as P


def padded_2(shard, sides, width):
    for axis, dim in sides:
        devices, length = (lax.axis_size(axis), shard.shape[dim])
        up = [(i, (i + 1) % devices) for i in range(devices)]
        down = [(j, i) for i, j in up]
        last = lax.slice_in_dim(shard, length - width, length, axis=dim)
        initial = lax.slice_in_dim(shard, 0, width, axis=dim)
        before = lax.ppermute(last, axis, up)
        after = lax.ppermute(initial, axis, down)
        shard = jnp.concatenate([before, shard, after], axis=dim)
    return shard


def gelu_slope(preact):
    normal_cdf = 0.5 * (1.0 + jax.scipy.special.erf(preact * 0.7071067811865476))
    density = jnp.exp(-0.5 * preact * preact) * 0.3989422804014327
    return normal_cdf + preact * density


def mask_rims(padded):
    lat_index = lax.axis_index("lat")
    band_count = lax.axis_size("lat")
    row_ids = jnp.arange(padded.shape[1])
    outside = (row_ids == 0) & (lat_index == 0) | (row_ids == padded.shape[1] - 1) & (
        lat_index == band_count - 1
    )
    return jnp.where(outside[None, :, None], jnp.zeros((), padded.dtype), padded)


def window_of(field, first_row, first_col, row_count, column_count):
    return field[
        :, first_row : first_row + row_count, first_col : first_col + column_count
    ].reshape(field.shape[0], -1)


def conv_taps(kernel, field, row_count, column_count, flip):
    total = None
    for tap_row in range(3):
        for tap_col in range(3):
            if flip:
                window = window_of(field, 2 - tap_row, 2 - tap_col, row_count, column_count)
            else:
                window = window_of(field, tap_row, tap_col, row_count, column_count)
            part = jnp.dot(kernel[tap_row, tap_col], window, preferred_element_type=jnp.float32)
            total = part if total is None else total + part
    return total


def ring_reduce_scatter(rows, axis, send_dtype):
    count, index = lax.axis_size(axis), lax.axis_index(axis)
    if count == 1:
        return rows
    chunks = rows.reshape(count, -1, rows.shape[-1])
    pairs = [(j, (j + 1) % count) for j in range(count)]
    acc = lax.dynamic_index_in_dim(chunks, (index - 1) % count, keepdims=False)
    for step in range(1, count):
        moved = lax.ppermute(acc.astype(send_dtype), axis, pairs).astype(jnp.float32)
        acc = moved + lax.dynamic_index_in_dim(chunks, (index - 1 - step) % count, keepdims=False)
    return acc


def ring_all_gather(chunk, axis, send_dtype):
    count, index = lax.axis_size(axis), lax.axis_index(axis)
    if count == 1:
        return chunk
    pairs = [(j, (j + 1) % count) for j in range(count)]
    pieces = [chunk]
    current = chunk.astype(send_dtype)
    for step in range(1, count):
        current = lax.ppermute(current, axis, pairs)
        pieces.append(current.astype(jnp.float32))
    stacked = jnp.stack(pieces[::-1])
    stacked = jnp.roll(stacked, (index + 1) % count, axis=0)
    return stacked.reshape(-1, chunk.shape[-1])


def all_sum(flat, send_dtype):
    parts = lax.axis_size("lat") * lax.axis_size("lon")
    quantum = parts * 8 * 128
    padded = jnp.pad(flat, (0, (-flat.size) % quantum)).reshape(-1, 128)
    rows = ring_reduce_scatter(padded, "lat", send_dtype)
    rows = ring_reduce_scatter(rows, "lon", send_dtype)
    rows = ring_all_gather(rows, "lon", send_dtype)
    rows = ring_all_gather(rows, "lat", send_dtype)
    return rows.reshape(-1)[: flat.size]


def local(inputs, cotangent, weight, bias_vector):
    own_channels, row_count, column_count = inputs.shape
    chan_count = lax.axis_size("chan")
    chan_index = lax.axis_index("chan")
    input_pad = mask_rims(padded_2(inputs, (("lon", 2), ("lat", 1)), 1))
    blocks = [input_pad]
    for shift in range(1, chan_count):
        pairs = [(i, (i - shift) % chan_count) for i in range(chan_count)]
        blocks.append(lax.ppermute(input_pad, "chan", pairs))
    kernel_cols = []
    for shift in range(chan_count):
        source = (chan_index + shift) % chan_count
        kernel_cols.append(
            lax.dynamic_slice_in_dim(weight, source * own_channels, own_channels, axis=3)
        )
    preact = None
    for shift in range(chan_count):
        part = conv_taps(kernel_cols[shift], blocks[shift], row_count, column_count, False)
        preact = part if preact is None else preact + part
    preact = preact + bias_vector[:, None]
    upstream = cotangent.reshape(own_channels, -1).astype(jnp.float32)
    grad_pre = (upstream * gelu_slope(preact)).astype(jnp.bfloat16)
    bias_part = jnp.sum(grad_pre.astype(jnp.float32), axis=1)
    input_local = jnp.concatenate(blocks, axis=0)
    taps = []
    for tap_row in range(3):
        row_taps = []
        for tap_col in range(3):
            window = window_of(input_local, tap_row, tap_col, row_count, column_count)
            row_taps.append(
                lax.dot_general(
                    grad_pre, window, (((1,), (1,)), ((), ())), preferred_element_type=jnp.float32
                )
            )
        taps.append(jnp.stack(row_taps))
    weight_part = jnp.stack(taps)
    flat = jnp.concatenate([weight_part.reshape(-1), bias_part])
    flat = all_sum(flat, jnp.float32)
    weight_local = flat[: weight_part.size].reshape(weight_part.shape)
    bias_grad = flat[weight_part.size :]
    doubled = jnp.concatenate([weight_local, weight_local], axis=3)
    weight_grad = lax.dynamic_slice_in_dim(
        doubled, (chan_count - chan_index) % chan_count * own_channels, chan_count * own_channels, axis=3
    )
    grad_field = grad_pre.reshape(own_channels, row_count, column_count)
    grad_pad = mask_rims(padded_2(grad_field, (("lon", 2), ("lat", 1)), 1))
    received = []
    for shift in range(1, chan_count):
        kernel_t = jnp.swapaxes(kernel_cols[shift], 2, 3)
        part = conv_taps(kernel_t, grad_pad, row_count, column_count, True)
        pairs = [(i, (i + shift) % chan_count) for i in range(chan_count)]
        received.append(lax.ppermute(part.astype(jnp.bfloat16), "chan", pairs))
    own_part = conv_taps(jnp.swapaxes(kernel_cols[0], 2, 3), grad_pad, row_count, column_count, True)
    for piece in received:
        own_part = own_part + piece.astype(jnp.float32)
    input_grad = own_part.astype(jnp.bfloat16).reshape(own_channels, row_count, column_count)
    return (input_grad, weight_grad, bias_grad)


def solution(mesh):
    placed = (
        P("chan", ("groups", "lat"), "lon"),
        P("chan", ("groups", "lat"), "lon"),
        P(None, None, "chan", None),
        P("chan"),
    )
    return jax.shard_map(
        local,
        mesh=mesh,
        in_specs=placed,
        out_specs=(
            P("chan", ("groups", "lat"), "lon"),
            P("groups", None, "chan", None),
            P(("groups", "chan")),
        ),
        check_vma=False,
    )
```

```python
import jax
import jax.numpy as jnp
from jax import lax
from jax.sharding import PartitionSpec as P


def padded_2(shard, sides, width):
    for axis, dim in sides:
        devices, length = (lax.axis_size(axis), shard.shape[dim])
        up = [(i, (i + 1) % devices) for i in range(devices)]
        down = [(j, i) for i, j in up]
        last = lax.slice_in_dim(shard, length - width, length, axis=dim)
        initial = lax.slice_in_dim(shard, 0, width, axis=dim)
        before = lax.ppermute(last, axis, up)
        after = lax.ppermute(initial, axis, down)
        shard = jnp.concatenate([before, shard, after], axis=dim)
    return shard


def gelu_slope(preact):
    normal_cdf = 0.5 * (1.0 + jax.scipy.special.erf(preact * 0.7071067811865476))
    density = jnp.exp(-0.5 * preact * preact) * 0.3989422804014327
    return normal_cdf + preact * density


def mask_rims(padded):
    lat_index = lax.axis_index("lat")
    band_count = lax.axis_size("lat")
    row_ids = jnp.arange(padded.shape[1])
    outside = (row_ids == 0) & (lat_index == 0) | (row_ids == padded.shape[1] - 1) & (
        lat_index == band_count - 1
    )
    return jnp.where(outside[None, :, None], jnp.zeros((), padded.dtype), padded)


def window_of(field, first_row, first_col, row_count, column_count):
    return field[
        :, first_row : first_row + row_count, first_col : first_col + column_count
    ].reshape(field.shape[0], -1)


def conv_taps(kernel, field, row_count, column_count, flip):
    total = None
    for tap_row in range(3):
        for tap_col in range(3):
            if flip:
                window = window_of(field, 2 - tap_row, 2 - tap_col, row_count, column_count)
            else:
                window = window_of(field, tap_row, tap_col, row_count, column_count)
            part = jnp.dot(kernel[tap_row, tap_col], window, preferred_element_type=jnp.float32)
            total = part if total is None else total + part
    return total


def direct_reduce_scatter(rows, axis, send_dtype):
    count, index = lax.axis_size(axis), lax.axis_index(axis)
    if count == 1:
        return rows
    chunks = rows.reshape(count, -1, rows.shape[-1])
    acc = lax.dynamic_index_in_dim(chunks, index, keepdims=False)
    for step in range(1, count):
        pairs = [(j, (j + step) % count) for j in range(count)]
        piece = lax.dynamic_index_in_dim(chunks, (index + step) % count, keepdims=False)
        acc = acc + lax.ppermute(piece.astype(send_dtype), axis, pairs).astype(jnp.float32)
    return acc


def direct_all_gather(chunk, axis, send_dtype):
    count, index = lax.axis_size(axis), lax.axis_index(axis)
    if count == 1:
        return chunk
    pieces = [chunk]
    sent = chunk.astype(send_dtype)
    for step in range(1, count):
        pairs = [(j, (j + step) % count) for j in range(count)]
        pieces.append(lax.ppermute(sent, axis, pairs).astype(jnp.float32))
    stacked = jnp.stack(pieces[::-1])
    stacked = jnp.roll(stacked, (index + 1) % count, axis=0)
    return stacked.reshape(-1, chunk.shape[-1])


def all_sum(flat, send_dtype):
    parts = lax.axis_size("lat") * lax.axis_size("lon")
    quantum = parts * 8 * 128
    padded = jnp.pad(flat, (0, (-flat.size) % quantum)).reshape(-1, 128)
    rows = direct_reduce_scatter(padded, "lat", jnp.float32)
    rows = direct_reduce_scatter(rows, "lon", send_dtype)
    rows = direct_all_gather(rows, "lon", send_dtype)
    rows = direct_all_gather(rows, "lat", jnp.float32)
    return rows.reshape(-1)[: flat.size]


def local(inputs, cotangent, weight, bias_vector):
    own_channels, row_count, column_count = inputs.shape
    chan_count = lax.axis_size("chan")
    chan_index = lax.axis_index("chan")
    input_pad = mask_rims(padded_2(inputs, (("lon", 2), ("lat", 1)), 1))
    blocks = [input_pad]
    for shift in range(1, chan_count):
        pairs = [(i, (i - shift) % chan_count) for i in range(chan_count)]
        blocks.append(lax.ppermute(input_pad, "chan", pairs))
    kernel_cols = []
    for shift in range(chan_count):
        source = (chan_index + shift) % chan_count
        kernel_cols.append(
            lax.dynamic_slice_in_dim(weight, source * own_channels, own_channels, axis=3)
        )
    preact = None
    for shift in range(chan_count):
        part = conv_taps(kernel_cols[shift], blocks[shift], row_count, column_count, False)
        preact = part if preact is None else preact + part
    preact = preact + bias_vector[:, None]
    upstream = cotangent.reshape(own_channels, -1).astype(jnp.float32)
    grad_pre = (upstream * gelu_slope(preact)).astype(jnp.bfloat16)
    bias_part = jnp.sum(grad_pre.astype(jnp.float32), axis=1)
    input_local = jnp.concatenate(blocks, axis=0)
    taps = []
    for tap_row in range(3):
        row_taps = []
        for tap_col in range(3):
            window = window_of(input_local, tap_row, tap_col, row_count, column_count)
            row_taps.append(
                lax.dot_general(
                    grad_pre, window, (((1,), (1,)), ((), ())), preferred_element_type=jnp.float32
                )
            )
        taps.append(jnp.stack(row_taps))
    weight_part = jnp.stack(taps)
    flat = jnp.concatenate([weight_part.reshape(-1), bias_part])
    flat = all_sum(flat, jnp.bfloat16)
    weight_local = flat[: weight_part.size].reshape(weight_part.shape)
    bias_grad = flat[weight_part.size :]
    doubled = jnp.concatenate([weight_local, weight_local], axis=3)
    weight_grad = lax.dynamic_slice_in_dim(
        doubled, (chan_count - chan_index) % chan_count * own_channels, chan_count * own_channels, axis=3
    )
    grad_field = grad_pre.reshape(own_channels, row_count, column_count)
    grad_pad = mask_rims(padded_2(grad_field, (("lon", 2), ("lat", 1)), 1))
    received = []
    for shift in range(1, chan_count):
        kernel_t = jnp.swapaxes(kernel_cols[shift], 2, 3)
        part = conv_taps(kernel_t, grad_pad, row_count, column_count, True)
        pairs = [(i, (i + shift) % chan_count) for i in range(chan_count)]
        received.append(lax.ppermute(part.astype(jnp.bfloat16), "chan", pairs))
    own_part = conv_taps(jnp.swapaxes(kernel_cols[0], 2, 3), grad_pad, row_count, column_count, True)
    for piece in received:
        own_part = own_part + piece.astype(jnp.float32)
    input_grad = own_part.astype(jnp.bfloat16).reshape(own_channels, row_count, column_count)
    return (input_grad, weight_grad, bias_grad)


def solution(mesh):
    placed = (
        P("chan", ("groups", "lat"), "lon"),
        P("chan", ("groups", "lat"), "lon"),
        P(None, None, "chan", None),
        P("chan"),
    )
    return jax.shard_map(
        local,
        mesh=mesh,
        in_specs=placed,
        out_specs=(
            P("chan", ("groups", "lat"), "lon"),
            P("groups", None, "chan", None),
            P(("groups", "chan")),
        ),
        check_vma=False,
    )
```

```python
import jax
import jax.numpy as jnp
from jax import lax
from jax.sharding import PartitionSpec as P


def padded_2(shard, sides, width):
    for axis, dim in sides:
        devices, length = (lax.axis_size(axis), shard.shape[dim])
        up = [(i, (i + 1) % devices) for i in range(devices)]
        down = [(j, i) for i, j in up]
        last = lax.slice_in_dim(shard, length - width, length, axis=dim)
        initial = lax.slice_in_dim(shard, 0, width, axis=dim)
        before = lax.ppermute(last, axis, up)
        after = lax.ppermute(initial, axis, down)
        shard = jnp.concatenate([before, shard, after], axis=dim)
    return shard


def gelu_slope(preact):
    normal_cdf = 0.5 * (1.0 + jax.scipy.special.erf(preact * 0.7071067811865476))
    density = jnp.exp(-0.5 * preact * preact) * 0.3989422804014327
    return normal_cdf + preact * density


def mask_rims(padded):
    lat_index = lax.axis_index("lat")
    band_count = lax.axis_size("lat")
    row_ids = jnp.arange(padded.shape[1])
    outside = (row_ids == 0) & (lat_index == 0) | (row_ids == padded.shape[1] - 1) & (
        lat_index == band_count - 1
    )
    return jnp.where(outside[None, :, None], jnp.zeros((), padded.dtype), padded)


def window_of(field, first_row, first_col, row_count, column_count):
    return field[
        :, first_row : first_row + row_count, first_col : first_col + column_count
    ].reshape(field.shape[0], -1)


def conv_taps(kernel, field, row_count, column_count, flip):
    total = None
    for tap_row in range(3):
        for tap_col in range(3):
            if flip:
                window = window_of(field, 2 - tap_row, 2 - tap_col, row_count, column_count)
            else:
                window = window_of(field, tap_row, tap_col, row_count, column_count)
            part = jnp.dot(kernel[tap_row, tap_col], window, preferred_element_type=jnp.float32)
            total = part if total is None else total + part
    return total


def direct_reduce_scatter(rows, axis, send_dtype):
    count, index = lax.axis_size(axis), lax.axis_index(axis)
    if count == 1:
        return rows
    chunks = rows.reshape(count, -1, rows.shape[-1])
    acc = lax.dynamic_index_in_dim(chunks, index, keepdims=False)
    for step in range(1, count):
        pairs = [(j, (j + step) % count) for j in range(count)]
        piece = lax.dynamic_index_in_dim(chunks, (index + step) % count, keepdims=False)
        acc = acc + lax.ppermute(piece.astype(send_dtype), axis, pairs).astype(jnp.float32)
    return acc


def direct_all_gather(chunk, axis, send_dtype):
    count, index = lax.axis_size(axis), lax.axis_index(axis)
    if count == 1:
        return chunk
    pieces = [chunk]
    sent = chunk.astype(send_dtype)
    for step in range(1, count):
        pairs = [(j, (j + step) % count) for j in range(count)]
        pieces.append(lax.ppermute(sent, axis, pairs).astype(jnp.float32))
    stacked = jnp.stack(pieces[::-1])
    stacked = jnp.roll(stacked, (index + 1) % count, axis=0)
    return stacked.reshape(-1, chunk.shape[-1])


def all_sum(flat, send_dtype):
    parts = lax.axis_size("lat") * lax.axis_size("lon")
    quantum = parts * 8 * 128
    padded = jnp.pad(flat, (0, (-flat.size) % quantum)).reshape(-1, 128)
    rows = direct_reduce_scatter(padded, "lat", jnp.float32)
    rows = direct_reduce_scatter(rows, "lon", send_dtype)
    rows = direct_all_gather(rows, "lon", send_dtype)
    rows = direct_all_gather(rows, "lat", jnp.float32)
    return rows.reshape(-1)[: flat.size]


def border_of(padded):
    rows, cols = padded.shape[1], padded.shape[2]
    return jnp.concatenate(
        [padded[:, 0, :], padded[:, rows - 1, :], padded[:, 1 : rows - 1, 0], padded[:, 1 : rows - 1, cols - 1]],
        axis=1,
    )


def with_border(field, border):
    rows, cols = field.shape[1], field.shape[2]
    top = border[:, : cols + 2]
    bottom = border[:, cols + 2 : 2 * cols + 4]
    left = border[:, 2 * cols + 4 : 2 * cols + 4 + rows]
    right = border[:, 2 * cols + 4 + rows :]
    middle = jnp.concatenate([left[:, :, None], field, right[:, :, None]], axis=2)
    return jnp.concatenate([top[:, None, :], middle, bottom[:, None, :]], axis=1)


def local(inputs, cotangent, weight, bias_vector):
    own_channels, row_count, column_count = inputs.shape
    chan_count = lax.axis_size("chan")
    chan_index = lax.axis_index("chan")
    raw_blocks = []
    for shift in range(1, chan_count):
        pairs = [(i, (i - shift) % chan_count) for i in range(chan_count)]
        raw_blocks.append(lax.ppermute(inputs, "chan", pairs))
    input_pad = mask_rims(padded_2(inputs, (("lon", 2), ("lat", 1)), 1))
    own_border = border_of(input_pad)
    blocks = [input_pad]
    for shift in range(1, chan_count):
        pairs = [(i, (i - shift) % chan_count) for i in range(chan_count)]
        border = lax.ppermute(own_border, "chan", pairs)
        blocks.append(with_border(raw_blocks[shift - 1], border))
    kernel_cols = []
    for shift in range(chan_count):
        source = (chan_index + shift) % chan_count
        kernel_cols.append(
            lax.dynamic_slice_in_dim(weight, source * own_channels, own_channels, axis=3)
        )
    windows = [
        [window_of(block, tap // 3, tap % 3, row_count, column_count) for tap in range(9)]
        for block in blocks
    ]
    preact = None
    for shift in range(chan_count):
        for tap in range(9):
            part = jnp.dot(
                kernel_cols[shift][tap // 3, tap % 3], windows[shift][tap], preferred_element_type=jnp.float32
            )
            preact = part if preact is None else preact + part
    preact = preact + bias_vector[:, None]
    upstream = cotangent.reshape(own_channels, -1).astype(jnp.float32)
    grad_pre = (upstream * gelu_slope(preact)).astype(jnp.bfloat16)
    bias_part = jnp.sum(grad_pre.astype(jnp.float32), axis=1)
    pieces = []
    for shift in range(chan_count):
        for tap in range(9):
            pieces.append(
                lax.dot_general(
                    grad_pre, windows[shift][tap], (((1,), (1,)), ((), ())), preferred_element_type=jnp.float32
                ).reshape(-1)
            )
    flat = jnp.concatenate(pieces + [bias_part])
    flat = all_sum(flat, jnp.bfloat16)
    block_size = 9 * own_channels * own_channels
    weight_local = flat[: chan_count * block_size].reshape(chan_count, 3, 3, own_channels, own_channels)
    bias_grad = flat[chan_count * block_size :]
    doubled = jnp.concatenate([weight_local, weight_local], axis=0)
    ordered = lax.dynamic_slice_in_dim(doubled, (chan_count - chan_index) % chan_count, chan_count, axis=0)
    weight_grad = jnp.transpose(ordered, (1, 2, 3, 0, 4)).reshape(3, 3, own_channels, chan_count * own_channels)
    grad_field = grad_pre.reshape(own_channels, row_count, column_count)
    grad_pad = mask_rims(padded_2(grad_field, (("lon", 2), ("lat", 1)), 1))
    received = []
    for shift in range(1, chan_count):
        kernel_t = jnp.swapaxes(kernel_cols[shift], 2, 3)
        part = conv_taps(kernel_t, grad_pad, row_count, column_count, True)
        pairs = [(i, (i + shift) % chan_count) for i in range(chan_count)]
        received.append(lax.ppermute(part.astype(jnp.bfloat16), "chan", pairs))
    own_part = conv_taps(jnp.swapaxes(kernel_cols[0], 2, 3), grad_pad, row_count, column_count, True)
    for piece in received:
        own_part = own_part + piece.astype(jnp.float32)
    input_grad = own_part.astype(jnp.bfloat16).reshape(own_channels, row_count, column_count)
    return (input_grad, weight_grad, bias_grad)


def solution(mesh):
    placed = (
        P("chan", ("groups", "lat"), "lon"),
        P("chan", ("groups", "lat"), "lon"),
        P(None, None, "chan", None),
        P("chan"),
    )
    return jax.shard_map(
        local,
        mesh=mesh,
        in_specs=placed,
        out_specs=(
            P("chan", ("groups", "lat"), "lon"),
            P("groups", None, "chan", None),
            P(("groups", "chan")),
        ),
        check_vma=False,
    )
```

```python
import jax
import jax.numpy as jnp
from jax import lax
from jax.sharding import PartitionSpec as P


def padded_2(shard, sides, width):
    for axis, dim in sides:
        devices, length = (lax.axis_size(axis), shard.shape[dim])
        up = [(i, (i + 1) % devices) for i in range(devices)]
        down = [(j, i) for i, j in up]
        last = lax.slice_in_dim(shard, length - width, length, axis=dim)
        initial = lax.slice_in_dim(shard, 0, width, axis=dim)
        before = lax.ppermute(last, axis, up)
        after = lax.ppermute(initial, axis, down)
        shard = jnp.concatenate([before, shard, after], axis=dim)
    return shard


def gelu_slope(preact):
    normal_cdf = 0.5 * (1.0 + jax.scipy.special.erf(preact * 0.7071067811865476))
    density = jnp.exp(-0.5 * preact * preact) * 0.3989422804014327
    return normal_cdf + preact * density


def mask_rims(padded):
    lat_index = lax.axis_index("lat")
    band_count = lax.axis_size("lat")
    row_ids = jnp.arange(padded.shape[1])
    outside = (row_ids == 0) & (lat_index == 0) | (row_ids == padded.shape[1] - 1) & (
        lat_index == band_count - 1
    )
    return jnp.where(outside[None, :, None], jnp.zeros((), padded.dtype), padded)


def window_of(field, first_row, first_col, row_count, column_count):
    return field[
        :, first_row : first_row + row_count, first_col : first_col + column_count
    ].reshape(field.shape[0], -1)


def conv_taps(kernel, field, row_count, column_count, flip):
    total = None
    for tap_row in range(3):
        for tap_col in range(3):
            if flip:
                window = window_of(field, 2 - tap_row, 2 - tap_col, row_count, column_count)
            else:
                window = window_of(field, tap_row, tap_col, row_count, column_count)
            part = jnp.dot(kernel[tap_row, tap_col], window, preferred_element_type=jnp.float32)
            total = part if total is None else total + part
    return total


def direct_reduce_scatter(rows, axis, send_dtype):
    count, index = lax.axis_size(axis), lax.axis_index(axis)
    if count == 1:
        return rows
    chunks = rows.reshape(count, -1, rows.shape[-1])
    acc = lax.dynamic_index_in_dim(chunks, index, keepdims=False)
    for step in range(1, count):
        pairs = [(j, (j + step) % count) for j in range(count)]
        piece = lax.dynamic_index_in_dim(chunks, (index + step) % count, keepdims=False)
        acc = acc + lax.ppermute(piece.astype(send_dtype), axis, pairs).astype(jnp.float32)
    return acc


def direct_all_gather(chunk, axis, send_dtype):
    count, index = lax.axis_size(axis), lax.axis_index(axis)
    if count == 1:
        return chunk
    pieces = [chunk]
    sent = chunk.astype(send_dtype)
    for step in range(1, count):
        pairs = [(j, (j + step) % count) for j in range(count)]
        pieces.append(lax.ppermute(sent, axis, pairs).astype(jnp.float32))
    stacked = jnp.stack(pieces[::-1])
    stacked = jnp.roll(stacked, (index + 1) % count, axis=0)
    return stacked.reshape(-1, chunk.shape[-1])


def all_sum(rows, send_dtype):
    parts = lax.axis_size("lat") * lax.axis_size("lon")
    quantum = parts * 8
    padded = jnp.pad(rows, ((0, (-rows.shape[0]) % quantum), (0, 0)))
    total = direct_reduce_scatter(padded, "lat", jnp.float32)
    total = direct_reduce_scatter(total, "lon", send_dtype)
    total = direct_all_gather(total, "lon", send_dtype)
    total = direct_all_gather(total, "lat", jnp.float32)
    return total[: rows.shape[0]]


def border_of(padded):
    rows, cols = padded.shape[1], padded.shape[2]
    return jnp.concatenate(
        [padded[:, 0, :], padded[:, rows - 1, :], padded[:, 1 : rows - 1, 0], padded[:, 1 : rows - 1, cols - 1]],
        axis=1,
    )


def with_border(field, border):
    rows, cols = field.shape[1], field.shape[2]
    top = border[:, : cols + 2]
    bottom = border[:, cols + 2 : 2 * cols + 4]
    left = border[:, 2 * cols + 4 : 2 * cols + 4 + rows]
    right = border[:, 2 * cols + 4 + rows :]
    middle = jnp.concatenate([left[:, :, None], field, right[:, :, None]], axis=2)
    return jnp.concatenate([top[:, None, :], middle, bottom[:, None, :]], axis=1)


def local(inputs, cotangent, weight, bias_vector):
    own_channels, row_count, column_count = inputs.shape
    chan_count = lax.axis_size("chan")
    chan_index = lax.axis_index("chan")
    raw_blocks = []
    for shift in range(1, chan_count):
        pairs = [(i, (i - shift) % chan_count) for i in range(chan_count)]
        raw_blocks.append(lax.ppermute(inputs, "chan", pairs))
    input_pad = mask_rims(padded_2(inputs, (("lon", 2), ("lat", 1)), 1))
    own_border = border_of(input_pad)
    blocks = [input_pad]
    for shift in range(1, chan_count):
        pairs = [(i, (i - shift) % chan_count) for i in range(chan_count)]
        border = lax.ppermute(own_border, "chan", pairs)
        blocks.append(with_border(raw_blocks[shift - 1], border))
    kernel_cols = []
    for shift in range(chan_count):
        source = (chan_index + shift) % chan_count
        kernel_cols.append(
            lax.dynamic_slice_in_dim(weight, source * own_channels, own_channels, axis=3)
        )
    windows = [
        [window_of(block, tap // 3, tap % 3, row_count, column_count) for tap in range(9)]
        for block in blocks
    ]
    preact = None
    for shift in range(chan_count):
        for tap in range(9):
            part = jnp.dot(
                kernel_cols[shift][tap // 3, tap % 3], windows[shift][tap], preferred_element_type=jnp.float32
            )
            preact = part if preact is None else preact + part
    preact = preact + bias_vector[:, None]
    upstream = cotangent.reshape(own_channels, -1).astype(jnp.float32)
    grad_pre = (upstream * gelu_slope(preact)).astype(jnp.bfloat16)
    bias_part = jnp.sum(grad_pre.astype(jnp.float32), axis=1)
    pieces = []
    for shift in range(chan_count):
        for tap in range(9):
            pieces.append(
                lax.dot_general(
                    grad_pre, windows[shift][tap], (((1,), (1,)), ((), ())), preferred_element_type=jnp.float32
                )
            )
    weight_rows = jnp.concatenate(pieces, axis=0).reshape(-1, 128)
    bias_rows = jnp.pad(bias_part, (0, (-bias_part.size) % 128)).reshape(-1, 128)
    summed = all_sum(jnp.concatenate([weight_rows, bias_rows], axis=0), jnp.bfloat16)
    weight_local = summed[: weight_rows.shape[0]].reshape(chan_count, 3, 3, own_channels, own_channels)
    bias_grad = summed[weight_rows.shape[0] :].reshape(-1)[: bias_part.size]
    doubled = jnp.concatenate([weight_local, weight_local], axis=0)
    ordered = lax.dynamic_slice_in_dim(doubled, (chan_count - chan_index) % chan_count, chan_count, axis=0)
    weight_grad = jnp.transpose(ordered, (1, 2, 3, 0, 4)).reshape(3, 3, own_channels, chan_count * own_channels)
    grad_field = grad_pre.reshape(own_channels, row_count, column_count)
    grad_pad = mask_rims(padded_2(grad_field, (("lon", 2), ("lat", 1)), 1))
    received = []
    for shift in range(1, chan_count):
        kernel_t = jnp.swapaxes(kernel_cols[shift], 2, 3)
        part = conv_taps(kernel_t, grad_pad, row_count, column_count, True)
        pairs = [(i, (i + shift) % chan_count) for i in range(chan_count)]
        received.append(lax.ppermute(part.astype(jnp.bfloat16), "chan", pairs))
    own_part = conv_taps(jnp.swapaxes(kernel_cols[0], 2, 3), grad_pad, row_count, column_count, True)
    for piece in received:
        own_part = own_part + piece.astype(jnp.float32)
    input_grad = own_part.astype(jnp.bfloat16).reshape(own_channels, row_count, column_count)
    return (input_grad, weight_grad, bias_grad)


def solution(mesh):
    placed = (
        P("chan", ("groups", "lat"), "lon"),
        P("chan", ("groups", "lat"), "lon"),
        P(None, None, "chan", None),
        P("chan"),
    )
    return jax.shard_map(
        local,
        mesh=mesh,
        in_specs=placed,
        out_specs=(
            P("chan", ("groups", "lat"), "lon"),
            P("groups", None, "chan", None),
            P(("groups", "chan")),
        ),
        check_vma=False,
    )
```

```python
import jax
import jax.numpy as jnp
from jax import lax
from jax.sharding import PartitionSpec as P


def padded_2(shard, sides, width):
    for axis, dim in sides:
        devices, length = (lax.axis_size(axis), shard.shape[dim])
        up = [(i, (i + 1) % devices) for i in range(devices)]
        down = [(j, i) for i, j in up]
        last = lax.slice_in_dim(shard, length - width, length, axis=dim)
        initial = lax.slice_in_dim(shard, 0, width, axis=dim)
        before = lax.ppermute(last, axis, up)
        after = lax.ppermute(initial, axis, down)
        shard = jnp.concatenate([before, shard, after], axis=dim)
    return shard


def gelu_slope(preact):
    normal_cdf = 0.5 * (1.0 + jax.scipy.special.erf(preact * 0.7071067811865476))
    density = jnp.exp(-0.5 * preact * preact) * 0.3989422804014327
    return normal_cdf + preact * density


def mask_rims(padded):
    lat_index = lax.axis_index("lat")
    band_count = lax.axis_size("lat")
    row_ids = jnp.arange(padded.shape[1])
    outside = (row_ids == 0) & (lat_index == 0) | (row_ids == padded.shape[1] - 1) & (
        lat_index == band_count - 1
    )
    return jnp.where(outside[None, :, None], jnp.zeros((), padded.dtype), padded)


def window_of(field, first_row, first_col, row_count, column_count):
    return field[
        :, first_row : first_row + row_count, first_col : first_col + column_count
    ].reshape(field.shape[0], -1)


def conv_taps(kernel, field, row_count, column_count, flip):
    total = None
    for tap_row in range(3):
        for tap_col in range(3):
            if flip:
                window = window_of(field, 2 - tap_row, 2 - tap_col, row_count, column_count)
            else:
                window = window_of(field, tap_row, tap_col, row_count, column_count)
            part = jnp.dot(kernel[tap_row, tap_col], window, preferred_element_type=jnp.float32)
            total = part if total is None else total + part
    return total


def direct_reduce_scatter(rows, axis, send_dtype):
    count, index = lax.axis_size(axis), lax.axis_index(axis)
    if count == 1:
        return rows
    chunks = rows.reshape(count, -1, rows.shape[-1])
    acc = lax.dynamic_index_in_dim(chunks, index, keepdims=False)
    for step in range(1, count):
        pairs = [(j, (j + step) % count) for j in range(count)]
        piece = lax.dynamic_index_in_dim(chunks, (index + step) % count, keepdims=False)
        acc = acc + lax.ppermute(piece.astype(send_dtype), axis, pairs).astype(jnp.float32)
    return acc


def direct_all_gather(chunk, axis, send_dtype):
    count, index = lax.axis_size(axis), lax.axis_index(axis)
    if count == 1:
        return chunk
    pieces = [chunk]
    sent = chunk.astype(send_dtype)
    for step in range(1, count):
        pairs = [(j, (j + step) % count) for j in range(count)]
        pieces.append(lax.ppermute(sent, axis, pairs).astype(jnp.float32))
    stacked = jnp.stack(pieces[::-1])
    stacked = jnp.roll(stacked, (index + 1) % count, axis=0)
    return stacked.reshape(-1, chunk.shape[-1])


def all_sum(rows, send_dtype):
    parts = lax.axis_size("lat") * lax.axis_size("lon")
    quantum = parts * 8
    padded = jnp.pad(rows, ((0, (-rows.shape[0]) % quantum), (0, 0)))
    total = direct_reduce_scatter(padded, "lat", jnp.float32)
    total = direct_reduce_scatter(total, "lon", send_dtype)
    total = direct_all_gather(total, "lon", send_dtype)
    total = direct_all_gather(total, "lat", jnp.float32)
    return total[: rows.shape[0]]


def border_of(padded):
    rows, cols = padded.shape[1], padded.shape[2]
    return jnp.concatenate(
        [padded[:, 0, :], padded[:, rows - 1, :], padded[:, 1 : rows - 1, 0], padded[:, 1 : rows - 1, cols - 1]],
        axis=1,
    )


def with_border(field, border):
    rows, cols = field.shape[1], field.shape[2]
    top = border[:, : cols + 2]
    bottom = border[:, cols + 2 : 2 * cols + 4]
    left = border[:, 2 * cols + 4 : 2 * cols + 4 + rows]
    right = border[:, 2 * cols + 4 + rows :]
    middle = jnp.concatenate([left[:, :, None], field, right[:, :, None]], axis=2)
    return jnp.concatenate([top[:, None, :], middle, bottom[:, None, :]], axis=1)


def local(inputs, cotangent, weight, bias_vector):
    own_channels, row_count, column_count = inputs.shape
    chan_count = lax.axis_size("chan")
    chan_index = lax.axis_index("chan")
    raw_blocks = []
    for shift in range(1, chan_count):
        pairs = [(i, (i - shift) % chan_count) for i in range(chan_count)]
        raw_blocks.append(lax.ppermute(inputs, "chan", pairs))
    input_pad = mask_rims(padded_2(inputs, (("lon", 2), ("lat", 1)), 1))
    own_border = border_of(input_pad)
    blocks = [input_pad]
    for shift in range(1, chan_count):
        pairs = [(i, (i - shift) % chan_count) for i in range(chan_count)]
        border = lax.ppermute(own_border, "chan", pairs)
        blocks.append(with_border(raw_blocks[shift - 1], border))
    kernel_cols = []
    for shift in range(chan_count):
        source = (chan_index + shift) % chan_count
        kernel_cols.append(
            lax.dynamic_slice_in_dim(weight, source * own_channels, own_channels, axis=3)
        )
    windows = [
        [window_of(block, tap // 3, tap % 3, row_count, column_count) for tap in range(9)]
        for block in blocks
    ]
    preact = None
    for shift in range(chan_count):
        for tap in range(9):
            part = jnp.dot(
                kernel_cols[shift][tap // 3, tap % 3], windows[shift][tap], preferred_element_type=jnp.float32
            )
            preact = part if preact is None else preact + part
    preact = preact + bias_vector[:, None]
    upstream = cotangent.reshape(own_channels, -1).astype(jnp.float32)
    grad_pre = (upstream * gelu_slope(preact)).astype(jnp.bfloat16)
    bias_part = jnp.sum(grad_pre.astype(jnp.float32), axis=1)
    input_local = jnp.concatenate(blocks, axis=0)
    taps = []
    for tap in range(9):
        window = window_of(input_local, tap // 3, tap % 3, row_count, column_count)
        taps.append(
            lax.dot_general(grad_pre, window, (((1,), (1,)), ((), ())), preferred_element_type=jnp.float32)
        )
    weight_rows = jnp.stack(taps).reshape(-1, 128)
    bias_rows = jnp.pad(bias_part, (0, (-bias_part.size) % 128)).reshape(-1, 128)
    summed = all_sum(jnp.concatenate([weight_rows, bias_rows], axis=0), jnp.bfloat16)
    weight_local = summed[: weight_rows.shape[0]].reshape(3, 3, own_channels, chan_count * own_channels)
    bias_grad = summed[weight_rows.shape[0] :].reshape(-1)[: bias_part.size]
    doubled = jnp.concatenate([weight_local, weight_local], axis=3)
    weight_grad = lax.dynamic_slice_in_dim(
        doubled, (chan_count - chan_index) % chan_count * own_channels, chan_count * own_channels, axis=3
    )
    grad_field = grad_pre.reshape(own_channels, row_count, column_count)
    grad_pad = mask_rims(padded_2(grad_field, (("lon", 2), ("lat", 1)), 1))
    received = []
    for shift in range(1, chan_count):
        kernel_t = jnp.swapaxes(kernel_cols[shift], 2, 3)
        part = conv_taps(kernel_t, grad_pad, row_count, column_count, True)
        pairs = [(i, (i + shift) % chan_count) for i in range(chan_count)]
        received.append(lax.ppermute(part.astype(jnp.bfloat16), "chan", pairs))
    own_part = conv_taps(jnp.swapaxes(kernel_cols[0], 2, 3), grad_pad, row_count, column_count, True)
    for piece in received:
        own_part = own_part + piece.astype(jnp.float32)
    input_grad = own_part.astype(jnp.bfloat16).reshape(own_channels, row_count, column_count)
    return (input_grad, weight_grad, bias_grad)


def solution(mesh):
    placed = (
        P("chan", ("groups", "lat"), "lon"),
        P("chan", ("groups", "lat"), "lon"),
        P(None, None, "chan", None),
        P("chan"),
    )
    return jax.shard_map(
        local,
        mesh=mesh,
        in_specs=placed,
        out_specs=(
            P("chan", ("groups", "lat"), "lon"),
            P("groups", None, "chan", None),
            P(("groups", "chan")),
        ),
        check_vma=False,
    )
```

```python
import jax
import jax.numpy as jnp
from jax import lax
from jax.sharding import PartitionSpec as P


def padded_2(shard, sides, width):
    for axis, dim in sides:
        devices, length = (lax.axis_size(axis), shard.shape[dim])
        up = [(i, (i + 1) % devices) for i in range(devices)]
        down = [(j, i) for i, j in up]
        last = lax.slice_in_dim(shard, length - width, length, axis=dim)
        initial = lax.slice_in_dim(shard, 0, width, axis=dim)
        before = lax.ppermute(last, axis, up)
        after = lax.ppermute(initial, axis, down)
        shard = jnp.concatenate([before, shard, after], axis=dim)
    return shard


def gelu_slope(preact):
    normal_cdf = 0.5 * (1.0 + jax.scipy.special.erf(preact * 0.7071067811865476))
    density = jnp.exp(-0.5 * preact * preact) * 0.3989422804014327
    return normal_cdf + preact * density


def mask_rims(padded):
    lat_index = lax.axis_index("lat")
    band_count = lax.axis_size("lat")
    row_ids = jnp.arange(padded.shape[1])
    outside = (row_ids == 0) & (lat_index == 0) | (row_ids == padded.shape[1] - 1) & (
        lat_index == band_count - 1
    )
    return jnp.where(outside[None, :, None], jnp.zeros((), padded.dtype), padded)


def window_of(field, first_row, first_col, row_count, column_count):
    return field[
        :, first_row : first_row + row_count, first_col : first_col + column_count
    ].reshape(field.shape[0], -1)


def conv_taps(kernel, field, row_count, column_count, flip):
    total = None
    for tap_row in range(3):
        for tap_col in range(3):
            if flip:
                window = window_of(field, 2 - tap_row, 2 - tap_col, row_count, column_count)
            else:
                window = window_of(field, tap_row, tap_col, row_count, column_count)
            part = jnp.dot(kernel[tap_row, tap_col], window, preferred_element_type=jnp.float32)
            total = part if total is None else total + part
    return total


def direct_reduce_scatter(rows, axis, send_dtype):
    count, index = lax.axis_size(axis), lax.axis_index(axis)
    if count == 1:
        return rows
    chunks = rows.reshape(count, -1, rows.shape[-1])
    acc = lax.dynamic_index_in_dim(chunks, index, keepdims=False)
    for step in range(1, count):
        pairs = [(j, (j + step) % count) for j in range(count)]
        piece = lax.dynamic_index_in_dim(chunks, (index + step) % count, keepdims=False)
        acc = acc + lax.ppermute(piece.astype(send_dtype), axis, pairs).astype(jnp.float32)
    return acc


def direct_all_gather(chunk, axis, send_dtype):
    count, index = lax.axis_size(axis), lax.axis_index(axis)
    if count == 1:
        return chunk
    pieces = [chunk]
    sent = chunk.astype(send_dtype)
    for step in range(1, count):
        pairs = [(j, (j + step) % count) for j in range(count)]
        pieces.append(lax.ppermute(sent, axis, pairs).astype(jnp.float32))
    stacked = jnp.stack(pieces[::-1])
    stacked = jnp.roll(stacked, (index + 1) % count, axis=0)
    return stacked.reshape(-1, chunk.shape[-1])


def all_sum(flat, send_dtype):
    parts = lax.axis_size("lat") * lax.axis_size("lon")
    quantum = parts * 8 * 128
    padded = jnp.pad(flat, (0, (-flat.size) % quantum)).reshape(-1, 128)
    rows = direct_reduce_scatter(padded, "lat", jnp.float32)
    rows = direct_reduce_scatter(rows, "lon", send_dtype)
    rows = direct_all_gather(rows, "lon", send_dtype)
    rows = direct_all_gather(rows, "lat", jnp.float32)
    return rows.reshape(-1)[: flat.size]


def border_of(padded):
    rows, cols = padded.shape[1], padded.shape[2]
    return jnp.concatenate(
        [padded[:, 0, :], padded[:, rows - 1, :], padded[:, 1 : rows - 1, 0], padded[:, 1 : rows - 1, cols - 1]],
        axis=1,
    )


def with_border(field, border):
    rows, cols = field.shape[1], field.shape[2]
    top = border[:, : cols + 2]
    bottom = border[:, cols + 2 : 2 * cols + 4]
    left = border[:, 2 * cols + 4 : 2 * cols + 4 + rows]
    right = border[:, 2 * cols + 4 + rows :]
    middle = jnp.concatenate([left[:, :, None], field, right[:, :, None]], axis=2)
    return jnp.concatenate([top[:, None, :], middle, bottom[:, None, :]], axis=1)


def local(inputs, cotangent, weight, bias_vector):
    own_channels, row_count, column_count = inputs.shape
    chan_count = lax.axis_size("chan")
    chan_index = lax.axis_index("chan")
    raw_blocks = []
    for shift in range(1, chan_count):
        pairs = [(i, (i - shift) % chan_count) for i in range(chan_count)]
        raw_blocks.append(lax.ppermute(inputs, "chan", pairs))
    input_pad = mask_rims(padded_2(inputs, (("lon", 2), ("lat", 1)), 1))
    own_border = border_of(input_pad)
    blocks = [input_pad]
    for shift in range(1, chan_count):
        pairs = [(i, (i - shift) % chan_count) for i in range(chan_count)]
        border = lax.ppermute(own_border, "chan", pairs)
        blocks.append(lax.optimization_barrier(with_border(raw_blocks[shift - 1], border)))
    kernel_cols = []
    for shift in range(chan_count):
        source = (chan_index + shift) % chan_count
        kernel_cols.append(
            lax.dynamic_slice_in_dim(weight, source * own_channels, own_channels, axis=3)
        )
    preact = None
    for shift in range(chan_count):
        part = conv_taps(kernel_cols[shift], blocks[shift], row_count, column_count, False)
        preact = part if preact is None else preact + part
    preact = preact + bias_vector[:, None]
    upstream = cotangent.reshape(own_channels, -1).astype(jnp.float32)
    grad_pre = (upstream * gelu_slope(preact)).astype(jnp.bfloat16)
    bias_part = jnp.sum(grad_pre.astype(jnp.float32), axis=1)
    input_local = jnp.concatenate(blocks, axis=0)
    taps = []
    for tap_row in range(3):
        row_taps = []
        for tap_col in range(3):
            window = window_of(input_local, tap_row, tap_col, row_count, column_count)
            row_taps.append(
                lax.dot_general(
                    grad_pre, window, (((1,), (1,)), ((), ())), preferred_element_type=jnp.float32
                )
            )
        taps.append(jnp.stack(row_taps))
    weight_part = jnp.stack(taps)
    flat = jnp.concatenate([weight_part.reshape(-1), bias_part])
    flat = all_sum(flat, jnp.bfloat16)
    weight_local = flat[: weight_part.size].reshape(weight_part.shape)
    bias_grad = flat[weight_part.size :]
    doubled = jnp.concatenate([weight_local, weight_local], axis=3)
    weight_grad = lax.dynamic_slice_in_dim(
        doubled, (chan_count - chan_index) % chan_count * own_channels, chan_count * own_channels, axis=3
    )
    grad_field = grad_pre.reshape(own_channels, row_count, column_count)
    grad_pad = mask_rims(padded_2(grad_field, (("lon", 2), ("lat", 1)), 1))
    received = []
    for shift in range(1, chan_count):
        kernel_t = jnp.swapaxes(kernel_cols[shift], 2, 3)
        part = conv_taps(kernel_t, grad_pad, row_count, column_count, True)
        pairs = [(i, (i + shift) % chan_count) for i in range(chan_count)]
        received.append(lax.ppermute(part.astype(jnp.bfloat16), "chan", pairs))
    own_part = conv_taps(jnp.swapaxes(kernel_cols[0], 2, 3), grad_pad, row_count, column_count, True)
    for piece in received:
        own_part = own_part + piece.astype(jnp.float32)
    input_grad = own_part.astype(jnp.bfloat16).reshape(own_channels, row_count, column_count)
    return (input_grad, weight_grad, bias_grad)


def solution(mesh):
    placed = (
        P("chan", ("groups", "lat"), "lon"),
        P("chan", ("groups", "lat"), "lon"),
        P(None, None, "chan", None),
        P("chan"),
    )
    return jax.shard_map(
        local,
        mesh=mesh,
        in_specs=placed,
        out_specs=(
            P("chan", ("groups", "lat"), "lon"),
            P("groups", None, "chan", None),
            P(("groups", "chan")),
        ),
        check_vma=False,
    )
```

```python
import jax
import jax.numpy as jnp
from jax import lax
from jax.sharding import PartitionSpec as P


def padded_2(shard, sides, width):
    for axis, dim in sides:
        devices, length = (lax.axis_size(axis), shard.shape[dim])
        up = [(i, (i + 1) % devices) for i in range(devices)]
        down = [(j, i) for i, j in up]
        last = lax.slice_in_dim(shard, length - width, length, axis=dim)
        initial = lax.slice_in_dim(shard, 0, width, axis=dim)
        before = lax.ppermute(last, axis, up)
        after = lax.ppermute(initial, axis, down)
        shard = jnp.concatenate([before, shard, after], axis=dim)
    return shard


def gelu_slope(preact):
    normal_cdf = 0.5 * (1.0 + jax.scipy.special.erf(preact * 0.7071067811865476))
    density = jnp.exp(-0.5 * preact * preact) * 0.3989422804014327
    return normal_cdf + preact * density


def mask_rims(padded):
    lat_index = lax.axis_index("lat")
    band_count = lax.axis_size("lat")
    row_ids = jnp.arange(padded.shape[1])
    outside = (row_ids == 0) & (lat_index == 0) | (row_ids == padded.shape[1] - 1) & (
        lat_index == band_count - 1
    )
    return jnp.where(outside[None, :, None], jnp.zeros((), padded.dtype), padded)


def window_of(field, first_row, first_col, row_count, column_count):
    return field[
        :, first_row : first_row + row_count, first_col : first_col + column_count
    ].reshape(field.shape[0], -1)


def conv_taps(kernel, field, row_count, column_count, flip):
    total = None
    for tap_row in range(3):
        for tap_col in range(3):
            if flip:
                window = window_of(field, 2 - tap_row, 2 - tap_col, row_count, column_count)
            else:
                window = window_of(field, tap_row, tap_col, row_count, column_count)
            part = jnp.dot(kernel[tap_row, tap_col], window, preferred_element_type=jnp.float32)
            total = part if total is None else total + part
    return total


def direct_reduce_scatter(rows, axis, send_dtype):
    count, index = lax.axis_size(axis), lax.axis_index(axis)
    if count == 1:
        return rows
    chunks = rows.reshape(count, -1, rows.shape[-1])
    acc = lax.dynamic_index_in_dim(chunks, index, keepdims=False)
    for step in range(1, count):
        pairs = [(j, (j + step) % count) for j in range(count)]
        piece = lax.dynamic_index_in_dim(chunks, (index + step) % count, keepdims=False)
        acc = acc + lax.ppermute(piece.astype(send_dtype), axis, pairs).astype(jnp.float32)
    return acc


def direct_all_gather(chunk, axis, send_dtype):
    count, index = lax.axis_size(axis), lax.axis_index(axis)
    if count == 1:
        return chunk
    pieces = [chunk]
    sent = chunk.astype(send_dtype)
    for step in range(1, count):
        pairs = [(j, (j + step) % count) for j in range(count)]
        pieces.append(lax.ppermute(sent, axis, pairs).astype(jnp.float32))
    stacked = jnp.stack(pieces[::-1])
    stacked = jnp.roll(stacked, (index + 1) % count, axis=0)
    return stacked.reshape(-1, chunk.shape[-1])


def sum_start(flat, send_dtype):
    parts = lax.axis_size("lat") * lax.axis_size("lon")
    quantum = parts * 8 * 128
    padded = jnp.pad(flat, (0, (-flat.size) % quantum)).reshape(-1, 128)
    rows = direct_reduce_scatter(padded, "lat", jnp.float32)
    return direct_reduce_scatter(rows, "lon", send_dtype)


def sum_finish(rows, size, send_dtype):
    rows = direct_all_gather(rows, "lon", send_dtype)
    rows = direct_all_gather(rows, "lat", jnp.float32)
    return rows.reshape(-1)[:size]


def border_of(padded):
    rows, cols = padded.shape[1], padded.shape[2]
    return jnp.concatenate(
        [padded[:, 0, :], padded[:, rows - 1, :], padded[:, 1 : rows - 1, 0], padded[:, 1 : rows - 1, cols - 1]],
        axis=1,
    )


def with_border(field, border):
    rows, cols = field.shape[1], field.shape[2]
    top = border[:, : cols + 2]
    bottom = border[:, cols + 2 : 2 * cols + 4]
    left = border[:, 2 * cols + 4 : 2 * cols + 4 + rows]
    right = border[:, 2 * cols + 4 + rows :]
    middle = jnp.concatenate([left[:, :, None], field, right[:, :, None]], axis=2)
    return jnp.concatenate([top[:, None, :], middle, bottom[:, None, :]], axis=1)


def local(inputs, cotangent, weight, bias_vector):
    own_channels, row_count, column_count = inputs.shape
    chan_count = lax.axis_size("chan")
    chan_index = lax.axis_index("chan")
    raw_blocks = []
    for shift in range(1, chan_count):
        pairs = [(i, (i - shift) % chan_count) for i in range(chan_count)]
        raw_blocks.append(lax.ppermute(inputs, "chan", pairs))
    input_pad = mask_rims(padded_2(inputs, (("lon", 2), ("lat", 1)), 1))
    own_border = border_of(input_pad)
    blocks = [input_pad]
    for shift in range(1, chan_count):
        pairs = [(i, (i - shift) % chan_count) for i in range(chan_count)]
        border = lax.ppermute(own_border, "chan", pairs)
        blocks.append(lax.optimization_barrier(with_border(raw_blocks[shift - 1], border)))
    kernel_cols = []
    for shift in range(chan_count):
        source = (chan_index + shift) % chan_count
        kernel_cols.append(
            lax.dynamic_slice_in_dim(weight, source * own_channels, own_channels, axis=3)
        )
    preact = None
    for shift in range(chan_count):
        part = conv_taps(kernel_cols[shift], blocks[shift], row_count, column_count, False)
        preact = part if preact is None else preact + part
    preact = preact + bias_vector[:, None]
    upstream = cotangent.reshape(own_channels, -1).astype(jnp.float32)
    grad_pre = (upstream * gelu_slope(preact)).astype(jnp.bfloat16)
    bias_part = jnp.sum(grad_pre.astype(jnp.float32), axis=1)
    input_local = jnp.concatenate(blocks, axis=0)
    taps = []
    for tap_row in range(3):
        row_taps = []
        for tap_col in range(3):
            window = window_of(input_local, tap_row, tap_col, row_count, column_count)
            row_taps.append(
                lax.dot_general(
                    grad_pre, window, (((1,), (1,)), ((), ())), preferred_element_type=jnp.float32
                )
            )
        taps.append(jnp.stack(row_taps))
    weight_part = jnp.stack(taps)
    flat = jnp.concatenate([weight_part.reshape(-1), bias_part])
    scattered = sum_start(flat, jnp.bfloat16)
    grad_pre, scattered = lax.optimization_barrier((grad_pre, scattered))
    flat = sum_finish(scattered, flat.size, jnp.bfloat16)
    weight_local = flat[: weight_part.size].reshape(weight_part.shape)
    bias_grad = flat[weight_part.size :]
    doubled = jnp.concatenate([weight_local, weight_local], axis=3)
    weight_grad = lax.dynamic_slice_in_dim(
        doubled, (chan_count - chan_index) % chan_count * own_channels, chan_count * own_channels, axis=3
    )
    grad_field = grad_pre.reshape(own_channels, row_count, column_count)
    grad_pad = mask_rims(padded_2(grad_field, (("lon", 2), ("lat", 1)), 1))
    received = []
    for shift in range(1, chan_count):
        kernel_t = jnp.swapaxes(kernel_cols[shift], 2, 3)
        part = conv_taps(kernel_t, grad_pad, row_count, column_count, True)
        pairs = [(i, (i + shift) % chan_count) for i in range(chan_count)]
        received.append(lax.ppermute(part.astype(jnp.bfloat16), "chan", pairs))
    own_part = conv_taps(jnp.swapaxes(kernel_cols[0], 2, 3), grad_pad, row_count, column_count, True)
    for piece in received:
        own_part = own_part + piece.astype(jnp.float32)
    input_grad = own_part.astype(jnp.bfloat16).reshape(own_channels, row_count, column_count)
    return (input_grad, weight_grad, bias_grad)


def solution(mesh):
    placed = (
        P("chan", ("groups", "lat"), "lon"),
        P("chan", ("groups", "lat"), "lon"),
        P(None, None, "chan", None),
        P("chan"),
    )
    return jax.shard_map(
        local,
        mesh=mesh,
        in_specs=placed,
        out_specs=(
            P("chan", ("groups", "lat"), "lon"),
            P("groups", None, "chan", None),
            P(("groups", "chan")),
        ),
        check_vma=False,
    )
```

```python
import jax
import jax.numpy as jnp
from jax import lax
from jax.sharding import PartitionSpec as P


def padded_2(shard, sides, width):
    for axis, dim in sides:
        devices, length = (lax.axis_size(axis), shard.shape[dim])
        up = [(i, (i + 1) % devices) for i in range(devices)]
        down = [(j, i) for i, j in up]
        last = lax.slice_in_dim(shard, length - width, length, axis=dim)
        initial = lax.slice_in_dim(shard, 0, width, axis=dim)
        before = lax.ppermute(last, axis, up)
        after = lax.ppermute(initial, axis, down)
        shard = jnp.concatenate([before, shard, after], axis=dim)
    return shard


def gelu_slope(preact):
    normal_cdf = 0.5 * (1.0 + jax.scipy.special.erf(preact * 0.7071067811865476))
    density = jnp.exp(-0.5 * preact * preact) * 0.3989422804014327
    return normal_cdf + preact * density


def mask_rims(padded):
    lat_index = lax.axis_index("lat")
    band_count = lax.axis_size("lat")
    row_ids = jnp.arange(padded.shape[1])
    outside = (row_ids == 0) & (lat_index == 0) | (row_ids == padded.shape[1] - 1) & (
        lat_index == band_count - 1
    )
    return jnp.where(outside[None, :, None], jnp.zeros((), padded.dtype), padded)


def window_of(field, first_row, first_col, row_count, column_count):
    return field[
        :, first_row : first_row + row_count, first_col : first_col + column_count
    ].reshape(field.shape[0], -1)


def conv_taps(kernel, field, row_count, column_count, flip):
    total = None
    for tap_row in range(3):
        for tap_col in range(3):
            if flip:
                window = window_of(field, 2 - tap_row, 2 - tap_col, row_count, column_count)
            else:
                window = window_of(field, tap_row, tap_col, row_count, column_count)
            part = jnp.dot(kernel[tap_row, tap_col], window, preferred_element_type=jnp.float32)
            total = part if total is None else total + part
    return total


def direct_reduce_scatter(rows, axis, send_dtype):
    count, index = lax.axis_size(axis), lax.axis_index(axis)
    if count == 1:
        return rows
    chunks = rows.reshape(count, -1, rows.shape[-1])
    acc = lax.dynamic_index_in_dim(chunks, index, keepdims=False)
    for step in range(1, count):
        pairs = [(j, (j + step) % count) for j in range(count)]
        piece = lax.dynamic_index_in_dim(chunks, (index + step) % count, keepdims=False)
        acc = acc + lax.ppermute(piece.astype(send_dtype), axis, pairs).astype(jnp.float32)
    return acc


def direct_all_gather(chunk, axis, send_dtype):
    count, index = lax.axis_size(axis), lax.axis_index(axis)
    if count == 1:
        return chunk
    pieces = [chunk]
    sent = chunk.astype(send_dtype)
    for step in range(1, count):
        pairs = [(j, (j + step) % count) for j in range(count)]
        pieces.append(lax.ppermute(sent, axis, pairs).astype(jnp.float32))
    stacked = jnp.stack(pieces[::-1])
    stacked = jnp.roll(stacked, (index + 1) % count, axis=0)
    return stacked.reshape(-1, chunk.shape[-1])


def sum_start(flat, send_dtype):
    parts = lax.axis_size("lat") * lax.axis_size("lon")
    quantum = parts * 8 * 128
    padded = jnp.pad(flat, (0, (-flat.size) % quantum)).reshape(-1, 128)
    rows = direct_reduce_scatter(padded, "lat", jnp.float32)
    return direct_reduce_scatter(rows, "lon", send_dtype)


def sum_finish(rows, size, send_dtype):
    rows = direct_all_gather(rows, "lon", send_dtype)
    rows = direct_all_gather(rows, "lat", jnp.float32)
    return rows.reshape(-1)[:size]


def border_of(padded):
    rows, cols = padded.shape[1], padded.shape[2]
    return jnp.concatenate(
        [padded[:, 0, :], padded[:, rows - 1, :], padded[:, 1 : rows - 1, 0], padded[:, 1 : rows - 1, cols - 1]],
        axis=1,
    )


def with_border(field, border):
    rows, cols = field.shape[1], field.shape[2]
    top = border[:, : cols + 2]
    bottom = border[:, cols + 2 : 2 * cols + 4]
    left = border[:, 2 * cols + 4 : 2 * cols + 4 + rows]
    right = border[:, 2 * cols + 4 + rows :]
    middle = jnp.concatenate([left[:, :, None], field, right[:, :, None]], axis=2)
    return jnp.concatenate([top[:, None, :], middle, bottom[:, None, :]], axis=1)


def local(inputs, cotangent, weight, bias_vector):
    own_channels, row_count, column_count = inputs.shape
    chan_count = lax.axis_size("chan")
    chan_index = lax.axis_index("chan")
    raw_blocks = []
    for shift in range(1, chan_count):
        pairs = [(i, (i - shift) % chan_count) for i in range(chan_count)]
        raw_blocks.append(lax.ppermute(inputs, "chan", pairs))
    input_pad = mask_rims(padded_2(inputs, (("lon", 2), ("lat", 1)), 1))
    own_border = border_of(input_pad)
    blocks = [input_pad]
    for shift in range(1, chan_count):
        pairs = [(i, (i - shift) % chan_count) for i in range(chan_count)]
        border = lax.ppermute(own_border, "chan", pairs)
        blocks.append(lax.optimization_barrier(with_border(raw_blocks[shift - 1], border)))
    kernel_cols = []
    for shift in range(chan_count):
        source = (chan_index + shift) % chan_count
        kernel_cols.append(
            lax.dynamic_slice_in_dim(weight, source * own_channels, own_channels, axis=3)
        )
    kernel_sends = []
    for shift in range(1, chan_count):
        target = (chan_index + shift) % chan_count
        kernel_sends.append(lax.dynamic_slice_in_dim(weight, target * own_channels, own_channels, axis=3))
    kernel_sends, _ = lax.optimization_barrier((kernel_sends, raw_blocks))
    kernel_blocks = []
    for shift in range(1, chan_count):
        pairs = [(i, (i + shift) % chan_count) for i in range(chan_count)]
        kernel_blocks.append(lax.ppermute(kernel_sends[shift - 1], "chan", pairs))
    preact = None
    for shift in range(chan_count):
        part = conv_taps(kernel_cols[shift], blocks[shift], row_count, column_count, False)
        preact = part if preact is None else preact + part
    preact = preact + bias_vector[:, None]
    upstream = cotangent.reshape(own_channels, -1).astype(jnp.float32)
    grad_pre = (upstream * gelu_slope(preact)).astype(jnp.bfloat16)
    bias_part = jnp.sum(grad_pre.astype(jnp.float32), axis=1)
    input_local = jnp.concatenate(blocks, axis=0)
    taps = []
    for tap_row in range(3):
        row_taps = []
        for tap_col in range(3):
            window = window_of(input_local, tap_row, tap_col, row_count, column_count)
            row_taps.append(
                lax.dot_general(
                    grad_pre, window, (((1,), (1,)), ((), ())), preferred_element_type=jnp.float32
                )
            )
        taps.append(jnp.stack(row_taps))
    weight_part = jnp.stack(taps)
    flat = jnp.concatenate([weight_part.reshape(-1), bias_part])
    scattered = sum_start(flat, jnp.bfloat16)
    grad_field = grad_pre.reshape(own_channels, row_count, column_count)
    grad_blocks = []
    for shift in range(1, chan_count):
        pairs = [(i, (i + shift) % chan_count) for i in range(chan_count)]
        grad_blocks.append(lax.ppermute(grad_field, "chan", pairs))
    grad_field, scattered = lax.optimization_barrier((grad_field, scattered))
    flat = sum_finish(scattered, flat.size, jnp.bfloat16)
    weight_local = flat[: weight_part.size].reshape(weight_part.shape)
    bias_grad = flat[weight_part.size :]
    doubled = jnp.concatenate([weight_local, weight_local], axis=3)
    weight_grad = lax.dynamic_slice_in_dim(
        doubled, (chan_count - chan_index) % chan_count * own_channels, chan_count * own_channels, axis=3
    )
    grad_pad = mask_rims(padded_2(grad_field, (("lon", 2), ("lat", 1)), 1))
    grad_border = border_of(grad_pad)
    input_sum = conv_taps(jnp.swapaxes(kernel_cols[0], 2, 3), grad_pad, row_count, column_count, True)
    for shift in range(1, chan_count):
        pairs = [(i, (i + shift) % chan_count) for i in range(chan_count)]
        border = lax.ppermute(grad_border, "chan", pairs)
        block = lax.optimization_barrier(with_border(grad_blocks[shift - 1], border))
        kernel_t = jnp.swapaxes(kernel_blocks[shift - 1], 2, 3)
        input_sum = input_sum + conv_taps(kernel_t, block, row_count, column_count, True)
    input_grad = input_sum.astype(jnp.bfloat16).reshape(own_channels, row_count, column_count)
    return (input_grad, weight_grad, bias_grad)


def solution(mesh):
    placed = (
        P("chan", ("groups", "lat"), "lon"),
        P("chan", ("groups", "lat"), "lon"),
        P(None, None, "chan", None),
        P("chan"),
    )
    return jax.shard_map(
        local,
        mesh=mesh,
        in_specs=placed,
        out_specs=(
            P("chan", ("groups", "lat"), "lon"),
            P("groups", None, "chan", None),
            P(("groups", "chan")),
        ),
        check_vma=False,
    )
```

```python
import jax
import jax.numpy as jnp
from jax import lax
from jax.sharding import PartitionSpec as P


def padded_2(shard, sides, width):
    for axis, dim in sides:
        devices, length = (lax.axis_size(axis), shard.shape[dim])
        up = [(i, (i + 1) % devices) for i in range(devices)]
        down = [(j, i) for i, j in up]
        last = lax.slice_in_dim(shard, length - width, length, axis=dim)
        initial = lax.slice_in_dim(shard, 0, width, axis=dim)
        before = lax.ppermute(last, axis, up)
        after = lax.ppermute(initial, axis, down)
        shard = jnp.concatenate([before, shard, after], axis=dim)
    return shard


def gelu_slope(preact):
    normal_cdf = 0.5 * (1.0 + jax.scipy.special.erf(preact * 0.7071067811865476))
    density = jnp.exp(-0.5 * preact * preact) * 0.3989422804014327
    return normal_cdf + preact * density


def mask_rims(padded):
    lat_index = lax.axis_index("lat")
    band_count = lax.axis_size("lat")
    row_ids = jnp.arange(padded.shape[1])
    outside = (row_ids == 0) & (lat_index == 0) | (row_ids == padded.shape[1] - 1) & (
        lat_index == band_count - 1
    )
    return jnp.where(outside[None, :, None], jnp.zeros((), padded.dtype), padded)


def window_of(field, first_row, first_col, row_count, column_count):
    return field[
        :, first_row : first_row + row_count, first_col : first_col + column_count
    ].reshape(field.shape[0], -1)


def conv_taps(kernel, field, row_count, column_count, flip):
    total = None
    for tap_row in range(3):
        for tap_col in range(3):
            if flip:
                window = window_of(field, 2 - tap_row, 2 - tap_col, row_count, column_count)
            else:
                window = window_of(field, tap_row, tap_col, row_count, column_count)
            part = jnp.dot(kernel[tap_row, tap_col], window, preferred_element_type=jnp.float32)
            total = part if total is None else total + part
    return total


def direct_reduce_scatter(rows, axis, send_dtype):
    count, index = lax.axis_size(axis), lax.axis_index(axis)
    if count == 1:
        return rows
    chunks = rows.reshape(count, -1, rows.shape[-1])
    acc = lax.dynamic_index_in_dim(chunks, index, keepdims=False)
    for step in range(1, count):
        pairs = [(j, (j + step) % count) for j in range(count)]
        piece = lax.dynamic_index_in_dim(chunks, (index + step) % count, keepdims=False)
        acc = acc + lax.ppermute(piece.astype(send_dtype), axis, pairs).astype(jnp.float32)
    return acc


def direct_all_gather(chunk, axis, send_dtype):
    count, index = lax.axis_size(axis), lax.axis_index(axis)
    if count == 1:
        return chunk
    pieces = [chunk]
    sent = chunk.astype(send_dtype)
    for step in range(1, count):
        pairs = [(j, (j + step) % count) for j in range(count)]
        pieces.append(lax.ppermute(sent, axis, pairs).astype(jnp.float32))
    stacked = jnp.stack(pieces[::-1])
    stacked = jnp.roll(stacked, (index + 1) % count, axis=0)
    return stacked.reshape(-1, chunk.shape[-1])


def sum_start(flat, send_dtype):
    parts = lax.axis_size("lat") * lax.axis_size("lon")
    quantum = parts * 8 * 128
    padded = jnp.pad(flat, (0, (-flat.size) % quantum)).reshape(-1, 128)
    rows = direct_reduce_scatter(padded, "lat", jnp.float32)
    return direct_reduce_scatter(rows, "lon", send_dtype)


def sum_finish(rows, size, send_dtype):
    rows = direct_all_gather(rows, "lon", send_dtype)
    rows = direct_all_gather(rows, "lat", jnp.float32)
    return rows.reshape(-1)[:size]


def border_of(padded):
    rows, cols = padded.shape[1], padded.shape[2]
    return jnp.concatenate(
        [padded[:, 0, :], padded[:, rows - 1, :], padded[:, 1 : rows - 1, 0], padded[:, 1 : rows - 1, cols - 1]],
        axis=1,
    )


def with_border(field, border):
    rows, cols = field.shape[1], field.shape[2]
    top = border[:, : cols + 2]
    bottom = border[:, cols + 2 : 2 * cols + 4]
    left = border[:, 2 * cols + 4 : 2 * cols + 4 + rows]
    right = border[:, 2 * cols + 4 + rows :]
    middle = jnp.concatenate([left[:, :, None], field, right[:, :, None]], axis=2)
    return jnp.concatenate([top[:, None, :], middle, bottom[:, None, :]], axis=1)


def local(inputs, cotangent, weight, bias_vector):
    own_channels, row_count, column_count = inputs.shape
    chan_count = lax.axis_size("chan")
    chan_index = lax.axis_index("chan")
    raw_blocks = []
    for shift in range(1, chan_count):
        pairs = [(i, (i - shift) % chan_count) for i in range(chan_count)]
        raw_blocks.append(lax.ppermute(inputs, "chan", pairs))
    input_pad = mask_rims(padded_2(inputs, (("lon", 2), ("lat", 1)), 1))
    own_border = border_of(input_pad)
    blocks = [input_pad]
    for shift in range(1, chan_count):
        pairs = [(i, (i - shift) % chan_count) for i in range(chan_count)]
        border = lax.ppermute(own_border, "chan", pairs)
        blocks.append(lax.optimization_barrier(with_border(raw_blocks[shift - 1], border)))
    kernel_cols = []
    for shift in range(chan_count):
        source = (chan_index + shift) % chan_count
        kernel_cols.append(
            lax.dynamic_slice_in_dim(weight, source * own_channels, own_channels, axis=3)
        )
    kernel_sends = []
    for shift in range(1, chan_count):
        target = (chan_index + shift) % chan_count
        kernel_sends.append(lax.dynamic_slice_in_dim(weight, target * own_channels, own_channels, axis=3))
    kernel_sends, _ = lax.optimization_barrier((kernel_sends, raw_blocks))
    kernel_blocks = []
    for shift in range(1, chan_count):
        pairs = [(i, (i + shift) % chan_count) for i in range(chan_count)]
        kernel_blocks.append(lax.ppermute(kernel_sends[shift - 1], "chan", pairs))
    preact = None
    for shift in range(chan_count):
        part = conv_taps(kernel_cols[shift], blocks[shift], row_count, column_count, False)
        preact = part if preact is None else preact + part
    preact = preact + bias_vector[:, None]
    upstream = cotangent.reshape(own_channels, -1).astype(jnp.float32)
    grad_pre = (upstream * gelu_slope(preact)).astype(jnp.bfloat16)
    grad_pre, kernel_blocks = lax.optimization_barrier((grad_pre, kernel_blocks))
    bias_part = jnp.sum(grad_pre.astype(jnp.float32), axis=1)
    input_local = jnp.concatenate(blocks, axis=0)
    taps = []
    for tap_row in range(3):
        row_taps = []
        for tap_col in range(3):
            window = window_of(input_local, tap_row, tap_col, row_count, column_count)
            row_taps.append(
                lax.dot_general(
                    grad_pre, window, (((1,), (1,)), ((), ())), preferred_element_type=jnp.float32
                )
            )
        taps.append(jnp.stack(row_taps))
    weight_part = jnp.stack(taps)
    flat = jnp.concatenate([weight_part.reshape(-1), bias_part])
    scattered = sum_start(flat, jnp.bfloat16)
    grad_field = grad_pre.reshape(own_channels, row_count, column_count)
    grad_blocks = []
    for shift in range(1, chan_count):
        pairs = [(i, (i + shift) % chan_count) for i in range(chan_count)]
        grad_blocks.append(lax.ppermute(grad_field, "chan", pairs))
    grad_field, scattered, grad_blocks = lax.optimization_barrier((grad_field, scattered, grad_blocks))
    flat = sum_finish(scattered, flat.size, jnp.bfloat16)
    weight_local = flat[: weight_part.size].reshape(weight_part.shape)
    bias_grad = flat[weight_part.size :]
    doubled = jnp.concatenate([weight_local, weight_local], axis=3)
    weight_grad = lax.dynamic_slice_in_dim(
        doubled, (chan_count - chan_index) % chan_count * own_channels, chan_count * own_channels, axis=3
    )
    grad_pad = mask_rims(padded_2(grad_field, (("lon", 2), ("lat", 1)), 1))
    grad_border = border_of(grad_pad)
    input_sum = conv_taps(jnp.swapaxes(kernel_cols[0], 2, 3), grad_pad, row_count, column_count, True)
    for shift in range(1, chan_count):
        pairs = [(i, (i + shift) % chan_count) for i in range(chan_count)]
        border = lax.ppermute(grad_border, "chan", pairs)
        block = lax.optimization_barrier(with_border(grad_blocks[shift - 1], border))
        kernel_t = jnp.swapaxes(kernel_blocks[shift - 1], 2, 3)
        input_sum = input_sum + conv_taps(kernel_t, block, row_count, column_count, True)
    input_grad = input_sum.astype(jnp.bfloat16).reshape(own_channels, row_count, column_count)
    return (input_grad, weight_grad, bias_grad)


def solution(mesh):
    placed = (
        P("chan", ("groups", "lat"), "lon"),
        P("chan", ("groups", "lat"), "lon"),
        P(None, None, "chan", None),
        P("chan"),
    )
    return jax.shard_map(
        local,
        mesh=mesh,
        in_specs=placed,
        out_specs=(
            P("chan", ("groups", "lat"), "lon"),
            P("groups", None, "chan", None),
            P(("groups", "chan")),
        ),
        check_vma=False,
    )
```

```python
import jax
import jax.numpy as jnp
from jax import lax
from jax.sharding import PartitionSpec as P


def padded_2(shard, sides, width):
    for axis, dim in sides:
        devices, length = (lax.axis_size(axis), shard.shape[dim])
        up = [(i, (i + 1) % devices) for i in range(devices)]
        down = [(j, i) for i, j in up]
        last = lax.slice_in_dim(shard, length - width, length, axis=dim)
        initial = lax.slice_in_dim(shard, 0, width, axis=dim)
        before = lax.ppermute(last, axis, up)
        after = lax.ppermute(initial, axis, down)
        shard = jnp.concatenate([before, shard, after], axis=dim)
    return shard


def gelu_slope(preact):
    normal_cdf = 0.5 * (1.0 + jax.scipy.special.erf(preact * 0.7071067811865476))
    density = jnp.exp(-0.5 * preact * preact) * 0.3989422804014327
    return normal_cdf + preact * density


def mask_rims(padded):
    lat_index = lax.axis_index("lat")
    band_count = lax.axis_size("lat")
    row_ids = jnp.arange(padded.shape[1])
    outside = (row_ids == 0) & (lat_index == 0) | (row_ids == padded.shape[1] - 1) & (
        lat_index == band_count - 1
    )
    return jnp.where(outside[None, :, None], jnp.zeros((), padded.dtype), padded)


def window_of(field, first_row, first_col, row_count, column_count):
    return field[
        :, first_row : first_row + row_count, first_col : first_col + column_count
    ].reshape(field.shape[0], -1)


def conv_taps(kernel, field, row_count, column_count, flip):
    total = None
    for tap_row in range(3):
        for tap_col in range(3):
            if flip:
                window = window_of(field, 2 - tap_row, 2 - tap_col, row_count, column_count)
            else:
                window = window_of(field, tap_row, tap_col, row_count, column_count)
            part = jnp.dot(kernel[tap_row, tap_col], window, preferred_element_type=jnp.float32)
            total = part if total is None else total + part
    return total


def direct_reduce_scatter(rows, axis, send_dtype):
    count, index = lax.axis_size(axis), lax.axis_index(axis)
    if count == 1:
        return rows
    chunks = rows.reshape(count, -1, rows.shape[-1])
    acc = lax.dynamic_index_in_dim(chunks, index, keepdims=False)
    for step in range(1, count):
        pairs = [(j, (j + step) % count) for j in range(count)]
        piece = lax.dynamic_index_in_dim(chunks, (index + step) % count, keepdims=False)
        acc = acc + lax.ppermute(piece.astype(send_dtype), axis, pairs).astype(jnp.float32)
    return acc


def direct_all_gather(chunk, axis, send_dtype):
    count, index = lax.axis_size(axis), lax.axis_index(axis)
    if count == 1:
        return chunk
    pieces = [chunk]
    sent = chunk.astype(send_dtype)
    for step in range(1, count):
        pairs = [(j, (j + step) % count) for j in range(count)]
        pieces.append(lax.ppermute(sent, axis, pairs).astype(jnp.float32))
    stacked = jnp.stack(pieces[::-1])
    stacked = jnp.roll(stacked, (index + 1) % count, axis=0)
    return stacked.reshape(-1, chunk.shape[-1])


def sum_start(flat, send_dtype, columns):
    parts = lax.axis_size("lat") * lax.axis_size("lon")
    quantum = parts * 16 * 128
    padded = jnp.pad(flat, (0, (-flat.size) % quantum)).reshape(-1, 128)
    rows = direct_reduce_scatter(padded, "lat", jnp.float32)
    count, index = lax.axis_size("lon"), lax.axis_index("lon")
    last, first = columns
    if count < 3:
        up = [(i, (i + 1) % count) for i in range(count)]
        down = [(j, i) for i, j in up]
        halo = (lax.ppermute(last, "lon", up), lax.ppermute(first, "lon", down))
        return direct_reduce_scatter(rows, "lon", send_dtype), halo
    chunks = rows.reshape(count, -1, rows.shape[-1])
    size = chunks.shape[1]
    acc = lax.dynamic_index_in_dim(chunks, index, keepdims=False)
    extra = {1: last, count - 1: first}
    got = {}
    for step in range(1, count):
        pairs = [(j, (j + step) % count) for j in range(count)]
        piece = lax.dynamic_index_in_dim(chunks, (index + step) % count, keepdims=False).astype(send_dtype)
        if step in extra:
            piece = jnp.concatenate([piece, extra[step].astype(send_dtype).reshape(-1, rows.shape[-1])], axis=0)
        moved = lax.ppermute(piece, "lon", pairs)
        acc = acc + moved[:size].astype(jnp.float32)
        if step in extra:
            got[step] = moved[size:].reshape(last.shape).astype(last.dtype)
    return acc, (got[1], got[count - 1])


def sum_finish(rows, size, send_dtype):
    rows = direct_all_gather(rows, "lon", send_dtype)
    rows = direct_all_gather(rows, "lat", jnp.float32)
    return rows.reshape(-1)[:size]


def border_of(padded):
    rows, cols = padded.shape[1], padded.shape[2]
    return jnp.concatenate(
        [padded[:, 0, :], padded[:, rows - 1, :], padded[:, 1 : rows - 1, 0], padded[:, 1 : rows - 1, cols - 1]],
        axis=1,
    )


def with_border(field, border):
    rows, cols = field.shape[1], field.shape[2]
    top = border[:, : cols + 2]
    bottom = border[:, cols + 2 : 2 * cols + 4]
    left = border[:, 2 * cols + 4 : 2 * cols + 4 + rows]
    right = border[:, 2 * cols + 4 + rows :]
    middle = jnp.concatenate([left[:, :, None], field, right[:, :, None]], axis=2)
    return jnp.concatenate([top[:, None, :], middle, bottom[:, None, :]], axis=1)


def local(inputs, cotangent, weight, bias_vector):
    own_channels, row_count, column_count = inputs.shape
    chan_count = lax.axis_size("chan")
    chan_index = lax.axis_index("chan")
    raw_blocks = []
    for shift in range(1, chan_count):
        pairs = [(i, (i - shift) % chan_count) for i in range(chan_count)]
        raw_blocks.append(lax.ppermute(inputs, "chan", pairs))
    input_pad = mask_rims(padded_2(inputs, (("lon", 2), ("lat", 1)), 1))
    own_border = border_of(input_pad)
    blocks = [input_pad]
    for shift in range(1, chan_count):
        pairs = [(i, (i - shift) % chan_count) for i in range(chan_count)]
        border = lax.ppermute(own_border, "chan", pairs)
        blocks.append(lax.optimization_barrier(with_border(raw_blocks[shift - 1], border)))
    kernel_cols = []
    for shift in range(chan_count):
        source = (chan_index + shift) % chan_count
        kernel_cols.append(
            lax.dynamic_slice_in_dim(weight, source * own_channels, own_channels, axis=3)
        )
    preact = None
    for shift in range(chan_count):
        part = conv_taps(kernel_cols[shift], blocks[shift], row_count, column_count, False)
        preact = part if preact is None else preact + part
    preact = preact + bias_vector[:, None]
    upstream = cotangent.reshape(own_channels, -1).astype(jnp.float32)
    grad_pre = (upstream * gelu_slope(preact)).astype(jnp.bfloat16)
    bias_part = jnp.sum(grad_pre.astype(jnp.float32), axis=1)
    input_local = jnp.concatenate(blocks, axis=0)
    taps = []
    for tap_row in range(3):
        row_taps = []
        for tap_col in range(3):
            window = window_of(input_local, tap_row, tap_col, row_count, column_count)
            row_taps.append(
                lax.dot_general(
                    grad_pre, window, (((1,), (1,)), ((), ())), preferred_element_type=jnp.float32
                )
            )
        taps.append(jnp.stack(row_taps))
    weight_part = jnp.stack(taps)
    flat = jnp.concatenate([weight_part.reshape(-1), bias_part])
    grad_field = grad_pre.reshape(own_channels, row_count, column_count)
    edges = (grad_field[:, :, column_count - 1 :], grad_field[:, :, :1])
    scattered, (before, after) = sum_start(flat, jnp.bfloat16, edges)
    flat = sum_finish(scattered, flat.size, jnp.bfloat16)
    weight_local = flat[: weight_part.size].reshape(weight_part.shape)
    bias_grad = flat[weight_part.size :]
    doubled = jnp.concatenate([weight_local, weight_local], axis=3)
    weight_grad = lax.dynamic_slice_in_dim(
        doubled, (chan_count - chan_index) % chan_count * own_channels, chan_count * own_channels, axis=3
    )
    grad_wide = jnp.concatenate([before, grad_field, after], axis=2)
    grad_pad = mask_rims(padded_2(grad_wide, (("lat", 1),), 1))
    received = []
    for shift in range(1, chan_count):
        kernel_t = jnp.swapaxes(kernel_cols[shift], 2, 3)
        part = conv_taps(kernel_t, grad_pad, row_count, column_count, True)
        pairs = [(i, (i + shift) % chan_count) for i in range(chan_count)]
        received.append(lax.ppermute(part.astype(jnp.bfloat16), "chan", pairs))
    own_part = conv_taps(jnp.swapaxes(kernel_cols[0], 2, 3), grad_pad, row_count, column_count, True)
    for piece in received:
        own_part = own_part + piece.astype(jnp.float32)
    input_grad = own_part.astype(jnp.bfloat16).reshape(own_channels, row_count, column_count)
    return (input_grad, weight_grad, bias_grad)


def solution(mesh):
    placed = (
        P("chan", ("groups", "lat"), "lon"),
        P("chan", ("groups", "lat"), "lon"),
        P(None, None, "chan", None),
        P("chan"),
    )
    return jax.shard_map(
        local,
        mesh=mesh,
        in_specs=placed,
        out_specs=(
            P("chan", ("groups", "lat"), "lon"),
            P("groups", None, "chan", None),
            P(("groups", "chan")),
        ),
        check_vma=False,
    )
```

```python
import jax
import jax.numpy as jnp
from jax import lax
from jax.sharding import PartitionSpec as P


def padded_2(shard, sides, width):
    for axis, dim in sides:
        devices, length = (lax.axis_size(axis), shard.shape[dim])
        up = [(i, (i + 1) % devices) for i in range(devices)]
        down = [(j, i) for i, j in up]
        last = lax.slice_in_dim(shard, length - width, length, axis=dim)
        initial = lax.slice_in_dim(shard, 0, width, axis=dim)
        before = lax.ppermute(last, axis, up)
        after = lax.ppermute(initial, axis, down)
        shard = jnp.concatenate([before, shard, after], axis=dim)
    return shard


def gelu_slope(preact):
    normal_cdf = 0.5 * (1.0 + jax.scipy.special.erf(preact * 0.7071067811865476))
    density = jnp.exp(-0.5 * preact * preact) * 0.3989422804014327
    return normal_cdf + preact * density


def mask_rims(padded):
    lat_index = lax.axis_index("lat")
    band_count = lax.axis_size("lat")
    row_ids = jnp.arange(padded.shape[1])
    outside = (row_ids == 0) & (lat_index == 0) | (row_ids == padded.shape[1] - 1) & (
        lat_index == band_count - 1
    )
    return jnp.where(outside[None, :, None], jnp.zeros((), padded.dtype), padded)


def window_of(field, first_row, first_col, row_count, column_count):
    return field[
        :, first_row : first_row + row_count, first_col : first_col + column_count
    ].reshape(field.shape[0], -1)


def conv_taps(kernel, field, row_count, column_count, flip):
    total = None
    for tap_row in range(3):
        for tap_col in range(3):
            if flip:
                window = window_of(field, 2 - tap_row, 2 - tap_col, row_count, column_count)
            else:
                window = window_of(field, tap_row, tap_col, row_count, column_count)
            part = jnp.dot(kernel[tap_row, tap_col], window, preferred_element_type=jnp.float32)
            total = part if total is None else total + part
    return total


def direct_reduce_scatter(rows, axis, send_dtype):
    count, index = lax.axis_size(axis), lax.axis_index(axis)
    if count == 1:
        return rows
    chunks = rows.reshape(count, -1, rows.shape[-1])
    acc = lax.dynamic_index_in_dim(chunks, index, keepdims=False)
    for step in range(1, count):
        pairs = [(j, (j + step) % count) for j in range(count)]
        piece = lax.dynamic_index_in_dim(chunks, (index + step) % count, keepdims=False)
        acc = acc + lax.ppermute(piece.astype(send_dtype), axis, pairs).astype(jnp.float32)
    return acc


def direct_all_gather(chunk, axis, send_dtype):
    count, index = lax.axis_size(axis), lax.axis_index(axis)
    if count == 1:
        return chunk
    pieces = [chunk]
    sent = chunk.astype(send_dtype)
    for step in range(1, count):
        pairs = [(j, (j + step) % count) for j in range(count)]
        pieces.append(lax.ppermute(sent, axis, pairs).astype(jnp.float32))
    stacked = jnp.stack(pieces[::-1])
    stacked = jnp.roll(stacked, (index + 1) % count, axis=0)
    return stacked.reshape(-1, chunk.shape[-1])


def sum_start(flat, send_dtype, columns):
    parts = lax.axis_size("lat") * lax.axis_size("lon")
    quantum = parts * 16 * 128
    padded = jnp.pad(flat, (0, (-flat.size) % quantum)).reshape(-1, 128)
    rows = direct_reduce_scatter(padded, "lat", jnp.float32)
    count, index = lax.axis_size("lon"), lax.axis_index("lon")
    last, first = columns
    if count < 3:
        up = [(i, (i + 1) % count) for i in range(count)]
        down = [(j, i) for i, j in up]
        halo = (lax.ppermute(last, "lon", up), lax.ppermute(first, "lon", down))
        return direct_reduce_scatter(rows, "lon", send_dtype), halo
    chunks = rows.reshape(count, -1, rows.shape[-1])
    size = chunks.shape[1]
    acc = lax.dynamic_index_in_dim(chunks, index, keepdims=False)
    extra = {1: last, count - 1: first}
    got = {}
    for step in range(1, count):
        pairs = [(j, (j + step) % count) for j in range(count)]
        piece = lax.dynamic_index_in_dim(chunks, (index + step) % count, keepdims=False).astype(send_dtype)
        if step in extra:
            piece = jnp.concatenate([piece, extra[step].astype(send_dtype).reshape(-1, rows.shape[-1])], axis=0)
        moved = lax.ppermute(piece, "lon", pairs)
        acc = acc + moved[:size].astype(jnp.float32)
        if step in extra:
            got[step] = moved[size:].reshape(last.shape).astype(last.dtype)
    return acc, (got[1], got[count - 1])


def sum_finish(rows, size, send_dtype):
    rows = direct_all_gather(rows, "lon", send_dtype)
    rows = direct_all_gather(rows, "lat", jnp.float32)
    return rows.reshape(-1)[:size]


def border_of(padded):
    rows, cols = padded.shape[1], padded.shape[2]
    return jnp.concatenate(
        [padded[:, 0, :], padded[:, rows - 1, :], padded[:, 1 : rows - 1, 0], padded[:, 1 : rows - 1, cols - 1]],
        axis=1,
    )


def with_border(field, border):
    rows, cols = field.shape[1], field.shape[2]
    top = border[:, : cols + 2]
    bottom = border[:, cols + 2 : 2 * cols + 4]
    left = border[:, 2 * cols + 4 : 2 * cols + 4 + rows]
    right = border[:, 2 * cols + 4 + rows :]
    middle = jnp.concatenate([left[:, :, None], field, right[:, :, None]], axis=2)
    return jnp.concatenate([top[:, None, :], middle, bottom[:, None, :]], axis=1)


def local(inputs, cotangent, weight, bias_vector):
    own_channels, row_count, column_count = inputs.shape
    chan_count = lax.axis_size("chan")
    chan_index = lax.axis_index("chan")
    raw_blocks = []
    for shift in range(1, chan_count):
        pairs = [(i, (i - shift) % chan_count) for i in range(chan_count)]
        raw_blocks.append(lax.ppermute(inputs, "chan", pairs))
    input_pad = mask_rims(padded_2(inputs, (("lon", 2), ("lat", 1)), 1))
    own_border = border_of(input_pad)
    blocks = [input_pad]
    for shift in range(1, chan_count):
        pairs = [(i, (i - shift) % chan_count) for i in range(chan_count)]
        border = lax.ppermute(own_border, "chan", pairs)
        blocks.append(lax.optimization_barrier(with_border(raw_blocks[shift - 1], border)))
    kernel_cols = []
    for shift in range(chan_count):
        source = (chan_index + shift) % chan_count
        kernel_cols.append(
            lax.dynamic_slice_in_dim(weight, source * own_channels, own_channels, axis=3)
        )
    kernel_sends = []
    for shift in range(1, chan_count):
        target = (chan_index + shift) % chan_count
        kernel_sends.append(lax.dynamic_slice_in_dim(weight, target * own_channels, own_channels, axis=3))
    kernel_sends, _ = lax.optimization_barrier((kernel_sends, raw_blocks))
    kernel_blocks = []
    for shift in range(1, chan_count):
        pairs = [(i, (i + shift) % chan_count) for i in range(chan_count)]
        kernel_blocks.append(lax.ppermute(kernel_sends[shift - 1], "chan", pairs))
    preact = None
    for shift in range(chan_count):
        part = conv_taps(kernel_cols[shift], blocks[shift], row_count, column_count, False)
        preact = part if preact is None else preact + part
    preact = preact + bias_vector[:, None]
    upstream = cotangent.reshape(own_channels, -1).astype(jnp.float32)
    grad_pre = (upstream * gelu_slope(preact)).astype(jnp.bfloat16)
    grad_pre, kernel_blocks = lax.optimization_barrier((grad_pre, kernel_blocks))
    bias_part = jnp.sum(grad_pre.astype(jnp.float32), axis=1)
    input_local = jnp.concatenate(blocks, axis=0)
    taps = []
    for tap_row in range(3):
        row_taps = []
        for tap_col in range(3):
            window = window_of(input_local, tap_row, tap_col, row_count, column_count)
            row_taps.append(
                lax.dot_general(
                    grad_pre, window, (((1,), (1,)), ((), ())), preferred_element_type=jnp.float32
                )
            )
        taps.append(jnp.stack(row_taps))
    weight_part = jnp.stack(taps)
    flat = jnp.concatenate([weight_part.reshape(-1), bias_part])
    grad_field = grad_pre.reshape(own_channels, row_count, column_count)
    edges = (grad_field[:, :, column_count - 1 :], grad_field[:, :, :1])
    scattered, (before, after) = sum_start(flat, jnp.bfloat16, edges)
    grad_blocks = []
    for shift in range(1, chan_count):
        pairs = [(i, (i + shift) % chan_count) for i in range(chan_count)]
        grad_blocks.append(lax.ppermute(grad_field, "chan", pairs))
    scattered, grad_blocks = lax.optimization_barrier((scattered, grad_blocks))
    flat = sum_finish(scattered, flat.size, jnp.bfloat16)
    weight_local = flat[: weight_part.size].reshape(weight_part.shape)
    bias_grad = flat[weight_part.size :]
    doubled = jnp.concatenate([weight_local, weight_local], axis=3)
    weight_grad = lax.dynamic_slice_in_dim(
        doubled, (chan_count - chan_index) % chan_count * own_channels, chan_count * own_channels, axis=3
    )
    grad_wide = jnp.concatenate([before, grad_field, after], axis=2)
    grad_pad = mask_rims(padded_2(grad_wide, (("lat", 1),), 1))
    grad_border = border_of(grad_pad)
    input_sum = conv_taps(jnp.swapaxes(kernel_cols[0], 2, 3), grad_pad, row_count, column_count, True)
    for shift in range(1, chan_count):
        pairs = [(i, (i + shift) % chan_count) for i in range(chan_count)]
        border = lax.ppermute(grad_border, "chan", pairs)
        block = lax.optimization_barrier(with_border(grad_blocks[shift - 1], border))
        kernel_t = jnp.swapaxes(kernel_blocks[shift - 1], 2, 3)
        input_sum = input_sum + conv_taps(kernel_t, block, row_count, column_count, True)
    input_grad = input_sum.astype(jnp.bfloat16).reshape(own_channels, row_count, column_count)
    return (input_grad, weight_grad, bias_grad)


def solution(mesh):
    placed = (
        P("chan", ("groups", "lat"), "lon"),
        P("chan", ("groups", "lat"), "lon"),
        P(None, None, "chan", None),
        P("chan"),
    )
    return jax.shard_map(
        local,
        mesh=mesh,
        in_specs=placed,
        out_specs=(
            P("chan", ("groups", "lat"), "lon"),
            P("groups", None, "chan", None),
            P(("groups", "chan")),
        ),
        check_vma=False,
    )
```

```python
import jax
import jax.numpy as jnp
from jax import lax
from jax.sharding import PartitionSpec as P


def padded_2(shard, sides, width):
    for axis, dim in sides:
        devices, length = (lax.axis_size(axis), shard.shape[dim])
        up = [(i, (i + 1) % devices) for i in range(devices)]
        down = [(j, i) for i, j in up]
        last = lax.slice_in_dim(shard, length - width, length, axis=dim)
        initial = lax.slice_in_dim(shard, 0, width, axis=dim)
        before = lax.ppermute(last, axis, up)
        after = lax.ppermute(initial, axis, down)
        shard = jnp.concatenate([before, shard, after], axis=dim)
    return shard


def gelu_slope(preact):
    normal_cdf = 0.5 * (1.0 + jax.scipy.special.erf(preact * 0.7071067811865476))
    density = jnp.exp(-0.5 * preact * preact) * 0.3989422804014327
    return normal_cdf + preact * density


def mask_rims(padded):
    lat_index = lax.axis_index("lat")
    band_count = lax.axis_size("lat")
    row_ids = jnp.arange(padded.shape[1])
    outside = (row_ids == 0) & (lat_index == 0) | (row_ids == padded.shape[1] - 1) & (
        lat_index == band_count - 1
    )
    return jnp.where(outside[None, :, None], jnp.zeros((), padded.dtype), padded)


def window_of(field, first_row, first_col, row_count, column_count):
    return field[
        :, first_row : first_row + row_count, first_col : first_col + column_count
    ].reshape(field.shape[0], -1)


def conv_taps(kernel, field, row_count, column_count, flip):
    total = None
    for tap_row in range(3):
        for tap_col in range(3):
            if flip:
                window = window_of(field, 2 - tap_row, 2 - tap_col, row_count, column_count)
            else:
                window = window_of(field, tap_row, tap_col, row_count, column_count)
            part = jnp.dot(kernel[tap_row, tap_col], window, preferred_element_type=jnp.float32)
            total = part if total is None else total + part
    return total


def direct_reduce_scatter(rows, axis, send_dtype):
    count, index = lax.axis_size(axis), lax.axis_index(axis)
    if count == 1:
        return rows
    chunks = rows.reshape(count, -1, rows.shape[-1])
    acc = lax.dynamic_index_in_dim(chunks, index, keepdims=False)
    for step in range(1, count):
        pairs = [(j, (j + step) % count) for j in range(count)]
        piece = lax.dynamic_index_in_dim(chunks, (index + step) % count, keepdims=False)
        acc = acc + lax.ppermute(piece.astype(send_dtype), axis, pairs).astype(jnp.float32)
    return acc


def direct_all_gather(chunk, axis, send_dtype):
    count, index = lax.axis_size(axis), lax.axis_index(axis)
    if count == 1:
        return chunk
    pieces = [chunk]
    sent = chunk.astype(send_dtype)
    for step in range(1, count):
        pairs = [(j, (j + step) % count) for j in range(count)]
        pieces.append(lax.ppermute(sent, axis, pairs).astype(jnp.float32))
    stacked = jnp.stack(pieces[::-1])
    stacked = jnp.roll(stacked, (index + 1) % count, axis=0)
    return stacked.reshape(-1, chunk.shape[-1])


def sum_start(flat, send_dtype, columns):
    parts = lax.axis_size("lat") * lax.axis_size("lon")
    quantum = parts * 16 * 128
    padded = jnp.pad(flat, (0, (-flat.size) % quantum)).reshape(-1, 128)
    rows = direct_reduce_scatter(padded, "lat", jnp.float32)
    count, index = lax.axis_size("lon"), lax.axis_index("lon")
    last, first = columns
    if count < 3:
        up = [(i, (i + 1) % count) for i in range(count)]
        down = [(j, i) for i, j in up]
        halo = (lax.ppermute(last, "lon", up), lax.ppermute(first, "lon", down))
        return direct_reduce_scatter(rows, "lon", send_dtype), halo
    chunks = rows.reshape(count, -1, rows.shape[-1])
    size = chunks.shape[1]
    acc = lax.dynamic_index_in_dim(chunks, index, keepdims=False)
    extra = {1: last, count - 1: first}
    got = {}
    for step in range(1, count):
        pairs = [(j, (j + step) % count) for j in range(count)]
        piece = lax.dynamic_index_in_dim(chunks, (index + step) % count, keepdims=False).astype(send_dtype)
        if step in extra:
            piece = jnp.concatenate([piece, extra[step].astype(send_dtype).reshape(-1, rows.shape[-1])], axis=0)
        moved = lax.ppermute(piece, "lon", pairs)
        acc = acc + moved[:size].astype(jnp.float32)
        if step in extra:
            got[step] = moved[size:].reshape(last.shape).astype(last.dtype)
    return acc, (got[1], got[count - 1])


def sum_finish(rows, size, send_dtype):
    rows = direct_all_gather(rows, "lon", send_dtype)
    rows = direct_all_gather(rows, "lat", jnp.float32)
    return rows.reshape(-1)[:size]


def border_of(padded):
    rows, cols = padded.shape[1], padded.shape[2]
    return jnp.concatenate(
        [padded[:, 0, :], padded[:, rows - 1, :], padded[:, 1 : rows - 1, 0], padded[:, 1 : rows - 1, cols - 1]],
        axis=1,
    )


def with_border(field, border):
    rows, cols = field.shape[1], field.shape[2]
    top = border[:, : cols + 2]
    bottom = border[:, cols + 2 : 2 * cols + 4]
    left = border[:, 2 * cols + 4 : 2 * cols + 4 + rows]
    right = border[:, 2 * cols + 4 + rows :]
    middle = jnp.concatenate([left[:, :, None], field, right[:, :, None]], axis=2)
    return jnp.concatenate([top[:, None, :], middle, bottom[:, None, :]], axis=1)


def local(inputs, cotangent, weight, bias_vector):
    own_channels, row_count, column_count = inputs.shape
    chan_count = lax.axis_size("chan")
    chan_index = lax.axis_index("chan")
    raw_blocks = []
    for shift in range(1, chan_count):
        pairs = [(i, (i - shift) % chan_count) for i in range(chan_count)]
        raw_blocks.append(lax.ppermute(inputs, "chan", pairs))
    input_pad = mask_rims(padded_2(inputs, (("lon", 2), ("lat", 1)), 1))
    own_border = border_of(input_pad)
    blocks = [input_pad]
    for shift in range(1, chan_count):
        pairs = [(i, (i - shift) % chan_count) for i in range(chan_count)]
        border = lax.ppermute(own_border, "chan", pairs)
        blocks.append(lax.optimization_barrier(with_border(raw_blocks[shift - 1], border)))
    kernel_cols = []
    for shift in range(chan_count):
        source = (chan_index + shift) % chan_count
        kernel_cols.append(
            lax.dynamic_slice_in_dim(weight, source * own_channels, own_channels, axis=3)
        )
    kernel_sends = []
    for shift in range(1, chan_count):
        target = (chan_index + shift) % chan_count
        kernel_sends.append(lax.dynamic_slice_in_dim(weight, target * own_channels, own_channels, axis=3))
    kernel_sends, _ = lax.optimization_barrier((kernel_sends, raw_blocks))
    kernel_blocks = []
    for shift in range(1, chan_count):
        pairs = [(i, (i + shift) % chan_count) for i in range(chan_count)]
        kernel_blocks.append(lax.ppermute(kernel_sends[shift - 1], "chan", pairs))
    preact = None
    for shift in range(chan_count):
        part = conv_taps(kernel_cols[shift], blocks[shift], row_count, column_count, False)
        preact = part if preact is None else preact + part
    preact = preact + bias_vector[:, None]
    upstream = cotangent.reshape(own_channels, -1).astype(jnp.float32)
    grad_pre = (upstream * gelu_slope(preact)).astype(jnp.bfloat16)
    bias_part = jnp.sum(grad_pre.astype(jnp.float32), axis=1)
    input_global = jnp.roll(jnp.stack(blocks), chan_index, axis=0).reshape(-1, *input_pad.shape[1:])
    taps = []
    for tap_row in range(3):
        row_taps = []
        for tap_col in range(3):
            window = window_of(input_global, tap_row, tap_col, row_count, column_count)
            row_taps.append(
                lax.dot_general(
                    grad_pre, window, (((1,), (1,)), ((), ())), preferred_element_type=jnp.float32
                )
            )
        taps.append(jnp.stack(row_taps))
    weight_part = jnp.stack(taps)
    flat = jnp.concatenate([weight_part.reshape(-1), bias_part])
    grad_field = grad_pre.reshape(own_channels, row_count, column_count)
    edges = (grad_field[:, :, column_count - 1 :], grad_field[:, :, :1])
    scattered, (before, after) = sum_start(flat, jnp.bfloat16, edges)
    grad_blocks = []
    for shift in range(1, chan_count):
        pairs = [(i, (i + shift) % chan_count) for i in range(chan_count)]
        grad_blocks.append(lax.ppermute(grad_field, "chan", pairs))
    scattered, grad_blocks, kernel_blocks = lax.optimization_barrier((scattered, grad_blocks, kernel_blocks))
    flat = sum_finish(scattered, flat.size, jnp.bfloat16)
    weight_grad = flat[: weight_part.size].reshape(weight_part.shape)
    bias_grad = flat[weight_part.size :]
    grad_wide = jnp.concatenate([before, grad_field, after], axis=2)
    grad_pad = mask_rims(padded_2(grad_wide, (("lat", 1),), 1))
    grad_border = border_of(grad_pad)
    input_sum = conv_taps(jnp.swapaxes(kernel_cols[0], 2, 3), grad_pad, row_count, column_count, True)
    for shift in range(1, chan_count):
        pairs = [(i, (i + shift) % chan_count) for i in range(chan_count)]
        border = lax.ppermute(grad_border, "chan", pairs)
        block = lax.optimization_barrier(with_border(grad_blocks[shift - 1], border))
        kernel_t = jnp.swapaxes(kernel_blocks[shift - 1], 2, 3)
        input_sum = input_sum + conv_taps(kernel_t, block, row_count, column_count, True)
    input_grad = input_sum.astype(jnp.bfloat16).reshape(own_channels, row_count, column_count)
    return (input_grad, weight_grad, bias_grad)


def solution(mesh):
    placed = (
        P("chan", ("groups", "lat"), "lon"),
        P("chan", ("groups", "lat"), "lon"),
        P(None, None, "chan", None),
        P("chan"),
    )
    return jax.shard_map(
        local,
        mesh=mesh,
        in_specs=placed,
        out_specs=(
            P("chan", ("groups", "lat"), "lon"),
            P("groups", None, "chan", None),
            P(("groups", "chan")),
        ),
        check_vma=False,
    )
```

```python
import jax
import jax.numpy as jnp
from jax import lax
from jax.sharding import PartitionSpec as P


def padded_2(shard, sides, width):
    for axis, dim in sides:
        devices, length = (lax.axis_size(axis), shard.shape[dim])
        up = [(i, (i + 1) % devices) for i in range(devices)]
        down = [(j, i) for i, j in up]
        last = lax.slice_in_dim(shard, length - width, length, axis=dim)
        initial = lax.slice_in_dim(shard, 0, width, axis=dim)
        before = lax.ppermute(last, axis, up)
        after = lax.ppermute(initial, axis, down)
        shard = jnp.concatenate([before, shard, after], axis=dim)
    return shard


def gelu_slope(preact):
    normal_cdf = 0.5 * (1.0 + jax.scipy.special.erf(preact * 0.7071067811865476))
    density = jnp.exp(-0.5 * preact * preact) * 0.3989422804014327
    return normal_cdf + preact * density


def mask_rims(padded):
    lat_index = lax.axis_index("lat")
    band_count = lax.axis_size("lat")
    row_ids = jnp.arange(padded.shape[1])
    outside = (row_ids == 0) & (lat_index == 0) | (row_ids == padded.shape[1] - 1) & (
        lat_index == band_count - 1
    )
    return jnp.where(outside[None, :, None], jnp.zeros((), padded.dtype), padded)


def window_of(field, first_row, first_col, row_count, column_count):
    return field[
        :, first_row : first_row + row_count, first_col : first_col + column_count
    ].reshape(field.shape[0], -1)


def conv_taps(kernel, field, row_count, column_count, flip):
    total = None
    for tap_row in range(3):
        for tap_col in range(3):
            if flip:
                window = window_of(field, 2 - tap_row, 2 - tap_col, row_count, column_count)
            else:
                window = window_of(field, tap_row, tap_col, row_count, column_count)
            part = jnp.dot(kernel[tap_row, tap_col], window, preferred_element_type=jnp.float32)
            total = part if total is None else total + part
    return total


def direct_reduce_scatter(rows, axis, send_dtype):
    count, index = lax.axis_size(axis), lax.axis_index(axis)
    if count == 1:
        return rows
    chunks = rows.reshape(count, -1, rows.shape[-1])
    acc = lax.dynamic_index_in_dim(chunks, index, keepdims=False)
    for step in range(1, count):
        pairs = [(j, (j + step) % count) for j in range(count)]
        piece = lax.dynamic_index_in_dim(chunks, (index + step) % count, keepdims=False)
        acc = acc + lax.ppermute(piece.astype(send_dtype), axis, pairs).astype(jnp.float32)
    return acc


def direct_all_gather(chunk, axis, send_dtype):
    count, index = lax.axis_size(axis), lax.axis_index(axis)
    if count == 1:
        return chunk
    pieces = [chunk]
    sent = chunk.astype(send_dtype)
    for step in range(1, count):
        pairs = [(j, (j + step) % count) for j in range(count)]
        pieces.append(lax.ppermute(sent, axis, pairs).astype(jnp.float32))
    stacked = jnp.stack(pieces[::-1])
    stacked = jnp.roll(stacked, (index + 1) % count, axis=0)
    return stacked.reshape(-1, chunk.shape[-1])


def piggyback_step(chunks, index, count, step, axis, send_dtype, extra):
    pairs = [(j, (j + step) % count) for j in range(count)]
    piece = lax.dynamic_index_in_dim(chunks, (index + step) % count, keepdims=False).astype(send_dtype)
    size = piece.shape[0]
    if extra is not None:
        tail = extra.astype(send_dtype).reshape(-1)
        tail = jnp.pad(tail, (0, (-tail.size) % chunks.shape[-1])).reshape(-1, chunks.shape[-1])
        piece = jnp.concatenate([piece, tail], axis=0)
    moved = lax.ppermute(piece, axis, pairs)
    got = None if extra is None else moved[size:].reshape(-1)[: extra.size].reshape(extra.shape)
    return moved[:size].astype(jnp.float32), got


def sum_start(flat, send_dtype, field):
    lanes = 128
    parts = lax.axis_size("lat") * lax.axis_size("lon")
    quantum = parts * 16 * lanes
    rows = jnp.pad(flat, (0, (-flat.size) % quantum)).reshape(-1, lanes)
    channels, height, width = field.shape
    count, index = lax.axis_size("lat"), lax.axis_index("lat")
    if count == 2:
        chunks = rows.reshape(count, -1, lanes)
        moved, extra = piggyback_step(
            chunks, index, count, 1, "lat", jnp.float32,
            jnp.concatenate([field[:, height - 1, :], field[:, 0, :]], axis=1),
        )
        rows = lax.dynamic_index_in_dim(chunks, index, keepdims=False) + moved
        extra = extra.reshape(channels, 2, width).astype(field.dtype)
        field = jnp.concatenate([extra[:, :1], field, extra[:, 1:]], axis=1)
    else:
        rows = direct_reduce_scatter(rows, "lat", jnp.float32)
        field = padded_2(field, (("lat", 1),), 1)
    last, first = field[:, :, width - 1], field[:, :, 0]
    count, index = lax.axis_size("lon"), lax.axis_index("lon")
    if count < 3:
        up = [(i, (i + 1) % count) for i in range(count)]
        down = [(j, i) for i, j in up]
        before, after = lax.ppermute(last, "lon", up), lax.ppermute(first, "lon", down)
        rows = direct_reduce_scatter(rows, "lon", send_dtype)
    else:
        chunks = rows.reshape(count, -1, lanes)
        rows = lax.dynamic_index_in_dim(chunks, index, keepdims=False)
        for step in range(1, count):
            extra = {1: last, count - 1: first}.get(step)
            moved, got = piggyback_step(chunks, index, count, step, "lon", send_dtype, extra)
            rows = rows + moved
            if step == 1:
                before = got.astype(field.dtype)
            if step == count - 1:
                after = got.astype(field.dtype)
    return rows, jnp.concatenate([before[:, :, None], field, after[:, :, None]], axis=2)


def sum_finish(rows, size, send_dtype):
    rows = direct_all_gather(rows, "lon", send_dtype)
    rows = direct_all_gather(rows, "lat", jnp.float32)
    return rows.reshape(-1)[:size]


def border_of(padded):
    rows, cols = padded.shape[1], padded.shape[2]
    return jnp.concatenate(
        [padded[:, 0, :], padded[:, rows - 1, :], padded[:, 1 : rows - 1, 0], padded[:, 1 : rows - 1, cols - 1]],
        axis=1,
    )


def with_border(field, border):
    rows, cols = field.shape[1], field.shape[2]
    top = border[:, : cols + 2]
    bottom = border[:, cols + 2 : 2 * cols + 4]
    left = border[:, 2 * cols + 4 : 2 * cols + 4 + rows]
    right = border[:, 2 * cols + 4 + rows :]
    middle = jnp.concatenate([left[:, :, None], field, right[:, :, None]], axis=2)
    return jnp.concatenate([top[:, None, :], middle, bottom[:, None, :]], axis=1)


def local(inputs, cotangent, weight, bias_vector):
    own_channels, row_count, column_count = inputs.shape
    chan_count = lax.axis_size("chan")
    chan_index = lax.axis_index("chan")
    raw_blocks = []
    for shift in range(1, chan_count):
        pairs = [(i, (i - shift) % chan_count) for i in range(chan_count)]
        raw_blocks.append(lax.ppermute(inputs, "chan", pairs))
    input_pad = mask_rims(padded_2(inputs, (("lon", 2), ("lat", 1)), 1))
    own_border = border_of(input_pad)
    blocks = [input_pad]
    for shift in range(1, chan_count):
        pairs = [(i, (i - shift) % chan_count) for i in range(chan_count)]
        border = lax.ppermute(own_border, "chan", pairs)
        blocks.append(lax.optimization_barrier(with_border(raw_blocks[shift - 1], border)))
    kernel_cols = []
    for shift in range(chan_count):
        source = (chan_index + shift) % chan_count
        kernel_cols.append(
            lax.dynamic_slice_in_dim(weight, source * own_channels, own_channels, axis=3)
        )
    preact = None
    for shift in range(chan_count):
        part = conv_taps(kernel_cols[shift], blocks[shift], row_count, column_count, False)
        preact = part if preact is None else preact + part
    preact = preact + bias_vector[:, None]
    upstream = cotangent.reshape(own_channels, -1).astype(jnp.float32)
    grad_pre = (upstream * gelu_slope(preact)).astype(jnp.bfloat16)
    bias_part = jnp.sum(grad_pre.astype(jnp.float32), axis=1)
    input_local = jnp.concatenate(blocks, axis=0)
    taps = []
    for tap_row in range(3):
        row_taps = []
        for tap_col in range(3):
            window = window_of(input_local, tap_row, tap_col, row_count, column_count)
            row_taps.append(
                lax.dot_general(
                    grad_pre, window, (((1,), (1,)), ((), ())), preferred_element_type=jnp.float32
                )
            )
        taps.append(jnp.stack(row_taps))
    weight_part = jnp.stack(taps)
    flat = jnp.concatenate([weight_part.reshape(-1), bias_part])
    grad_field = grad_pre.reshape(own_channels, row_count, column_count)
    scattered, grad_pad = sum_start(flat, jnp.bfloat16, grad_field)
    grad_pad = mask_rims(grad_pad)
    flat = sum_finish(scattered, flat.size, jnp.bfloat16)
    weight_local = flat[: weight_part.size].reshape(weight_part.shape)
    bias_grad = flat[weight_part.size :]
    doubled = jnp.concatenate([weight_local, weight_local], axis=3)
    weight_grad = lax.dynamic_slice_in_dim(
        doubled, (chan_count - chan_index) % chan_count * own_channels, chan_count * own_channels, axis=3
    )
    received = []
    for shift in range(1, chan_count):
        kernel_t = jnp.swapaxes(kernel_cols[shift], 2, 3)
        part = conv_taps(kernel_t, grad_pad, row_count, column_count, True)
        pairs = [(i, (i + shift) % chan_count) for i in range(chan_count)]
        received.append(lax.ppermute(part.astype(jnp.bfloat16), "chan", pairs))
    grad_pad, received = lax.optimization_barrier((grad_pad, received))
    own_part = conv_taps(jnp.swapaxes(kernel_cols[0], 2, 3), grad_pad, row_count, column_count, True)
    for piece in received:
        own_part = own_part + piece.astype(jnp.float32)
    input_grad = own_part.astype(jnp.bfloat16).reshape(own_channels, row_count, column_count)
    return (input_grad, weight_grad, bias_grad)


def solution(mesh):
    placed = (
        P("chan", ("groups", "lat"), "lon"),
        P("chan", ("groups", "lat"), "lon"),
        P(None, None, "chan", None),
        P("chan"),
    )
    return jax.shard_map(
        local,
        mesh=mesh,
        in_specs=placed,
        out_specs=(
            P("chan", ("groups", "lat"), "lon"),
            P("groups", None, "chan", None),
            P(("groups", "chan")),
        ),
        check_vma=False,
    )
```

```python
import jax
import jax.numpy as jnp
from jax import lax
from jax.sharding import PartitionSpec as P


def padded_2(shard, sides, width):
    for axis, dim in sides:
        devices, length = (lax.axis_size(axis), shard.shape[dim])
        up = [(i, (i + 1) % devices) for i in range(devices)]
        down = [(j, i) for i, j in up]
        last = lax.slice_in_dim(shard, length - width, length, axis=dim)
        initial = lax.slice_in_dim(shard, 0, width, axis=dim)
        before = lax.ppermute(last, axis, up)
        after = lax.ppermute(initial, axis, down)
        shard = jnp.concatenate([before, shard, after], axis=dim)
    return shard


def gelu_slope(preact):
    normal_cdf = 0.5 * (1.0 + jax.scipy.special.erf(preact * 0.7071067811865476))
    density = jnp.exp(-0.5 * preact * preact) * 0.3989422804014327
    return normal_cdf + preact * density


def mask_rims(padded):
    lat_index = lax.axis_index("lat")
    band_count = lax.axis_size("lat")
    row_ids = jnp.arange(padded.shape[1])
    outside = (row_ids == 0) & (lat_index == 0) | (row_ids == padded.shape[1] - 1) & (
        lat_index == band_count - 1
    )
    return jnp.where(outside[None, :, None], jnp.zeros((), padded.dtype), padded)


def window_of(field, first_row, first_col, row_count, column_count):
    return field[
        :, first_row : first_row + row_count, first_col : first_col + column_count
    ].reshape(field.shape[0], -1)


def conv_taps(kernel, field, row_count, column_count, flip):
    total = None
    for tap_row in range(3):
        for tap_col in range(3):
            if flip:
                window = window_of(field, 2 - tap_row, 2 - tap_col, row_count, column_count)
            else:
                window = window_of(field, tap_row, tap_col, row_count, column_count)
            part = jnp.dot(kernel[tap_row, tap_col], window, preferred_element_type=jnp.float32)
            total = part if total is None else total + part
    return total


def direct_reduce_scatter(rows, axis, send_dtype):
    count, index = lax.axis_size(axis), lax.axis_index(axis)
    if count == 1:
        return rows
    chunks = rows.reshape(count, -1, rows.shape[-1])
    acc = lax.dynamic_index_in_dim(chunks, index, keepdims=False)
    for step in range(1, count):
        pairs = [(j, (j + step) % count) for j in range(count)]
        piece = lax.dynamic_index_in_dim(chunks, (index + step) % count, keepdims=False)
        acc = acc + lax.ppermute(piece.astype(send_dtype), axis, pairs).astype(jnp.float32)
    return acc


def direct_all_gather(chunk, axis, send_dtype):
    count, index = lax.axis_size(axis), lax.axis_index(axis)
    if count == 1:
        return chunk
    pieces = [chunk]
    sent = chunk.astype(send_dtype)
    for step in range(1, count):
        pairs = [(j, (j + step) % count) for j in range(count)]
        pieces.append(lax.ppermute(sent, axis, pairs).astype(jnp.float32))
    stacked = jnp.stack(pieces[::-1])
    stacked = jnp.roll(stacked, (index + 1) % count, axis=0)
    return stacked.reshape(-1, chunk.shape[-1])


def piggyback_step(chunks, index, count, step, axis, send_dtype, extra):
    pairs = [(j, (j + step) % count) for j in range(count)]
    piece = lax.dynamic_index_in_dim(chunks, (index + step) % count, keepdims=False).astype(send_dtype)
    size = piece.shape[0]
    if extra is not None:
        tail = extra.astype(send_dtype).reshape(-1)
        tail = jnp.pad(tail, (0, (-tail.size) % chunks.shape[-1])).reshape(-1, chunks.shape[-1])
        piece = jnp.concatenate([piece, tail], axis=0)
    moved = lax.ppermute(piece, axis, pairs)
    got = None if extra is None else moved[size:].reshape(-1)[: extra.size].reshape(extra.shape)
    return moved[:size].astype(jnp.float32), got


def sum_start(flat, send_dtype, field):
    lanes = 128
    parts = lax.axis_size("lat") * lax.axis_size("lon")
    quantum = parts * 16 * lanes
    rows = jnp.pad(flat, (0, (-flat.size) % quantum)).reshape(-1, lanes)
    channels, height, width = field.shape
    count, index = lax.axis_size("lat"), lax.axis_index("lat")
    if count == 2:
        chunks = rows.reshape(count, -1, lanes)
        moved, extra = piggyback_step(
            chunks, index, count, 1, "lat", jnp.float32,
            jnp.concatenate([field[:, height - 1, :], field[:, 0, :]], axis=1),
        )
        rows = lax.dynamic_index_in_dim(chunks, index, keepdims=False) + moved
        extra = extra.reshape(channels, 2, width).astype(field.dtype)
        field = jnp.concatenate([extra[:, :1], field, extra[:, 1:]], axis=1)
    else:
        rows = direct_reduce_scatter(rows, "lat", jnp.float32)
        field = padded_2(field, (("lat", 1),), 1)
    last, first = field[:, :, width - 1], field[:, :, 0]
    count, index = lax.axis_size("lon"), lax.axis_index("lon")
    if count < 3:
        up = [(i, (i + 1) % count) for i in range(count)]
        down = [(j, i) for i, j in up]
        before, after = lax.ppermute(last, "lon", up), lax.ppermute(first, "lon", down)
        rows = direct_reduce_scatter(rows, "lon", send_dtype)
    else:
        chunks = rows.reshape(count, -1, lanes)
        rows = lax.dynamic_index_in_dim(chunks, index, keepdims=False)
        for step in range(1, count):
            extra = {1: last, count - 1: first}.get(step)
            moved, got = piggyback_step(chunks, index, count, step, "lon", send_dtype, extra)
            rows = rows + moved
            if step == 1:
                before = got.astype(field.dtype)
            if step == count - 1:
                after = got.astype(field.dtype)
    return rows, jnp.concatenate([before[:, :, None], field, after[:, :, None]], axis=2)


def sum_finish(rows, size, send_dtype):
    rows = direct_all_gather(rows, "lon", send_dtype)
    rows = direct_all_gather(rows, "lat", jnp.float32)
    return rows.reshape(-1)[:size]


def border_of(padded):
    rows, cols = padded.shape[1], padded.shape[2]
    return jnp.concatenate(
        [padded[:, 0, :], padded[:, rows - 1, :], padded[:, 1 : rows - 1, 0], padded[:, 1 : rows - 1, cols - 1]],
        axis=1,
    )


def with_border(field, border):
    rows, cols = field.shape[1], field.shape[2]
    top = border[:, : cols + 2]
    bottom = border[:, cols + 2 : 2 * cols + 4]
    left = border[:, 2 * cols + 4 : 2 * cols + 4 + rows]
    right = border[:, 2 * cols + 4 + rows :]
    middle = jnp.concatenate([left[:, :, None], field, right[:, :, None]], axis=2)
    return jnp.concatenate([top[:, None, :], middle, bottom[:, None, :]], axis=1)


def local(inputs, cotangent, weight, bias_vector):
    own_channels, row_count, column_count = inputs.shape
    chan_count = lax.axis_size("chan")
    chan_index = lax.axis_index("chan")
    raw_blocks = []
    for shift in range(1, chan_count):
        pairs = [(i, (i - shift) % chan_count) for i in range(chan_count)]
        raw_blocks.append(lax.ppermute(inputs, "chan", pairs))
    input_pad = mask_rims(padded_2(inputs, (("lon", 2), ("lat", 1)), 1))
    own_border = border_of(input_pad)
    blocks = [input_pad]
    for shift in range(1, chan_count):
        pairs = [(i, (i - shift) % chan_count) for i in range(chan_count)]
        border = lax.ppermute(own_border, "chan", pairs)
        blocks.append(lax.optimization_barrier(with_border(raw_blocks[shift - 1], border)))
    kernel_cols = []
    for shift in range(chan_count):
        source = (chan_index + shift) % chan_count
        kernel_cols.append(
            lax.dynamic_slice_in_dim(weight, source * own_channels, own_channels, axis=3)
        )
    preact = None
    for shift in range(chan_count):
        part = conv_taps(kernel_cols[shift], blocks[shift], row_count, column_count, False)
        preact = part if preact is None else preact + part
    preact = preact + bias_vector[:, None]
    upstream = cotangent.reshape(own_channels, -1).astype(jnp.float32)
    grad_pre = (upstream * gelu_slope(preact)).astype(jnp.bfloat16)
    bias_part = jnp.sum(grad_pre.astype(jnp.float32), axis=1)
    input_local = jnp.concatenate(blocks, axis=0)
    taps = []
    for tap_row in range(3):
        row_taps = []
        for tap_col in range(3):
            window = window_of(input_local, tap_row, tap_col, row_count, column_count)
            row_taps.append(
                lax.dot_general(
                    grad_pre, window, (((1,), (1,)), ((), ())), preferred_element_type=jnp.float32
                )
            )
        taps.append(jnp.stack(row_taps))
    weight_part = jnp.stack(taps)
    flat = jnp.concatenate([weight_part.reshape(-1), bias_part])
    grad_field = grad_pre.reshape(own_channels, row_count, column_count)
    scattered, grad_pad = sum_start(flat, jnp.bfloat16, grad_field)
    grad_pad = mask_rims(grad_pad)
    flat = sum_finish(scattered, flat.size, jnp.bfloat16)
    weight_local = flat[: weight_part.size].reshape(weight_part.shape)
    bias_grad = flat[weight_part.size :]
    doubled = jnp.concatenate([weight_local, weight_local], axis=3)
    weight_grad = lax.dynamic_slice_in_dim(
        doubled, (chan_count - chan_index) % chan_count * own_channels, chan_count * own_channels, axis=3
    )
    outgoing = []
    for shift in range(1, chan_count):
        kernel_t = jnp.swapaxes(kernel_cols[shift], 2, 3)
        outgoing.append(conv_taps(kernel_t, grad_pad, row_count, column_count, True).astype(jnp.bfloat16))
    grad_pad, outgoing = lax.optimization_barrier((grad_pad, outgoing))
    received = []
    for shift in range(1, chan_count):
        pairs = [(i, (i + shift) % chan_count) for i in range(chan_count)]
        received.append(lax.ppermute(outgoing[shift - 1], "chan", pairs))
    own_part = conv_taps(jnp.swapaxes(kernel_cols[0], 2, 3), grad_pad, row_count, column_count, True)
    for piece in received:
        own_part = own_part + piece.astype(jnp.float32)
    input_grad = own_part.astype(jnp.bfloat16).reshape(own_channels, row_count, column_count)
    return (input_grad, weight_grad, bias_grad)


def solution(mesh):
    placed = (
        P("chan", ("groups", "lat"), "lon"),
        P("chan", ("groups", "lat"), "lon"),
        P(None, None, "chan", None),
        P("chan"),
    )
    return jax.shard_map(
        local,
        mesh=mesh,
        in_specs=placed,
        out_specs=(
            P("chan", ("groups", "lat"), "lon"),
            P("groups", None, "chan", None),
            P(("groups", "chan")),
        ),
        check_vma=False,
    )
```

```python
import jax
import jax.numpy as jnp
from jax import lax
from jax.sharding import PartitionSpec as P


def padded_2(shard, sides, width):
    for axis, dim in sides:
        devices, length = (lax.axis_size(axis), shard.shape[dim])
        up = [(i, (i + 1) % devices) for i in range(devices)]
        down = [(j, i) for i, j in up]
        last = lax.slice_in_dim(shard, length - width, length, axis=dim)
        initial = lax.slice_in_dim(shard, 0, width, axis=dim)
        before = lax.ppermute(last, axis, up)
        after = lax.ppermute(initial, axis, down)
        shard = jnp.concatenate([before, shard, after], axis=dim)
    return shard


def gelu_slope(preact):
    normal_cdf = 0.5 * (1.0 + jax.scipy.special.erf(preact * 0.7071067811865476))
    density = jnp.exp(-0.5 * preact * preact) * 0.3989422804014327
    return normal_cdf + preact * density


def mask_rims(padded):
    lat_index = lax.axis_index("lat")
    band_count = lax.axis_size("lat")
    row_ids = jnp.arange(padded.shape[1])
    outside = (row_ids == 0) & (lat_index == 0) | (row_ids == padded.shape[1] - 1) & (
        lat_index == band_count - 1
    )
    return jnp.where(outside[None, :, None], jnp.zeros((), padded.dtype), padded)


def window_of(field, first_row, first_col, row_count, column_count):
    return field[
        :, first_row : first_row + row_count, first_col : first_col + column_count
    ].reshape(field.shape[0], -1)


def conv_taps(kernel, field, row_count, column_count, flip):
    total = None
    for tap_row in range(3):
        for tap_col in range(3):
            if flip:
                window = window_of(field, 2 - tap_row, 2 - tap_col, row_count, column_count)
            else:
                window = window_of(field, tap_row, tap_col, row_count, column_count)
            part = jnp.dot(kernel[tap_row, tap_col], window, preferred_element_type=jnp.float32)
            total = part if total is None else total + part
    return total


def direct_reduce_scatter(rows, axis, send_dtype):
    count, index = lax.axis_size(axis), lax.axis_index(axis)
    if count == 1:
        return rows
    chunks = rows.reshape(count, -1, rows.shape[-1])
    acc = lax.dynamic_index_in_dim(chunks, index, keepdims=False)
    for step in range(1, count):
        pairs = [(j, (j + step) % count) for j in range(count)]
        piece = lax.dynamic_index_in_dim(chunks, (index + step) % count, keepdims=False)
        acc = acc + lax.ppermute(piece.astype(send_dtype), axis, pairs).astype(jnp.float32)
    return acc


def direct_all_gather(chunk, axis, send_dtype):
    count, index = lax.axis_size(axis), lax.axis_index(axis)
    if count == 1:
        return chunk
    pieces = [chunk]
    sent = chunk.astype(send_dtype)
    for step in range(1, count):
        pairs = [(j, (j + step) % count) for j in range(count)]
        pieces.append(lax.ppermute(sent, axis, pairs).astype(jnp.float32))
    stacked = jnp.stack(pieces[::-1])
    stacked = jnp.roll(stacked, (index + 1) % count, axis=0)
    return stacked.reshape(-1, chunk.shape[-1])


def sum_start(flat, send_dtype, columns):
    parts = lax.axis_size("lat") * lax.axis_size("lon")
    quantum = parts * 16 * 128
    padded = jnp.pad(flat, (0, (-flat.size) % quantum)).reshape(-1, 128)
    rows = direct_reduce_scatter(padded, "lat", jnp.float32)
    count, index = lax.axis_size("lon"), lax.axis_index("lon")
    last, first = columns
    if count < 3:
        up = [(i, (i + 1) % count) for i in range(count)]
        down = [(j, i) for i, j in up]
        halo = (lax.ppermute(last, "lon", up), lax.ppermute(first, "lon", down))
        return direct_reduce_scatter(rows, "lon", send_dtype), halo
    chunks = rows.reshape(count, -1, rows.shape[-1])
    size = chunks.shape[1]
    acc = lax.dynamic_index_in_dim(chunks, index, keepdims=False)
    extra = {1: last, count - 1: first}
    got = {}
    for step in range(1, count):
        pairs = [(j, (j + step) % count) for j in range(count)]
        piece = lax.dynamic_index_in_dim(chunks, (index + step) % count, keepdims=False).astype(send_dtype)
        if step in extra:
            piece = jnp.concatenate([piece, extra[step].astype(send_dtype).reshape(-1, rows.shape[-1])], axis=0)
        moved = lax.ppermute(piece, "lon", pairs)
        acc = acc + moved[:size].astype(jnp.float32)
        if step in extra:
            got[step] = moved[size:].reshape(last.shape).astype(last.dtype)
    return acc, (got[1], got[count - 1])


def sum_finish(rows, size, send_dtype):
    rows = direct_all_gather(rows, "lon", send_dtype)
    rows = direct_all_gather(rows, "lat", jnp.float32)
    return rows.reshape(-1)[:size]


def border_of(padded):
    rows, cols = padded.shape[1], padded.shape[2]
    return jnp.concatenate(
        [padded[:, 0, :], padded[:, rows - 1, :], padded[:, 1 : rows - 1, 0], padded[:, 1 : rows - 1, cols - 1]],
        axis=1,
    )


def with_border(field, border):
    rows, cols = field.shape[1], field.shape[2]
    top = border[:, : cols + 2]
    bottom = border[:, cols + 2 : 2 * cols + 4]
    left = border[:, 2 * cols + 4 : 2 * cols + 4 + rows]
    right = border[:, 2 * cols + 4 + rows :]
    middle = jnp.concatenate([left[:, :, None], field, right[:, :, None]], axis=2)
    return jnp.concatenate([top[:, None, :], middle, bottom[:, None, :]], axis=1)


def local(inputs, cotangent, weight, bias_vector):
    own_channels, row_count, column_count = inputs.shape
    chan_count = lax.axis_size("chan")
    chan_index = lax.axis_index("chan")
    raw_blocks = []
    for shift in range(1, chan_count):
        pairs = [(i, (i - shift) % chan_count) for i in range(chan_count)]
        raw_blocks.append(lax.ppermute(inputs, "chan", pairs))
    input_pad = mask_rims(padded_2(inputs, (("lon", 2), ("lat", 1)), 1))
    own_border = border_of(input_pad)
    blocks = [input_pad]
    for shift in range(1, chan_count):
        pairs = [(i, (i - shift) % chan_count) for i in range(chan_count)]
        border = lax.ppermute(own_border, "chan", pairs)
        blocks.append(lax.optimization_barrier(with_border(raw_blocks[shift - 1], border)))
    kernel_cols = []
    for shift in range(chan_count):
        source = (chan_index + shift) % chan_count
        kernel_cols.append(
            lax.dynamic_slice_in_dim(weight, source * own_channels, own_channels, axis=3)
        )
    preact = None
    for shift in range(chan_count):
        part = conv_taps(kernel_cols[shift], blocks[shift], row_count, column_count, False)
        preact = part if preact is None else preact + part
    preact = preact + bias_vector[:, None]
    upstream = cotangent.reshape(own_channels, -1).astype(jnp.float32)
    grad_pre = (upstream * gelu_slope(preact)).astype(jnp.bfloat16)
    bias_part = jnp.sum(grad_pre.astype(jnp.float32), axis=1)
    input_local = jnp.concatenate(blocks, axis=0)
    taps = []
    for tap_row in range(3):
        row_taps = []
        for tap_col in range(3):
            window = window_of(input_local, tap_row, tap_col, row_count, column_count)
            row_taps.append(
                lax.dot_general(
                    grad_pre, window, (((1,), (1,)), ((), ())), preferred_element_type=jnp.float32
                )
            )
        taps.append(jnp.stack(row_taps))
    weight_part = jnp.stack(taps)
    flat = jnp.concatenate([weight_part.reshape(-1), bias_part])
    grad_field = grad_pre.reshape(own_channels, row_count, column_count)
    edges = (grad_field[:, :, column_count - 1 :], grad_field[:, :, :1])
    scattered, (before, after) = sum_start(flat, jnp.bfloat16, edges)
    flat = sum_finish(scattered, flat.size, jnp.bfloat16)
    weight_local = flat[: weight_part.size].reshape(weight_part.shape)
    bias_grad = flat[weight_part.size :]
    doubled = jnp.concatenate([weight_local, weight_local], axis=3)
    weight_grad = lax.dynamic_slice_in_dim(
        doubled, (chan_count - chan_index) % chan_count * own_channels, chan_count * own_channels, axis=3
    )
    grad_wide = jnp.concatenate([before, grad_field, after], axis=2)
    grad_pad = mask_rims(padded_2(grad_wide, (("lat", 1),), 1))
    outgoing = []
    for shift in range(1, chan_count):
        kernel_t = jnp.swapaxes(kernel_cols[shift], 2, 3)
        outgoing.append(conv_taps(kernel_t, grad_pad, row_count, column_count, True).astype(jnp.bfloat16))
    grad_pad, outgoing = lax.optimization_barrier((grad_pad, outgoing))
    received = []
    for shift in range(1, chan_count):
        pairs = [(i, (i + shift) % chan_count) for i in range(chan_count)]
        received.append(lax.ppermute(outgoing[shift - 1], "chan", pairs))
    own_part = conv_taps(jnp.swapaxes(kernel_cols[0], 2, 3), grad_pad, row_count, column_count, True)
    for piece in received:
        own_part = own_part + piece.astype(jnp.float32)
    input_grad = own_part.astype(jnp.bfloat16).reshape(own_channels, row_count, column_count)
    return (input_grad, weight_grad, bias_grad)


def solution(mesh):
    placed = (
        P("chan", ("groups", "lat"), "lon"),
        P("chan", ("groups", "lat"), "lon"),
        P(None, None, "chan", None),
        P("chan"),
    )
    return jax.shard_map(
        local,
        mesh=mesh,
        in_specs=placed,
        out_specs=(
            P("chan", ("groups", "lat"), "lon"),
            P("groups", None, "chan", None),
            P(("groups", "chan")),
        ),
        check_vma=False,
    )
```

```python
import jax
import jax.numpy as jnp
from jax import lax
from jax.sharding import PartitionSpec as P


def padded_2(shard, sides, width):
    for axis, dim in sides:
        devices, length = (lax.axis_size(axis), shard.shape[dim])
        up = [(i, (i + 1) % devices) for i in range(devices)]
        down = [(j, i) for i, j in up]
        last = lax.slice_in_dim(shard, length - width, length, axis=dim)
        initial = lax.slice_in_dim(shard, 0, width, axis=dim)
        before = lax.ppermute(last, axis, up)
        after = lax.ppermute(initial, axis, down)
        shard = jnp.concatenate([before, shard, after], axis=dim)
    return shard


def gelu_slope(preact):
    normal_cdf = 0.5 * (1.0 + jax.scipy.special.erf(preact * 0.7071067811865476))
    density = jnp.exp(-0.5 * preact * preact) * 0.3989422804014327
    return normal_cdf + preact * density


def mask_rims(padded):
    lat_index = lax.axis_index("lat")
    band_count = lax.axis_size("lat")
    row_ids = jnp.arange(padded.shape[1])
    outside = (row_ids == 0) & (lat_index == 0) | (row_ids == padded.shape[1] - 1) & (
        lat_index == band_count - 1
    )
    return jnp.where(outside[None, :, None], jnp.zeros((), padded.dtype), padded)


def window_of(field, first_row, first_col, row_count, column_count):
    return field[
        :, first_row : first_row + row_count, first_col : first_col + column_count
    ].reshape(field.shape[0], -1)


def conv_taps(kernel, field, row_count, column_count, flip):
    total = None
    for tap_row in range(3):
        for tap_col in range(3):
            if flip:
                window = window_of(field, 2 - tap_row, 2 - tap_col, row_count, column_count)
            else:
                window = window_of(field, tap_row, tap_col, row_count, column_count)
            part = jnp.dot(kernel[tap_row, tap_col], window, preferred_element_type=jnp.float32)
            total = part if total is None else total + part
    return total


def direct_reduce_scatter(rows, axis, send_dtype):
    count, index = lax.axis_size(axis), lax.axis_index(axis)
    if count == 1:
        return rows
    chunks = rows.reshape(count, -1, rows.shape[-1])
    acc = lax.dynamic_index_in_dim(chunks, index, keepdims=False)
    for step in range(1, count):
        pairs = [(j, (j + step) % count) for j in range(count)]
        piece = lax.dynamic_index_in_dim(chunks, (index + step) % count, keepdims=False)
        acc = acc + lax.ppermute(piece.astype(send_dtype), axis, pairs).astype(jnp.float32)
    return acc


def direct_all_gather(chunk, axis, send_dtype):
    count, index = lax.axis_size(axis), lax.axis_index(axis)
    if count == 1:
        return chunk
    pieces = [chunk]
    sent = chunk.astype(send_dtype)
    for step in range(1, count):
        pairs = [(j, (j + step) % count) for j in range(count)]
        pieces.append(lax.ppermute(sent, axis, pairs).astype(jnp.float32))
    stacked = jnp.stack(pieces[::-1])
    stacked = jnp.roll(stacked, (index + 1) % count, axis=0)
    return stacked.reshape(-1, chunk.shape[-1])


def sum_start(flat, send_dtype, columns):
    parts = lax.axis_size("lat") * lax.axis_size("lon")
    quantum = parts * 16 * 128
    padded = jnp.pad(flat, (0, (-flat.size) % quantum)).reshape(-1, 128)
    rows = direct_reduce_scatter(padded, "lat", jnp.float32)
    count, index = lax.axis_size("lon"), lax.axis_index("lon")
    last, first = columns
    if count < 3:
        up = [(i, (i + 1) % count) for i in range(count)]
        down = [(j, i) for i, j in up]
        halo = (lax.ppermute(last, "lon", up), lax.ppermute(first, "lon", down))
        return direct_reduce_scatter(rows, "lon", send_dtype), halo
    chunks = rows.reshape(count, -1, rows.shape[-1])
    size = chunks.shape[1]
    acc = lax.dynamic_index_in_dim(chunks, index, keepdims=False)
    extra = {1: last, count - 1: first}
    got = {}
    for step in range(1, count):
        pairs = [(j, (j + step) % count) for j in range(count)]
        piece = lax.dynamic_index_in_dim(chunks, (index + step) % count, keepdims=False).astype(send_dtype)
        if step in extra:
            piece = jnp.concatenate([piece, extra[step].astype(send_dtype).reshape(-1, rows.shape[-1])], axis=0)
        moved = lax.ppermute(piece, "lon", pairs)
        acc = acc + moved[:size].astype(jnp.float32)
        if step in extra:
            got[step] = moved[size:].reshape(last.shape).astype(last.dtype)
    return acc, (got[1], got[count - 1])


def sum_finish(rows, size, send_dtype):
    rows = direct_all_gather(rows, "lon", send_dtype)
    rows = direct_all_gather(rows, "lat", jnp.float32)
    return rows.reshape(-1)[:size]


def border_of(padded):
    rows, cols = padded.shape[1], padded.shape[2]
    return jnp.concatenate(
        [padded[:, 0, :], padded[:, rows - 1, :], padded[:, 1 : rows - 1, 0], padded[:, 1 : rows - 1, cols - 1]],
        axis=1,
    )


def with_border(field, border):
    rows, cols = field.shape[1], field.shape[2]
    top = border[:, : cols + 2]
    bottom = border[:, cols + 2 : 2 * cols + 4]
    left = border[:, 2 * cols + 4 : 2 * cols + 4 + rows]
    right = border[:, 2 * cols + 4 + rows :]
    middle = jnp.concatenate([left[:, :, None], field, right[:, :, None]], axis=2)
    return jnp.concatenate([top[:, None, :], middle, bottom[:, None, :]], axis=1)


def local(inputs, cotangent, weight, bias_vector):
    own_channels, row_count, column_count = inputs.shape
    chan_count = lax.axis_size("chan")
    chan_index = lax.axis_index("chan")
    raw_blocks = []
    for shift in range(1, chan_count):
        pairs = [(i, (i - shift) % chan_count) for i in range(chan_count)]
        raw_blocks.append(lax.ppermute(inputs, "chan", pairs))
    input_pad = mask_rims(padded_2(inputs, (("lon", 2), ("lat", 1)), 1))
    own_border = border_of(input_pad)
    blocks = [input_pad]
    for shift in range(1, chan_count):
        pairs = [(i, (i - shift) % chan_count) for i in range(chan_count)]
        border = lax.ppermute(own_border, "chan", pairs)
        blocks.append(lax.optimization_barrier(with_border(raw_blocks[shift - 1], border)))
    kernel_cols = []
    for shift in range(chan_count):
        source = (chan_index + shift) % chan_count
        kernel_cols.append(
            lax.dynamic_slice_in_dim(weight, source * own_channels, own_channels, axis=3)
        )
    preact = None
    for shift in range(chan_count):
        part = conv_taps(kernel_cols[shift], blocks[shift], row_count, column_count, False)
        preact = part if preact is None else preact + part
    preact = preact + bias_vector[:, None]
    upstream = cotangent.reshape(own_channels, -1).astype(jnp.float32)
    grad_pre = (upstream * gelu_slope(preact)).astype(jnp.bfloat16)
    bias_part = jnp.sum(grad_pre.astype(jnp.float32), axis=1)
    input_local = jnp.concatenate(blocks, axis=0)
    taps = []
    for tap_row in range(3):
        row_taps = []
        for tap_col in range(3):
            window = window_of(input_local, tap_row, tap_col, row_count, column_count)
            row_taps.append(
                lax.dot_general(
                    grad_pre, window, (((1,), (1,)), ((), ())), preferred_element_type=jnp.float32
                )
            )
        taps.append(jnp.stack(row_taps))
    weight_part = jnp.stack(taps)
    flat = jnp.concatenate([weight_part.reshape(-1), bias_part])
    grad_field = grad_pre.reshape(own_channels, row_count, column_count)
    edges = (grad_field[:, :, column_count - 1 :], grad_field[:, :, :1])
    scattered, (before, after) = sum_start(flat, jnp.bfloat16, edges)
    flat = sum_finish(scattered, flat.size, jnp.bfloat16)
    weight_local = flat[: weight_part.size].reshape(weight_part.shape)
    bias_grad = flat[weight_part.size :]
    doubled = jnp.concatenate([weight_local, weight_local], axis=3)
    weight_grad = lax.dynamic_slice_in_dim(
        doubled, (chan_count - chan_index) % chan_count * own_channels, chan_count * own_channels, axis=3
    )
    grad_wide = jnp.concatenate([before, grad_field, after], axis=2)
    grad_pad = mask_rims(padded_2(grad_wide, (("lat", 1),), 1))
    interiors = []
    outgoing = []
    for shift in range(1, chan_count):
        pairs = [(i, (i + shift) % chan_count) for i in range(chan_count)]
        kernel_t = jnp.swapaxes(kernel_cols[shift], 2, 3)
        inner = conv_taps(kernel_t, grad_field, row_count - 2, column_count - 2, True)
        interiors.append(lax.ppermute(inner.astype(jnp.bfloat16), "chan", pairs))
        whole = conv_taps(kernel_t, grad_pad, row_count, column_count, True)
        outgoing.append(border_of(whole.reshape(own_channels, row_count, column_count)).astype(jnp.bfloat16))
    grad_pad, outgoing = lax.optimization_barrier((grad_pad, outgoing))
    received = []
    for shift in range(1, chan_count):
        pairs = [(i, (i + shift) % chan_count) for i in range(chan_count)]
        ring = lax.ppermute(outgoing[shift - 1], "chan", pairs)
        inner = interiors[shift - 1].reshape(own_channels, row_count - 2, column_count - 2)
        received.append(with_border(inner, ring).reshape(own_channels, -1))
    own_part = conv_taps(jnp.swapaxes(kernel_cols[0], 2, 3), grad_pad, row_count, column_count, True)
    for piece in received:
        own_part = own_part + piece.astype(jnp.float32)
    input_grad = own_part.astype(jnp.bfloat16).reshape(own_channels, row_count, column_count)
    return (input_grad, weight_grad, bias_grad)


def solution(mesh):
    placed = (
        P("chan", ("groups", "lat"), "lon"),
        P("chan", ("groups", "lat"), "lon"),
        P(None, None, "chan", None),
        P("chan"),
    )
    return jax.shard_map(
        local,
        mesh=mesh,
        in_specs=placed,
        out_specs=(
            P("chan", ("groups", "lat"), "lon"),
            P("groups", None, "chan", None),
            P(("groups", "chan")),
        ),
        check_vma=False,
    )
```

```python
import jax
import jax.numpy as jnp
from jax import lax
from jax.sharding import PartitionSpec as P


def padded_2(shard, sides, width):
    for axis, dim in sides:
        devices, length = (lax.axis_size(axis), shard.shape[dim])
        up = [(i, (i + 1) % devices) for i in range(devices)]
        down = [(j, i) for i, j in up]
        last = lax.slice_in_dim(shard, length - width, length, axis=dim)
        initial = lax.slice_in_dim(shard, 0, width, axis=dim)
        before = lax.ppermute(last, axis, up)
        after = lax.ppermute(initial, axis, down)
        shard = jnp.concatenate([before, shard, after], axis=dim)
    return shard


def gelu_slope(preact):
    normal_cdf = 0.5 * (1.0 + jax.scipy.special.erf(preact * 0.7071067811865476))
    density = jnp.exp(-0.5 * preact * preact) * 0.3989422804014327
    return normal_cdf + preact * density


def mask_rims(padded):
    lat_index = lax.axis_index("lat")
    band_count = lax.axis_size("lat")
    row_ids = jnp.arange(padded.shape[1])
    outside = (row_ids == 0) & (lat_index == 0) | (row_ids == padded.shape[1] - 1) & (
        lat_index == band_count - 1
    )
    return jnp.where(outside[None, :, None], jnp.zeros((), padded.dtype), padded)


def window_of(field, first_row, first_col, row_count, column_count):
    return field[
        :, first_row : first_row + row_count, first_col : first_col + column_count
    ].reshape(field.shape[0], -1)


def conv_taps(kernel, field, row_count, column_count, flip):
    total = None
    for tap_row in range(3):
        for tap_col in range(3):
            if flip:
                window = window_of(field, 2 - tap_row, 2 - tap_col, row_count, column_count)
            else:
                window = window_of(field, tap_row, tap_col, row_count, column_count)
            part = jnp.dot(kernel[tap_row, tap_col], window, preferred_element_type=jnp.float32)
            total = part if total is None else total + part
    return total


def direct_reduce_scatter(rows, axis, send_dtype):
    count, index = lax.axis_size(axis), lax.axis_index(axis)
    if count == 1:
        return rows
    chunks = rows.reshape(count, -1, rows.shape[-1])
    acc = lax.dynamic_index_in_dim(chunks, index, keepdims=False)
    for step in range(1, count):
        pairs = [(j, (j + step) % count) for j in range(count)]
        piece = lax.dynamic_index_in_dim(chunks, (index + step) % count, keepdims=False)
        acc = acc + lax.ppermute(piece.astype(send_dtype), axis, pairs).astype(jnp.float32)
    return acc


def direct_all_gather(chunk, axis, send_dtype):
    count, index = lax.axis_size(axis), lax.axis_index(axis)
    if count == 1:
        return chunk
    pieces = [chunk]
    sent = chunk.astype(send_dtype)
    for step in range(1, count):
        pairs = [(j, (j + step) % count) for j in range(count)]
        pieces.append(lax.ppermute(sent, axis, pairs).astype(jnp.float32))
    stacked = jnp.stack(pieces[::-1])
    stacked = jnp.roll(stacked, (index + 1) % count, axis=0)
    return stacked.reshape(-1, chunk.shape[-1])


def sum_start(flat, send_dtype, columns):
    parts = lax.axis_size("lat") * lax.axis_size("lon")
    quantum = parts * 16 * 128
    padded = jnp.pad(flat, (0, (-flat.size) % quantum)).reshape(-1, 128)
    rows = direct_reduce_scatter(padded, "lat", jnp.float32)
    count, index = lax.axis_size("lon"), lax.axis_index("lon")
    last, first = columns
    if count < 3:
        up = [(i, (i + 1) % count) for i in range(count)]
        down = [(j, i) for i, j in up]
        halo = (lax.ppermute(last, "lon", up), lax.ppermute(first, "lon", down))
        return direct_reduce_scatter(rows, "lon", send_dtype), halo
    chunks = rows.reshape(count, -1, rows.shape[-1])
    size = chunks.shape[1]
    acc = lax.dynamic_index_in_dim(chunks, index, keepdims=False)
    extra = {1: last, count - 1: first}
    got = {}
    for step in range(1, count):
        pairs = [(j, (j + step) % count) for j in range(count)]
        piece = lax.dynamic_index_in_dim(chunks, (index + step) % count, keepdims=False).astype(send_dtype)
        if step in extra:
            piece = jnp.concatenate([piece, extra[step].astype(send_dtype).reshape(-1, rows.shape[-1])], axis=0)
        moved = lax.ppermute(piece, "lon", pairs)
        acc = acc + moved[:size].astype(jnp.float32)
        if step in extra:
            got[step] = moved[size:].reshape(last.shape).astype(last.dtype)
    return acc, (got[1], got[count - 1])


def sum_finish(rows, size, send_dtype):
    rows = direct_all_gather(rows, "lon", send_dtype)
    rows = direct_all_gather(rows, "lat", jnp.float32)
    return rows.reshape(-1)[:size]


def border_of(padded):
    rows, cols = padded.shape[1], padded.shape[2]
    return jnp.concatenate(
        [padded[:, 0, :], padded[:, rows - 1, :], padded[:, 1 : rows - 1, 0], padded[:, 1 : rows - 1, cols - 1]],
        axis=1,
    )


def with_border(field, border):
    rows, cols = field.shape[1], field.shape[2]
    top = border[:, : cols + 2]
    bottom = border[:, cols + 2 : 2 * cols + 4]
    left = border[:, 2 * cols + 4 : 2 * cols + 4 + rows]
    right = border[:, 2 * cols + 4 + rows :]
    middle = jnp.concatenate([left[:, :, None], field, right[:, :, None]], axis=2)
    return jnp.concatenate([top[:, None, :], middle, bottom[:, None, :]], axis=1)


def local(inputs, cotangent, weight, bias_vector):
    own_channels, row_count, column_count = inputs.shape
    chan_count = lax.axis_size("chan")
    chan_index = lax.axis_index("chan")
    raw_blocks = []
    for shift in range(1, chan_count):
        pairs = [(i, (i - shift) % chan_count) for i in range(chan_count)]
        raw_blocks.append(lax.ppermute(inputs, "chan", pairs))
    input_pad = mask_rims(padded_2(inputs, (("lon", 2), ("lat", 1)), 1))
    own_border = border_of(input_pad)
    blocks = [input_pad]
    for shift in range(1, chan_count):
        pairs = [(i, (i - shift) % chan_count) for i in range(chan_count)]
        border = lax.ppermute(own_border, "chan", pairs)
        blocks.append(lax.optimization_barrier(with_border(raw_blocks[shift - 1], border)))
    kernel_cols = []
    for shift in range(chan_count):
        source = (chan_index + shift) % chan_count
        kernel_cols.append(
            lax.dynamic_slice_in_dim(weight, source * own_channels, own_channels, axis=3)
        )
    preact = None
    for shift in range(chan_count):
        part = conv_taps(kernel_cols[shift], blocks[shift], row_count, column_count, False)
        preact = part if preact is None else preact + part
    preact = preact + bias_vector[:, None]
    upstream = cotangent.reshape(own_channels, -1).astype(jnp.float32)
    grad_pre = (upstream * gelu_slope(preact)).astype(jnp.bfloat16)
    bias_part = jnp.sum(grad_pre.astype(jnp.float32), axis=1)
    input_local = jnp.concatenate(blocks, axis=0)
    taps = []
    for tap_row in range(3):
        row_taps = []
        for tap_col in range(3):
            window = window_of(input_local, tap_row, tap_col, row_count, column_count)
            row_taps.append(
                lax.dot_general(
                    grad_pre, window, (((1,), (1,)), ((), ())), preferred_element_type=jnp.float32
                )
            )
        taps.append(jnp.stack(row_taps))
    weight_part = jnp.stack(taps)
    flat = jnp.concatenate([weight_part.reshape(-1), bias_part])
    grad_field = grad_pre.reshape(own_channels, row_count, column_count)
    edges = (grad_field[:, :, column_count - 1 :], grad_field[:, :, :1])
    scattered, (before, after) = sum_start(flat, jnp.bfloat16, edges)
    flat = sum_finish(scattered, flat.size, jnp.bfloat16)
    weight_local = flat[: weight_part.size].reshape(weight_part.shape)
    bias_grad = flat[weight_part.size :]
    doubled = jnp.concatenate([weight_local, weight_local], axis=3)
    weight_grad = lax.dynamic_slice_in_dim(
        doubled, (chan_count - chan_index) % chan_count * own_channels, chan_count * own_channels, axis=3
    )
    grad_wide = jnp.concatenate([before, grad_field, after], axis=2)
    grad_pad = mask_rims(padded_2(grad_wide, (("lat", 1),), 1))
    interiors = []
    outgoing = []
    for shift in range(1, chan_count):
        pairs = [(i, (i + shift) % chan_count) for i in range(chan_count)]
        kernel_t = jnp.swapaxes(kernel_cols[shift], 2, 3)
        zero_pad = jnp.pad(grad_field, ((0, 0), (1, 1), (1, 1)))
        early = conv_taps(kernel_t, zero_pad, row_count, column_count, True)
        interiors.append(lax.ppermute(early.astype(jnp.bfloat16), "chan", pairs))
        whole = conv_taps(kernel_t, grad_pad, row_count, column_count, True)
        outgoing.append(border_of(whole.reshape(own_channels, row_count, column_count)).astype(jnp.bfloat16))
    grad_pad, outgoing = lax.optimization_barrier((grad_pad, outgoing))
    received = []
    for shift in range(1, chan_count):
        pairs = [(i, (i + shift) % chan_count) for i in range(chan_count)]
        ring = lax.ppermute(outgoing[shift - 1], "chan", pairs)
        inner = interiors[shift - 1].reshape(own_channels, row_count, column_count)[:, 1:-1, 1:-1]
        received.append(with_border(inner, ring).reshape(own_channels, -1))
    own_part = conv_taps(jnp.swapaxes(kernel_cols[0], 2, 3), grad_pad, row_count, column_count, True)
    for piece in received:
        own_part = own_part + piece.astype(jnp.float32)
    input_grad = own_part.astype(jnp.bfloat16).reshape(own_channels, row_count, column_count)
    return (input_grad, weight_grad, bias_grad)


def solution(mesh):
    placed = (
        P("chan", ("groups", "lat"), "lon"),
        P("chan", ("groups", "lat"), "lon"),
        P(None, None, "chan", None),
        P("chan"),
    )
    return jax.shard_map(
        local,
        mesh=mesh,
        in_specs=placed,
        out_specs=(
            P("chan", ("groups", "lat"), "lon"),
            P("groups", None, "chan", None),
            P(("groups", "chan")),
        ),
        check_vma=False,
    )
```

```python
import jax
import jax.numpy as jnp
from jax import lax
from jax.sharding import PartitionSpec as P


def padded_2(shard, sides, width):
    for axis, dim in sides:
        devices, length = (lax.axis_size(axis), shard.shape[dim])
        up = [(i, (i + 1) % devices) for i in range(devices)]
        down = [(j, i) for i, j in up]
        last = lax.slice_in_dim(shard, length - width, length, axis=dim)
        initial = lax.slice_in_dim(shard, 0, width, axis=dim)
        before = lax.ppermute(last, axis, up)
        after = lax.ppermute(initial, axis, down)
        shard = jnp.concatenate([before, shard, after], axis=dim)
    return shard


def gelu_slope(preact):
    normal_cdf = 0.5 * (1.0 + jax.scipy.special.erf(preact * 0.7071067811865476))
    density = jnp.exp(-0.5 * preact * preact) * 0.3989422804014327
    return normal_cdf + preact * density


def mask_rims(padded):
    lat_index = lax.axis_index("lat")
    band_count = lax.axis_size("lat")
    row_ids = jnp.arange(padded.shape[1])
    outside = (row_ids == 0) & (lat_index == 0) | (row_ids == padded.shape[1] - 1) & (
        lat_index == band_count - 1
    )
    return jnp.where(outside[None, :, None], jnp.zeros((), padded.dtype), padded)


def window_of(field, first_row, first_col, row_count, column_count):
    return field[
        :, first_row : first_row + row_count, first_col : first_col + column_count
    ].reshape(field.shape[0], -1)


def conv_taps(kernel, field, row_count, column_count, flip):
    total = None
    for tap_row in range(3):
        for tap_col in range(3):
            if flip:
                window = window_of(field, 2 - tap_row, 2 - tap_col, row_count, column_count)
            else:
                window = window_of(field, tap_row, tap_col, row_count, column_count)
            part = jnp.dot(kernel[tap_row, tap_col], window, preferred_element_type=jnp.float32)
            total = part if total is None else total + part
    return total


def direct_reduce_scatter(rows, axis, send_dtype):
    count, index = lax.axis_size(axis), lax.axis_index(axis)
    if count == 1:
        return rows
    chunks = rows.reshape(count, -1, rows.shape[-1])
    acc = lax.dynamic_index_in_dim(chunks, index, keepdims=False)
    for step in range(1, count):
        pairs = [(j, (j + step) % count) for j in range(count)]
        piece = lax.dynamic_index_in_dim(chunks, (index + step) % count, keepdims=False)
        acc = acc + lax.ppermute(piece.astype(send_dtype), axis, pairs).astype(jnp.float32)
    return acc


def direct_all_gather(chunk, axis, send_dtype):
    count, index = lax.axis_size(axis), lax.axis_index(axis)
    if count == 1:
        return chunk
    pieces = [chunk]
    sent = chunk.astype(send_dtype)
    for step in range(1, count):
        pairs = [(j, (j + step) % count) for j in range(count)]
        pieces.append(lax.ppermute(sent, axis, pairs).astype(jnp.float32))
    stacked = jnp.stack(pieces[::-1])
    stacked = jnp.roll(stacked, (index + 1) % count, axis=0)
    return stacked.reshape(-1, chunk.shape[-1])


def sum_start(flat, send_dtype, columns):
    parts = lax.axis_size("lat") * lax.axis_size("lon")
    quantum = parts * 16 * 128
    padded = jnp.pad(flat, (0, (-flat.size) % quantum)).reshape(-1, 128)
    rows = direct_reduce_scatter(padded, "lat", jnp.float32)
    count, index = lax.axis_size("lon"), lax.axis_index("lon")
    last, first = columns
    if count < 3:
        up = [(i, (i + 1) % count) for i in range(count)]
        down = [(j, i) for i, j in up]
        halo = (lax.ppermute(last, "lon", up), lax.ppermute(first, "lon", down))
        return direct_reduce_scatter(rows, "lon", send_dtype), halo
    chunks = rows.reshape(count, -1, rows.shape[-1])
    size = chunks.shape[1]
    acc = lax.dynamic_index_in_dim(chunks, index, keepdims=False)
    extra = {1: last, count - 1: first}
    got = {}
    for step in range(1, count):
        pairs = [(j, (j + step) % count) for j in range(count)]
        piece = lax.dynamic_index_in_dim(chunks, (index + step) % count, keepdims=False).astype(send_dtype)
        if step in extra:
            piece = jnp.concatenate([piece, extra[step].astype(send_dtype).reshape(-1, rows.shape[-1])], axis=0)
        moved = lax.ppermute(piece, "lon", pairs)
        acc = acc + moved[:size].astype(jnp.float32)
        if step in extra:
            got[step] = moved[size:].reshape(last.shape).astype(last.dtype)
    return acc, (got[1], got[count - 1])


def sum_finish(rows, size, send_dtype):
    rows = direct_all_gather(rows, "lon", send_dtype)
    rows = direct_all_gather(rows, "lat", jnp.float32)
    return rows.reshape(-1)[:size]


def border_of(padded):
    rows, cols = padded.shape[1], padded.shape[2]
    return jnp.concatenate(
        [padded[:, 0, :], padded[:, rows - 1, :], padded[:, 1 : rows - 1, 0], padded[:, 1 : rows - 1, cols - 1]],
        axis=1,
    )


def with_border(field, border):
    rows, cols = field.shape[1], field.shape[2]
    top = border[:, : cols + 2]
    bottom = border[:, cols + 2 : 2 * cols + 4]
    left = border[:, 2 * cols + 4 : 2 * cols + 4 + rows]
    right = border[:, 2 * cols + 4 + rows :]
    middle = jnp.concatenate([left[:, :, None], field, right[:, :, None]], axis=2)
    return jnp.concatenate([top[:, None, :], middle, bottom[:, None, :]], axis=1)


def local(inputs, cotangent, weight, bias_vector):
    own_channels, row_count, column_count = inputs.shape
    chan_count = lax.axis_size("chan")
    chan_index = lax.axis_index("chan")
    raw_blocks = []
    for shift in range(1, chan_count):
        pairs = [(i, (i - shift) % chan_count) for i in range(chan_count)]
        raw_blocks.append(lax.ppermute(inputs, "chan", pairs))
    input_pad = mask_rims(padded_2(inputs, (("lon", 2), ("lat", 1)), 1))
    own_border = border_of(input_pad)
    blocks = [input_pad]
    for shift in range(1, chan_count):
        pairs = [(i, (i - shift) % chan_count) for i in range(chan_count)]
        border = lax.ppermute(own_border, "chan", pairs)
        blocks.append(lax.optimization_barrier(with_border(raw_blocks[shift - 1], border)))
    kernel_cols = []
    for shift in range(chan_count):
        source = (chan_index + shift) % chan_count
        kernel_cols.append(
            lax.dynamic_slice_in_dim(weight, source * own_channels, own_channels, axis=3)
        )
    preact = None
    for shift in range(chan_count):
        part = conv_taps(kernel_cols[shift], blocks[shift], row_count, column_count, False)
        preact = part if preact is None else preact + part
    preact = preact + bias_vector[:, None]
    upstream = cotangent.reshape(own_channels, -1).astype(jnp.float32)
    grad_pre = (upstream * gelu_slope(preact)).astype(jnp.bfloat16)
    bias_part = jnp.sum(grad_pre.astype(jnp.float32), axis=1)
    input_local = jnp.concatenate(blocks, axis=0)
    taps = []
    for tap_row in range(3):
        row_taps = []
        for tap_col in range(3):
            window = window_of(input_local, tap_row, tap_col, row_count, column_count)
            row_taps.append(
                lax.dot_general(
                    grad_pre, window, (((1,), (1,)), ((), ())), preferred_element_type=jnp.float32
                )
            )
        taps.append(jnp.stack(row_taps))
    weight_part = jnp.stack(taps)
    flat = jnp.concatenate([weight_part.reshape(-1), bias_part])
    grad_field = grad_pre.reshape(own_channels, row_count, column_count)
    edges = (grad_field[:, :, column_count - 1 :], grad_field[:, :, :1])
    scattered, (before, after) = sum_start(flat, jnp.bfloat16, edges)
    flat = sum_finish(scattered, flat.size, jnp.bfloat16)
    weight_local = flat[: weight_part.size].reshape(weight_part.shape)
    bias_grad = flat[weight_part.size :]
    doubled = jnp.concatenate([weight_local, weight_local], axis=3)
    weight_grad = lax.dynamic_slice_in_dim(
        doubled, (chan_count - chan_index) % chan_count * own_channels, chan_count * own_channels, axis=3
    )
    grad_wide = jnp.concatenate([before, grad_field, after], axis=2)
    grad_pad = mask_rims(padded_2(grad_wide, (("lat", 1),), 1))
    outgoing = []
    for shift in range(1, chan_count):
        kernel_t = jnp.swapaxes(kernel_cols[shift], 2, 3)
        outgoing.append(conv_taps(kernel_t, grad_pad, row_count, column_count, True).astype(jnp.bfloat16))
    grad_pad, outgoing = lax.optimization_barrier((grad_pad, outgoing))
    received = []
    for shift in range(1, chan_count):
        pairs = [(i, (i + shift) % chan_count) for i in range(chan_count)]
        received.append(lax.ppermute(outgoing[shift - 1], "chan", pairs))
    own_part = conv_taps(jnp.swapaxes(kernel_cols[0], 2, 3), grad_pad, row_count, column_count, True)
    own_part, weight_grad, bias_grad = lax.optimization_barrier((own_part, weight_grad, bias_grad))
    for piece in received:
        own_part = own_part + piece.astype(jnp.float32)
    input_grad = own_part.astype(jnp.bfloat16).reshape(own_channels, row_count, column_count)
    return (input_grad, weight_grad, bias_grad)


def solution(mesh):
    placed = (
        P("chan", ("groups", "lat"), "lon"),
        P("chan", ("groups", "lat"), "lon"),
        P(None, None, "chan", None),
        P("chan"),
    )
    return jax.shard_map(
        local,
        mesh=mesh,
        in_specs=placed,
        out_specs=(
            P("chan", ("groups", "lat"), "lon"),
            P("groups", None, "chan", None),
            P(("groups", "chan")),
        ),
        check_vma=False,
    )
```

```python
import jax
import jax.numpy as jnp
from jax import lax
from jax.sharding import PartitionSpec as P


def padded_2(shard, sides, width):
    for axis, dim in sides:
        devices, length = (lax.axis_size(axis), shard.shape[dim])
        up = [(i, (i + 1) % devices) for i in range(devices)]
        down = [(j, i) for i, j in up]
        last = lax.slice_in_dim(shard, length - width, length, axis=dim)
        initial = lax.slice_in_dim(shard, 0, width, axis=dim)
        before = lax.ppermute(last, axis, up)
        after = lax.ppermute(initial, axis, down)
        shard = jnp.concatenate([before, shard, after], axis=dim)
    return shard


def gelu_slope(preact):
    normal_cdf = 0.5 * (1.0 + jax.scipy.special.erf(preact * 0.7071067811865476))
    density = jnp.exp(-0.5 * preact * preact) * 0.3989422804014327
    return normal_cdf + preact * density


def mask_rims(padded):
    lat_index = lax.axis_index("lat")
    band_count = lax.axis_size("lat")
    row_ids = jnp.arange(padded.shape[1])
    outside = (row_ids == 0) & (lat_index == 0) | (row_ids == padded.shape[1] - 1) & (
        lat_index == band_count - 1
    )
    return jnp.where(outside[None, :, None], jnp.zeros((), padded.dtype), padded)


def window_of(field, first_row, first_col, row_count, column_count):
    return field[
        :, first_row : first_row + row_count, first_col : first_col + column_count
    ].reshape(field.shape[0], -1)


def conv_taps(kernel, field, row_count, column_count, flip):
    total = None
    for tap_row in range(3):
        for tap_col in range(3):
            if flip:
                window = window_of(field, 2 - tap_row, 2 - tap_col, row_count, column_count)
            else:
                window = window_of(field, tap_row, tap_col, row_count, column_count)
            part = jnp.dot(kernel[tap_row, tap_col], window, preferred_element_type=jnp.float32)
            total = part if total is None else total + part
    return total


def direct_reduce_scatter(rows, axis, send_dtype):
    count, index = lax.axis_size(axis), lax.axis_index(axis)
    if count == 1:
        return rows
    chunks = rows.reshape(count, -1, rows.shape[-1])
    acc = lax.dynamic_index_in_dim(chunks, index, keepdims=False)
    for step in range(1, count):
        pairs = [(j, (j + step) % count) for j in range(count)]
        piece = lax.dynamic_index_in_dim(chunks, (index + step) % count, keepdims=False)
        acc = acc + lax.ppermute(piece.astype(send_dtype), axis, pairs).astype(jnp.float32)
    return acc


def direct_all_gather(chunk, axis, send_dtype):
    count, index = lax.axis_size(axis), lax.axis_index(axis)
    if count == 1:
        return chunk
    pieces = [chunk]
    sent = chunk.astype(send_dtype)
    for step in range(1, count):
        pairs = [(j, (j + step) % count) for j in range(count)]
        pieces.append(lax.ppermute(sent, axis, pairs).astype(jnp.float32))
    stacked = jnp.stack(pieces[::-1])
    stacked = jnp.roll(stacked, (index + 1) % count, axis=0)
    return stacked.reshape(-1, chunk.shape[-1])


def sum_start(flat, send_dtype, columns):
    parts = lax.axis_size("lat") * lax.axis_size("lon")
    quantum = parts * 16 * 128
    padded = jnp.pad(flat, (0, (-flat.size) % quantum)).reshape(-1, 128)
    rows = direct_reduce_scatter(padded, "lat", jnp.float32)
    count, index = lax.axis_size("lon"), lax.axis_index("lon")
    last, first = columns
    if count < 3:
        up = [(i, (i + 1) % count) for i in range(count)]
        down = [(j, i) for i, j in up]
        halo = (lax.ppermute(last, "lon", up), lax.ppermute(first, "lon", down))
        return direct_reduce_scatter(rows, "lon", send_dtype), halo
    chunks = rows.reshape(count, -1, rows.shape[-1])
    size = chunks.shape[1]
    acc = lax.dynamic_index_in_dim(chunks, index, keepdims=False)
    extra = {1: last, count - 1: first}
    got = {}
    for step in range(1, count):
        pairs = [(j, (j + step) % count) for j in range(count)]
        piece = lax.dynamic_index_in_dim(chunks, (index + step) % count, keepdims=False).astype(send_dtype)
        if step in extra:
            piece = jnp.concatenate([piece, extra[step].astype(send_dtype).reshape(-1, rows.shape[-1])], axis=0)
        moved = lax.ppermute(piece, "lon", pairs)
        acc = acc + moved[:size].astype(jnp.float32)
        if step in extra:
            got[step] = moved[size:].reshape(last.shape).astype(last.dtype)
    return acc, (got[1], got[count - 1])


def sum_finish(rows, size, send_dtype):
    rows = direct_all_gather(rows, "lon", send_dtype)
    rows = direct_all_gather(rows, "lat", jnp.float32)
    return rows.reshape(-1)[:size]


def border_of(padded):
    rows, cols = padded.shape[1], padded.shape[2]
    return jnp.concatenate(
        [padded[:, 0, :], padded[:, rows - 1, :], padded[:, 1 : rows - 1, 0], padded[:, 1 : rows - 1, cols - 1]],
        axis=1,
    )


def with_border(field, border):
    rows, cols = field.shape[1], field.shape[2]
    top = border[:, : cols + 2]
    bottom = border[:, cols + 2 : 2 * cols + 4]
    left = border[:, 2 * cols + 4 : 2 * cols + 4 + rows]
    right = border[:, 2 * cols + 4 + rows :]
    middle = jnp.concatenate([left[:, :, None], field, right[:, :, None]], axis=2)
    return jnp.concatenate([top[:, None, :], middle, bottom[:, None, :]], axis=1)


def local(inputs, cotangent, weight, bias_vector):
    own_channels, row_count, column_count = inputs.shape
    chan_count = lax.axis_size("chan")
    chan_index = lax.axis_index("chan")
    raw_blocks = []
    for shift in range(1, chan_count):
        pairs = [(i, (i - shift) % chan_count) for i in range(chan_count)]
        raw_blocks.append(lax.ppermute(inputs, "chan", pairs))
    input_pad = mask_rims(padded_2(inputs, (("lon", 2), ("lat", 1)), 1))
    own_border = border_of(input_pad)
    blocks = [input_pad]
    for shift in range(1, chan_count):
        pairs = [(i, (i - shift) % chan_count) for i in range(chan_count)]
        border = lax.ppermute(own_border, "chan", pairs)
        blocks.append(lax.optimization_barrier(with_border(raw_blocks[shift - 1], border)))
    kernel_cols = []
    for shift in range(chan_count):
        source = (chan_index + shift) % chan_count
        kernel_cols.append(
            lax.dynamic_slice_in_dim(weight, source * own_channels, own_channels, axis=3)
        )
    preact = None
    for shift in range(chan_count):
        part = conv_taps(kernel_cols[shift], blocks[shift], row_count, column_count, False)
        preact = part if preact is None else preact + part
    preact = preact + bias_vector[:, None]
    upstream = cotangent.reshape(own_channels, -1).astype(jnp.float32)
    grad_pre = (upstream * gelu_slope(preact)).astype(jnp.bfloat16)
    bias_part = jnp.sum(grad_pre.astype(jnp.float32), axis=1)
    input_local = jnp.concatenate(blocks, axis=0)
    taps = []
    for tap_row in range(3):
        row_taps = []
        for tap_col in range(3):
            window = window_of(input_local, tap_row, tap_col, row_count, column_count)
            row_taps.append(
                lax.dot_general(
                    grad_pre, window, (((1,), (1,)), ((), ())), preferred_element_type=jnp.float32
                )
            )
        taps.append(jnp.stack(row_taps))
    weight_part = jnp.stack(taps)
    flat = jnp.concatenate([weight_part.reshape(-1), bias_part])
    grad_field = grad_pre.reshape(own_channels, row_count, column_count)
    edges = (grad_field[:, :, column_count - 1 :], grad_field[:, :, :1])
    scattered, (before, after) = sum_start(flat, jnp.bfloat16, edges)
    grad_wide = jnp.concatenate([before, grad_field, after], axis=2)
    grad_pad = mask_rims(padded_2(grad_wide, (("lat", 1),), 1))
    outgoing = []
    for shift in range(1, chan_count):
        kernel_t = jnp.swapaxes(kernel_cols[shift], 2, 3)
        outgoing.append(conv_taps(kernel_t, grad_pad, row_count, column_count, True).astype(jnp.bfloat16))
    grad_pad, outgoing, scattered = lax.optimization_barrier((grad_pad, outgoing, scattered))
    flat = sum_finish(scattered, flat.size, jnp.bfloat16)
    weight_local = flat[: weight_part.size].reshape(weight_part.shape)
    bias_grad = flat[weight_part.size :]
    doubled = jnp.concatenate([weight_local, weight_local], axis=3)
    weight_grad = lax.dynamic_slice_in_dim(
        doubled, (chan_count - chan_index) % chan_count * own_channels, chan_count * own_channels, axis=3
    )
    received = []
    for shift in range(1, chan_count):
        pairs = [(i, (i + shift) % chan_count) for i in range(chan_count)]
        received.append(lax.ppermute(outgoing[shift - 1], "chan", pairs))
    own_part = conv_taps(jnp.swapaxes(kernel_cols[0], 2, 3), grad_pad, row_count, column_count, True)
    own_part, weight_grad, bias_grad = lax.optimization_barrier((own_part, weight_grad, bias_grad))
    for piece in received:
        own_part = own_part + piece.astype(jnp.float32)
    input_grad = own_part.astype(jnp.bfloat16).reshape(own_channels, row_count, column_count)
    return (input_grad, weight_grad, bias_grad)


def solution(mesh):
    placed = (
        P("chan", ("groups", "lat"), "lon"),
        P("chan", ("groups", "lat"), "lon"),
        P(None, None, "chan", None),
        P("chan"),
    )
    return jax.shard_map(
        local,
        mesh=mesh,
        in_specs=placed,
        out_specs=(
            P("chan", ("groups", "lat"), "lon"),
            P("groups", None, "chan", None),
            P(("groups", "chan")),
        ),
        check_vma=False,
    )
```

```python
import jax
import jax.numpy as jnp
from jax import lax
from jax.sharding import PartitionSpec as P


def padded_2(shard, sides, width):
    for axis, dim in sides:
        devices, length = (lax.axis_size(axis), shard.shape[dim])
        up = [(i, (i + 1) % devices) for i in range(devices)]
        down = [(j, i) for i, j in up]
        last = lax.slice_in_dim(shard, length - width, length, axis=dim)
        initial = lax.slice_in_dim(shard, 0, width, axis=dim)
        before = lax.ppermute(last, axis, up)
        after = lax.ppermute(initial, axis, down)
        shard = jnp.concatenate([before, shard, after], axis=dim)
    return shard


def gelu_slope(preact):
    normal_cdf = 0.5 * (1.0 + jax.scipy.special.erf(preact * 0.7071067811865476))
    density = jnp.exp(-0.5 * preact * preact) * 0.3989422804014327
    return normal_cdf + preact * density


def mask_rims(padded):
    lat_index = lax.axis_index("lat")
    band_count = lax.axis_size("lat")
    row_ids = jnp.arange(padded.shape[1])
    outside = (row_ids == 0) & (lat_index == 0) | (row_ids == padded.shape[1] - 1) & (
        lat_index == band_count - 1
    )
    return jnp.where(outside[None, :, None], jnp.zeros((), padded.dtype), padded)


def window_of(field, first_row, first_col, row_count, column_count):
    return field[
        :, first_row : first_row + row_count, first_col : first_col + column_count
    ].reshape(field.shape[0], -1)


def conv_taps(kernel, field, row_count, column_count, flip):
    total = None
    for tap_row in range(3):
        for tap_col in range(3):
            if flip:
                window = window_of(field, 2 - tap_row, 2 - tap_col, row_count, column_count)
            else:
                window = window_of(field, tap_row, tap_col, row_count, column_count)
            part = jnp.dot(kernel[tap_row, tap_col], window, preferred_element_type=jnp.float32)
            total = part if total is None else total + part
    return total


def direct_reduce_scatter(rows, axis, send_dtype):
    count, index = lax.axis_size(axis), lax.axis_index(axis)
    if count == 1:
        return rows
    chunks = rows.reshape(count, -1, rows.shape[-1])
    acc = lax.dynamic_index_in_dim(chunks, index, keepdims=False)
    for step in range(1, count):
        pairs = [(j, (j + step) % count) for j in range(count)]
        piece = lax.dynamic_index_in_dim(chunks, (index + step) % count, keepdims=False)
        acc = acc + lax.ppermute(piece.astype(send_dtype), axis, pairs).astype(jnp.float32)
    return acc


def direct_all_gather(chunk, axis, send_dtype):
    count, index = lax.axis_size(axis), lax.axis_index(axis)
    if count == 1:
        return chunk
    pieces = [chunk]
    sent = chunk.astype(send_dtype)
    for step in range(1, count):
        pairs = [(j, (j + step) % count) for j in range(count)]
        pieces.append(lax.ppermute(sent, axis, pairs).astype(jnp.float32))
    stacked = jnp.stack(pieces[::-1])
    stacked = jnp.roll(stacked, (index + 1) % count, axis=0)
    return stacked.reshape(-1, chunk.shape[-1])


def sum_start(flat, send_dtype, columns):
    parts = lax.axis_size("lat") * lax.axis_size("lon")
    quantum = parts * 16 * 128
    padded = jnp.pad(flat, (0, (-flat.size) % quantum)).reshape(-1, 128)
    rows = direct_reduce_scatter(padded, "lat", jnp.float32)
    count, index = lax.axis_size("lon"), lax.axis_index("lon")
    last, first = columns
    if count < 3:
        up = [(i, (i + 1) % count) for i in range(count)]
        down = [(j, i) for i, j in up]
        halo = (lax.ppermute(last, "lon", up), lax.ppermute(first, "lon", down))
        return direct_reduce_scatter(rows, "lon", send_dtype), halo
    chunks = rows.reshape(count, -1, rows.shape[-1])
    size = chunks.shape[1]
    acc = lax.dynamic_index_in_dim(chunks, index, keepdims=False)
    extra = {1: last, count - 1: first}
    got = {}
    for step in range(1, count):
        pairs = [(j, (j + step) % count) for j in range(count)]
        piece = lax.dynamic_index_in_dim(chunks, (index + step) % count, keepdims=False).astype(send_dtype)
        if step in extra:
            piece = jnp.concatenate([piece, extra[step].astype(send_dtype).reshape(-1, rows.shape[-1])], axis=0)
        moved = lax.ppermute(piece, "lon", pairs)
        acc = acc + moved[:size].astype(jnp.float32)
        if step in extra:
            got[step] = moved[size:].reshape(last.shape).astype(last.dtype)
    return acc, (got[1], got[count - 1])


def sum_finish(rows, size, send_dtype):
    rows = direct_all_gather(rows, "lon", send_dtype)
    rows = direct_all_gather(rows, "lat", jnp.float32)
    return rows.reshape(-1)[:size]


def border_of(padded):
    rows, cols = padded.shape[1], padded.shape[2]
    return jnp.concatenate(
        [padded[:, 0, :], padded[:, rows - 1, :], padded[:, 1 : rows - 1, 0], padded[:, 1 : rows - 1, cols - 1]],
        axis=1,
    )


def with_border(field, border):
    rows, cols = field.shape[1], field.shape[2]
    top = border[:, : cols + 2]
    bottom = border[:, cols + 2 : 2 * cols + 4]
    left = border[:, 2 * cols + 4 : 2 * cols + 4 + rows]
    right = border[:, 2 * cols + 4 + rows :]
    middle = jnp.concatenate([left[:, :, None], field, right[:, :, None]], axis=2)
    return jnp.concatenate([top[:, None, :], middle, bottom[:, None, :]], axis=1)


def local(inputs, cotangent, weight, bias_vector):
    own_channels, row_count, column_count = inputs.shape
    chan_count = lax.axis_size("chan")
    chan_index = lax.axis_index("chan")
    raw_blocks = []
    for shift in range(1, chan_count):
        pairs = [(i, (i - shift) % chan_count) for i in range(chan_count)]
        stored = inputs.reshape(-1, column_count)
        raw_blocks.append(lax.ppermute(stored, "chan", pairs).reshape(inputs.shape))
    input_pad = mask_rims(padded_2(inputs, (("lon", 2), ("lat", 1)), 1))
    own_border = border_of(input_pad)
    blocks = [input_pad]
    for shift in range(1, chan_count):
        pairs = [(i, (i - shift) % chan_count) for i in range(chan_count)]
        border = lax.ppermute(own_border, "chan", pairs)
        blocks.append(lax.optimization_barrier(with_border(raw_blocks[shift - 1], border)))
    kernel_cols = []
    for shift in range(chan_count):
        source = (chan_index + shift) % chan_count
        kernel_cols.append(
            lax.dynamic_slice_in_dim(weight, source * own_channels, own_channels, axis=3)
        )
    preact = None
    for shift in range(chan_count):
        part = conv_taps(kernel_cols[shift], blocks[shift], row_count, column_count, False)
        preact = part if preact is None else preact + part
    preact = preact + bias_vector[:, None]
    upstream = cotangent.reshape(own_channels, -1).astype(jnp.float32)
    grad_pre = (upstream * gelu_slope(preact)).astype(jnp.bfloat16)
    bias_part = jnp.sum(grad_pre.astype(jnp.float32), axis=1)
    input_local = jnp.concatenate(blocks, axis=0)
    taps = []
    for tap_row in range(3):
        row_taps = []
        for tap_col in range(3):
            window = window_of(input_local, tap_row, tap_col, row_count, column_count)
            row_taps.append(
                lax.dot_general(
                    grad_pre, window, (((1,), (1,)), ((), ())), preferred_element_type=jnp.float32
                )
            )
        taps.append(jnp.stack(row_taps))
    weight_part = jnp.stack(taps)
    flat = jnp.concatenate([weight_part.reshape(-1), bias_part])
    grad_field = grad_pre.reshape(own_channels, row_count, column_count)
    edges = (grad_field[:, :, column_count - 1 :], grad_field[:, :, :1])
    scattered, (before, after) = sum_start(flat, jnp.bfloat16, edges)
    flat = sum_finish(scattered, flat.size, jnp.bfloat16)
    weight_local = flat[: weight_part.size].reshape(weight_part.shape)
    bias_grad = flat[weight_part.size :]
    doubled = jnp.concatenate([weight_local, weight_local], axis=3)
    weight_grad = lax.dynamic_slice_in_dim(
        doubled, (chan_count - chan_index) % chan_count * own_channels, chan_count * own_channels, axis=3
    )
    grad_wide = jnp.concatenate([before, grad_field, after], axis=2)
    grad_pad = mask_rims(padded_2(grad_wide, (("lat", 1),), 1))
    outgoing = []
    for shift in range(1, chan_count):
        kernel_t = jnp.swapaxes(kernel_cols[shift], 2, 3)
        outgoing.append(conv_taps(kernel_t, grad_pad, row_count, column_count, True).astype(jnp.bfloat16))
    grad_pad, outgoing = lax.optimization_barrier((grad_pad, outgoing))
    received = []
    for shift in range(1, chan_count):
        pairs = [(i, (i + shift) % chan_count) for i in range(chan_count)]
        received.append(lax.ppermute(outgoing[shift - 1], "chan", pairs))
    own_part = conv_taps(jnp.swapaxes(kernel_cols[0], 2, 3), grad_pad, row_count, column_count, True)
    own_part, weight_grad, bias_grad = lax.optimization_barrier((own_part, weight_grad, bias_grad))
    for piece in received:
        own_part = own_part + piece.astype(jnp.float32)
    input_grad = own_part.astype(jnp.bfloat16).reshape(own_channels, row_count, column_count)
    return (input_grad, weight_grad, bias_grad)


def solution(mesh):
    placed = (
        P("chan", ("groups", "lat"), "lon"),
        P("chan", ("groups", "lat"), "lon"),
        P(None, None, "chan", None),
        P("chan"),
    )
    return jax.shard_map(
        local,
        mesh=mesh,
        in_specs=placed,
        out_specs=(
            P("chan", ("groups", "lat"), "lon"),
            P("groups", None, "chan", None),
            P(("groups", "chan")),
        ),
        check_vma=False,
    )
```

```python
import jax
import jax.numpy as jnp
from jax import lax
from jax.sharding import PartitionSpec as P


def padded_2(shard, sides, width):
    for axis, dim in sides:
        devices, length = (lax.axis_size(axis), shard.shape[dim])
        up = [(i, (i + 1) % devices) for i in range(devices)]
        down = [(j, i) for i, j in up]
        last = lax.slice_in_dim(shard, length - width, length, axis=dim)
        initial = lax.slice_in_dim(shard, 0, width, axis=dim)
        before = lax.ppermute(last, axis, up)
        after = lax.ppermute(initial, axis, down)
        shard = jnp.concatenate([before, shard, after], axis=dim)
    return shard


def gelu_slope(preact):
    normal_cdf = 0.5 * (1.0 + jax.scipy.special.erf(preact * 0.7071067811865476))
    density = jnp.exp(-0.5 * preact * preact) * 0.3989422804014327
    return normal_cdf + preact * density


def mask_rims(padded):
    lat_index = lax.axis_index("lat")
    band_count = lax.axis_size("lat")
    row_ids = jnp.arange(padded.shape[1])
    outside = (row_ids == 0) & (lat_index == 0) | (row_ids == padded.shape[1] - 1) & (
        lat_index == band_count - 1
    )
    return jnp.where(outside[None, :, None], jnp.zeros((), padded.dtype), padded)


def window_of(field, first_row, first_col, row_count, column_count):
    return field[
        :, first_row : first_row + row_count, first_col : first_col + column_count
    ].reshape(field.shape[0], -1)


def conv_taps(kernel, field, row_count, column_count, flip):
    total = None
    for tap_row in range(3):
        for tap_col in range(3):
            if flip:
                window = window_of(field, 2 - tap_row, 2 - tap_col, row_count, column_count)
            else:
                window = window_of(field, tap_row, tap_col, row_count, column_count)
            part = jnp.dot(kernel[tap_row, tap_col], window, preferred_element_type=jnp.float32)
            total = part if total is None else total + part
    return total


def direct_reduce_scatter(rows, axis, send_dtype):
    count, index = lax.axis_size(axis), lax.axis_index(axis)
    if count == 1:
        return rows
    chunks = rows.reshape(count, -1, rows.shape[-1])
    acc = lax.dynamic_index_in_dim(chunks, index, keepdims=False)
    for step in range(1, count):
        pairs = [(j, (j + step) % count) for j in range(count)]
        piece = lax.dynamic_index_in_dim(chunks, (index + step) % count, keepdims=False)
        acc = acc + lax.ppermute(piece.astype(send_dtype), axis, pairs).astype(jnp.float32)
    return acc


def direct_all_gather(chunk, axis, send_dtype):
    count, index = lax.axis_size(axis), lax.axis_index(axis)
    if count == 1:
        return chunk
    pieces = [chunk]
    sent = chunk.astype(send_dtype)
    for step in range(1, count):
        pairs = [(j, (j + step) % count) for j in range(count)]
        pieces.append(lax.ppermute(sent, axis, pairs).astype(jnp.float32))
    stacked = jnp.stack(pieces[::-1])
    stacked = jnp.roll(stacked, (index + 1) % count, axis=0)
    return stacked.reshape(-1, chunk.shape[-1])


def sum_start(flat, send_dtype, columns):
    parts = lax.axis_size("lat") * lax.axis_size("lon")
    quantum = parts * 16 * 128
    padded = jnp.pad(flat, (0, (-flat.size) % quantum)).reshape(-1, 128)
    rows = direct_reduce_scatter(padded, "lat", jnp.float32)
    count, index = lax.axis_size("lon"), lax.axis_index("lon")
    last, first = columns
    if count < 3:
        up = [(i, (i + 1) % count) for i in range(count)]
        down = [(j, i) for i, j in up]
        halo = (lax.ppermute(last, "lon", up), lax.ppermute(first, "lon", down))
        return direct_reduce_scatter(rows, "lon", send_dtype), halo
    chunks = rows.reshape(count, -1, rows.shape[-1])
    size = chunks.shape[1]
    acc = lax.dynamic_index_in_dim(chunks, index, keepdims=False)
    extra = {1: last, count - 1: first}
    got = {}
    for step in range(1, count):
        pairs = [(j, (j + step) % count) for j in range(count)]
        piece = lax.dynamic_index_in_dim(chunks, (index + step) % count, keepdims=False).astype(send_dtype)
        if step in extra:
            piece = jnp.concatenate([piece, extra[step].astype(send_dtype).reshape(-1, rows.shape[-1])], axis=0)
        moved = lax.ppermute(piece, "lon", pairs)
        acc = acc + moved[:size].astype(jnp.float32)
        if step in extra:
            got[step] = moved[size:].reshape(last.shape).astype(last.dtype)
    return acc, (got[1], got[count - 1])


def sum_finish(rows, size, send_dtype):
    rows = direct_all_gather(rows, "lon", send_dtype)
    rows = direct_all_gather(rows, "lat", jnp.float32)
    return rows.reshape(-1)[:size]


def border_of(padded):
    rows, cols = padded.shape[1], padded.shape[2]
    return jnp.concatenate(
        [padded[:, 0, :], padded[:, rows - 1, :], padded[:, 1 : rows - 1, 0], padded[:, 1 : rows - 1, cols - 1]],
        axis=1,
    )


def with_border(field, border):
    rows, cols = field.shape[1], field.shape[2]
    top = border[:, : cols + 2]
    bottom = border[:, cols + 2 : 2 * cols + 4]
    left = border[:, 2 * cols + 4 : 2 * cols + 4 + rows]
    right = border[:, 2 * cols + 4 + rows :]
    middle = jnp.concatenate([left[:, :, None], field, right[:, :, None]], axis=2)
    return jnp.concatenate([top[:, None, :], middle, bottom[:, None, :]], axis=1)


def local(inputs, cotangent, weight, bias_vector):
    own_channels, row_count, column_count = inputs.shape
    chan_count = lax.axis_size("chan")
    chan_index = lax.axis_index("chan")
    raw_blocks = []
    for shift in range(1, chan_count):
        pairs = [(i, (i - shift) % chan_count) for i in range(chan_count)]
        raw_blocks.append(lax.ppermute(inputs, "chan", pairs))
    input_pad = mask_rims(padded_2(inputs, (("lon", 2), ("lat", 1)), 1))
    own_border = border_of(input_pad)
    blocks = [input_pad]
    for shift in range(1, chan_count):
        pairs = [(i, (i - shift) % chan_count) for i in range(chan_count)]
        border = lax.ppermute(own_border, "chan", pairs)
        blocks.append(lax.optimization_barrier(with_border(raw_blocks[shift - 1], border)))
    kernel_cols = []
    for shift in range(chan_count):
        source = (chan_index + shift) % chan_count
        kernel_cols.append(
            lax.dynamic_slice_in_dim(weight, source * own_channels, own_channels, axis=3)
        )
    kernel_sends = []
    for shift in range(1, chan_count):
        target = (chan_index + shift) % chan_count
        kernel_sends.append(lax.dynamic_slice_in_dim(weight, target * own_channels, own_channels, axis=3))
    kernel_sends, _ = lax.optimization_barrier((kernel_sends, raw_blocks))
    kernel_blocks = []
    for shift in range(1, chan_count):
        pairs = [(i, (i + shift) % chan_count) for i in range(chan_count)]
        kernel_blocks.append(lax.ppermute(kernel_sends[shift - 1], "chan", pairs))
    preact = None
    for shift in range(chan_count):
        part = conv_taps(kernel_cols[shift], blocks[shift], row_count, column_count, False)
        preact = part if preact is None else preact + part
    preact = preact + bias_vector[:, None]
    upstream = cotangent.reshape(own_channels, -1).astype(jnp.float32)
    grad_pre = (upstream * gelu_slope(preact)).astype(jnp.bfloat16)
    bias_part = jnp.sum(grad_pre.astype(jnp.float32), axis=1)
    input_local = jnp.concatenate(blocks, axis=0)
    taps = []
    for tap_row in range(3):
        row_taps = []
        for tap_col in range(3):
            window = window_of(input_local, tap_row, tap_col, row_count, column_count)
            row_taps.append(
                lax.dot_general(
                    grad_pre, window, (((1,), (1,)), ((), ())), preferred_element_type=jnp.float32
                )
            )
        taps.append(jnp.stack(row_taps))
    weight_part = jnp.stack(taps)
    flat = jnp.concatenate([weight_part.reshape(-1), bias_part])
    flat, kernel_blocks = lax.optimization_barrier((flat, kernel_blocks))
    grad_field = grad_pre.reshape(own_channels, row_count, column_count)
    edges = (grad_field[:, :, column_count - 1 :], grad_field[:, :, :1])
    scattered, (before, after) = sum_start(flat, jnp.bfloat16, edges)
    grad_blocks = []
    for shift in range(1, chan_count):
        pairs = [(i, (i + shift) % chan_count) for i in range(chan_count)]
        grad_blocks.append(lax.ppermute(grad_field, "chan", pairs))
    scattered, grad_blocks = lax.optimization_barrier((scattered, grad_blocks))
    flat = sum_finish(scattered, flat.size, jnp.bfloat16)
    weight_local = flat[: weight_part.size].reshape(weight_part.shape)
    bias_grad = flat[weight_part.size :]
    doubled = jnp.concatenate([weight_local, weight_local], axis=3)
    weight_grad = lax.dynamic_slice_in_dim(
        doubled, (chan_count - chan_index) % chan_count * own_channels, chan_count * own_channels, axis=3
    )
    grad_wide = jnp.concatenate([before, grad_field, after], axis=2)
    grad_pad = mask_rims(padded_2(grad_wide, (("lat", 1),), 1))
    grad_border = border_of(grad_pad)
    input_sum = conv_taps(jnp.swapaxes(kernel_cols[0], 2, 3), grad_pad, row_count, column_count, True)
    for shift in range(1, chan_count):
        pairs = [(i, (i + shift) % chan_count) for i in range(chan_count)]
        border = lax.ppermute(grad_border, "chan", pairs)
        block = lax.optimization_barrier(with_border(grad_blocks[shift - 1], border))
        kernel_t = jnp.swapaxes(kernel_blocks[shift - 1], 2, 3)
        input_sum = input_sum + conv_taps(kernel_t, block, row_count, column_count, True)
    input_grad = input_sum.astype(jnp.bfloat16).reshape(own_channels, row_count, column_count)
    return (input_grad, weight_grad, bias_grad)


def solution(mesh):
    placed = (
        P("chan", ("groups", "lat"), "lon"),
        P("chan", ("groups", "lat"), "lon"),
        P(None, None, "chan", None),
        P("chan"),
    )
    return jax.shard_map(
        local,
        mesh=mesh,
        in_specs=placed,
        out_specs=(
            P("chan", ("groups", "lat"), "lon"),
            P("groups", None, "chan", None),
            P(("groups", "chan")),
        ),
        check_vma=False,
    )
```

```python
import jax
import jax.numpy as jnp
from jax import lax
from jax.sharding import PartitionSpec as P


def padded_2(shard, sides, width):
    for axis, dim in sides:
        devices, length = (lax.axis_size(axis), shard.shape[dim])
        up = [(i, (i + 1) % devices) for i in range(devices)]
        down = [(j, i) for i, j in up]
        last = lax.slice_in_dim(shard, length - width, length, axis=dim)
        initial = lax.slice_in_dim(shard, 0, width, axis=dim)
        before = lax.ppermute(last, axis, up)
        after = lax.ppermute(initial, axis, down)
        shard = jnp.concatenate([before, shard, after], axis=dim)
    return shard


def gelu_slope(preact):
    normal_cdf = 0.5 * (1.0 + jax.scipy.special.erf(preact * 0.7071067811865476))
    density = jnp.exp(-0.5 * preact * preact) * 0.3989422804014327
    return normal_cdf + preact * density


def mask_rims(padded):
    lat_index = lax.axis_index("lat")
    band_count = lax.axis_size("lat")
    row_ids = jnp.arange(padded.shape[1])
    outside = (row_ids == 0) & (lat_index == 0) | (row_ids == padded.shape[1] - 1) & (
        lat_index == band_count - 1
    )
    return jnp.where(outside[None, :, None], jnp.zeros((), padded.dtype), padded)


def window_of(field, first_row, first_col, row_count, column_count):
    return field[
        :, first_row : first_row + row_count, first_col : first_col + column_count
    ].reshape(field.shape[0], -1)


def conv_taps(kernel, field, row_count, column_count, flip):
    total = None
    for tap_row in range(3):
        for tap_col in range(3):
            if flip:
                window = window_of(field, 2 - tap_row, 2 - tap_col, row_count, column_count)
            else:
                window = window_of(field, tap_row, tap_col, row_count, column_count)
            part = jnp.dot(kernel[tap_row, tap_col], window, preferred_element_type=jnp.float32)
            total = part if total is None else total + part
    return total


def direct_reduce_scatter(rows, axis, send_dtype):
    count, index = lax.axis_size(axis), lax.axis_index(axis)
    if count == 1:
        return rows
    chunks = rows.reshape(count, -1, rows.shape[-1])
    acc = lax.dynamic_index_in_dim(chunks, index, keepdims=False)
    for step in range(1, count):
        pairs = [(j, (j + step) % count) for j in range(count)]
        piece = lax.dynamic_index_in_dim(chunks, (index + step) % count, keepdims=False)
        acc = acc + lax.ppermute(piece.astype(send_dtype), axis, pairs).astype(jnp.float32)
    return acc


def direct_all_gather(chunk, axis, send_dtype):
    count, index = lax.axis_size(axis), lax.axis_index(axis)
    if count == 1:
        return chunk
    pieces = [chunk]
    sent = chunk.astype(send_dtype)
    for step in range(1, count):
        pairs = [(j, (j + step) % count) for j in range(count)]
        pieces.append(lax.ppermute(sent, axis, pairs).astype(jnp.float32))
    stacked = jnp.stack(pieces[::-1])
    stacked = jnp.roll(stacked, (index + 1) % count, axis=0)
    return stacked.reshape(-1, chunk.shape[-1])


def sum_start(flat, send_dtype, columns):
    parts = lax.axis_size("lat") * lax.axis_size("lon")
    quantum = parts * 16 * 128
    padded = jnp.pad(flat, (0, (-flat.size) % quantum)).reshape(-1, 128)
    rows = direct_reduce_scatter(padded, "lat", jnp.float32)
    count, index = lax.axis_size("lon"), lax.axis_index("lon")
    last, first = columns
    if count < 3:
        up = [(i, (i + 1) % count) for i in range(count)]
        down = [(j, i) for i, j in up]
        halo = (lax.ppermute(last, "lon", up), lax.ppermute(first, "lon", down))
        return direct_reduce_scatter(rows, "lon", send_dtype), halo
    chunks = rows.reshape(count, -1, rows.shape[-1])
    size = chunks.shape[1]
    acc = lax.dynamic_index_in_dim(chunks, index, keepdims=False)
    extra = {1: last, count - 1: first}
    got = {}
    for step in range(1, count):
        pairs = [(j, (j + step) % count) for j in range(count)]
        piece = lax.dynamic_index_in_dim(chunks, (index + step) % count, keepdims=False).astype(send_dtype)
        if step in extra:
            piece = jnp.concatenate([piece, extra[step].astype(send_dtype).reshape(-1, rows.shape[-1])], axis=0)
        moved = lax.ppermute(piece, "lon", pairs)
        acc = acc + moved[:size].astype(jnp.float32)
        if step in extra:
            got[step] = moved[size:].reshape(last.shape).astype(last.dtype)
    return acc, (got[1], got[count - 1])


def sum_finish(rows, size, send_dtype):
    rows = direct_all_gather(rows, "lon", send_dtype)
    rows = direct_all_gather(rows, "lat", jnp.float32)
    return rows.reshape(-1)[:size]


def border_of(padded):
    rows, cols = padded.shape[1], padded.shape[2]
    return jnp.concatenate(
        [padded[:, 0, :], padded[:, rows - 1, :], padded[:, 1 : rows - 1, 0], padded[:, 1 : rows - 1, cols - 1]],
        axis=1,
    )


def with_border(field, border):
    rows, cols = field.shape[1], field.shape[2]
    top = border[:, : cols + 2]
    bottom = border[:, cols + 2 : 2 * cols + 4]
    left = border[:, 2 * cols + 4 : 2 * cols + 4 + rows]
    right = border[:, 2 * cols + 4 + rows :]
    middle = jnp.concatenate([left[:, :, None], field, right[:, :, None]], axis=2)
    return jnp.concatenate([top[:, None, :], middle, bottom[:, None, :]], axis=1)


def local(inputs, cotangent, weight, bias_vector):
    own_channels, row_count, column_count = inputs.shape
    chan_count = lax.axis_size("chan")
    chan_index = lax.axis_index("chan")
    raw_blocks = []
    for shift in range(1, chan_count):
        pairs = [(i, (i - shift) % chan_count) for i in range(chan_count)]
        raw_blocks.append(lax.ppermute(inputs, "chan", pairs))
    input_pad = mask_rims(padded_2(inputs, (("lon", 2), ("lat", 1)), 1))
    own_border = border_of(input_pad)
    blocks = [input_pad]
    for shift in range(1, chan_count):
        pairs = [(i, (i - shift) % chan_count) for i in range(chan_count)]
        border = lax.ppermute(own_border, "chan", pairs)
        blocks.append(lax.optimization_barrier(with_border(raw_blocks[shift - 1], border)))
    kernel_cols = []
    for shift in range(chan_count):
        source = (chan_index + shift) % chan_count
        kernel_cols.append(
            lax.dynamic_slice_in_dim(weight, source * own_channels, own_channels, axis=3)
        )
    preact = None
    for shift in range(chan_count):
        part = conv_taps(kernel_cols[shift], blocks[shift], row_count, column_count, False)
        preact = part if preact is None else preact + part
    preact = preact + bias_vector[:, None]
    upstream = cotangent.reshape(own_channels, -1).astype(jnp.float32)
    grad_pre = (upstream * gelu_slope(preact)).astype(jnp.bfloat16)
    bias_part = jnp.sum(grad_pre.astype(jnp.float32), axis=1)
    input_local = jnp.concatenate(blocks, axis=0)
    taps = []
    for tap_row in range(3):
        row_taps = []
        for tap_col in range(3):
            window = window_of(input_local, tap_row, tap_col, row_count, column_count)
            row_taps.append(
                lax.dot_general(
                    grad_pre, window, (((1,), (1,)), ((), ())), preferred_element_type=jnp.float32
                )
            )
        taps.append(jnp.stack(row_taps))
    weight_part = jnp.stack(taps)
    flat = jnp.concatenate([weight_part.reshape(-1), bias_part])
    grad_field = grad_pre.reshape(own_channels, row_count, column_count)
    edges = (grad_field[:, :, column_count - 1 :], grad_field[:, :, :1])
    scattered, (before, after) = sum_start(flat, jnp.bfloat16, edges)
    flat = sum_finish(scattered, flat.size, jnp.bfloat16)
    weight_local = flat[: weight_part.size].reshape(weight_part.shape)
    bias_grad = flat[weight_part.size :]
    doubled = jnp.concatenate([weight_local, weight_local], axis=3)
    weight_grad = lax.dynamic_slice_in_dim(
        doubled, (chan_count - chan_index) % chan_count * own_channels, chan_count * own_channels, axis=3
    )
    grad_wide = jnp.concatenate([before, grad_field, after], axis=2)
    grad_pad = mask_rims(padded_2(grad_wide, (("lat", 1),), 1))
    outgoing = []
    for shift in range(1, chan_count):
        kernel_t = jnp.swapaxes(kernel_cols[shift], 2, 3)
        half = own_channels // 2 if own_channels % 32 == 0 else own_channels
        outgoing.append(
            [
                conv_taps(kernel_t[:, :, lo : lo + half], grad_pad, row_count, column_count, True).astype(jnp.bfloat16)
                for lo in range(0, own_channels, half)
            ]
        )
    grad_pad, outgoing = lax.optimization_barrier((grad_pad, outgoing))
    received = []
    for shift in range(1, chan_count):
        pairs = [(i, (i + shift) % chan_count) for i in range(chan_count)]
        pieces = [lax.ppermute(piece, "chan", pairs) for piece in outgoing[shift - 1]]
        received.append(jnp.concatenate(pieces, axis=0))
    own_part = conv_taps(jnp.swapaxes(kernel_cols[0], 2, 3), grad_pad, row_count, column_count, True)
    own_part, weight_grad, bias_grad = lax.optimization_barrier((own_part, weight_grad, bias_grad))
    for piece in received:
        own_part = own_part + piece.astype(jnp.float32)
    input_grad = own_part.astype(jnp.bfloat16).reshape(own_channels, row_count, column_count)
    return (input_grad, weight_grad, bias_grad)


def solution(mesh):
    placed = (
        P("chan", ("groups", "lat"), "lon"),
        P("chan", ("groups", "lat"), "lon"),
        P(None, None, "chan", None),
        P("chan"),
    )
    return jax.shard_map(
        local,
        mesh=mesh,
        in_specs=placed,
        out_specs=(
            P("chan", ("groups", "lat"), "lon"),
            P("groups", None, "chan", None),
            P(("groups", "chan")),
        ),
        check_vma=False,
    )
```

```python
import jax
import jax.numpy as jnp
from jax import lax
from jax.sharding import PartitionSpec as P


def padded_2(shard, sides, width):
    for axis, dim in sides:
        devices, length = (lax.axis_size(axis), shard.shape[dim])
        up = [(i, (i + 1) % devices) for i in range(devices)]
        down = [(j, i) for i, j in up]
        last = lax.slice_in_dim(shard, length - width, length, axis=dim)
        initial = lax.slice_in_dim(shard, 0, width, axis=dim)
        before = lax.ppermute(last, axis, up)
        after = lax.ppermute(initial, axis, down)
        shard = jnp.concatenate([before, shard, after], axis=dim)
    return shard


def gelu_slope(preact):
    normal_cdf = 0.5 * (1.0 + jax.scipy.special.erf(preact * 0.7071067811865476))
    density = jnp.exp(-0.5 * preact * preact) * 0.3989422804014327
    return normal_cdf + preact * density


def mask_rims(padded):
    lat_index = lax.axis_index("lat")
    band_count = lax.axis_size("lat")
    row_ids = jnp.arange(padded.shape[1])
    outside = (row_ids == 0) & (lat_index == 0) | (row_ids == padded.shape[1] - 1) & (
        lat_index == band_count - 1
    )
    return jnp.where(outside[None, :, None], jnp.zeros((), padded.dtype), padded)


def window_of(field, first_row, first_col, row_count, column_count):
    return field[
        :, first_row : first_row + row_count, first_col : first_col + column_count
    ].reshape(field.shape[0], -1)


def conv_taps(kernel, field, row_count, column_count, flip):
    total = None
    for tap_row in range(3):
        for tap_col in range(3):
            if flip:
                window = window_of(field, 2 - tap_row, 2 - tap_col, row_count, column_count)
            else:
                window = window_of(field, tap_row, tap_col, row_count, column_count)
            part = jnp.dot(kernel[tap_row, tap_col], window, preferred_element_type=jnp.float32)
            total = part if total is None else total + part
    return total


def direct_reduce_scatter(rows, axis, send_dtype):
    count, index = lax.axis_size(axis), lax.axis_index(axis)
    if count == 1:
        return rows
    chunks = rows.reshape(count, -1, rows.shape[-1])
    acc = lax.dynamic_index_in_dim(chunks, index, keepdims=False)
    for step in range(1, count):
        pairs = [(j, (j + step) % count) for j in range(count)]
        piece = lax.dynamic_index_in_dim(chunks, (index + step) % count, keepdims=False)
        acc = acc + lax.ppermute(piece.astype(send_dtype), axis, pairs).astype(jnp.float32)
    return acc


def direct_all_gather(chunk, axis, send_dtype):
    count, index = lax.axis_size(axis), lax.axis_index(axis)
    if count == 1:
        return chunk
    pieces = [chunk]
    sent = chunk.astype(send_dtype)
    for step in range(1, count):
        pairs = [(j, (j + step) % count) for j in range(count)]
        pieces.append(lax.ppermute(sent, axis, pairs).astype(jnp.float32))
    stacked = jnp.stack(pieces[::-1])
    stacked = jnp.roll(stacked, (index + 1) % count, axis=0)
    return stacked.reshape(-1, chunk.shape[-1])


def sum_start(flat, send_dtype, columns):
    parts = lax.axis_size("lat") * lax.axis_size("lon")
    quantum = parts * 16 * 128
    padded = jnp.pad(flat, (0, (-flat.size) % quantum)).reshape(-1, 128)
    rows = direct_reduce_scatter(padded, "lat", jnp.float32)
    count, index = lax.axis_size("lon"), lax.axis_index("lon")
    last, first = columns
    if count < 3:
        up = [(i, (i + 1) % count) for i in range(count)]
        down = [(j, i) for i, j in up]
        halo = (lax.ppermute(last, "lon", up), lax.ppermute(first, "lon", down))
        return direct_reduce_scatter(rows, "lon", send_dtype), halo
    chunks = rows.reshape(count, -1, rows.shape[-1])
    size = chunks.shape[1]
    acc = lax.dynamic_index_in_dim(chunks, index, keepdims=False)
    extra = {1: last, count - 1: first}
    got = {}
    for step in range(1, count):
        pairs = [(j, (j + step) % count) for j in range(count)]
        piece = lax.dynamic_index_in_dim(chunks, (index + step) % count, keepdims=False).astype(send_dtype)
        if step in extra:
            piece = jnp.concatenate([piece, extra[step].astype(send_dtype).reshape(-1, rows.shape[-1])], axis=0)
        moved = lax.ppermute(piece, "lon", pairs)
        acc = acc + moved[:size].astype(jnp.float32)
        if step in extra:
            got[step] = moved[size:].reshape(last.shape).astype(last.dtype)
    return acc, (got[1], got[count - 1])


def sum_finish(rows, size, send_dtype):
    rows = direct_all_gather(rows, "lon", send_dtype)
    rows = direct_all_gather(rows, "lat", jnp.float32)
    return rows.reshape(-1)[:size]


def border_of(padded):
    rows, cols = padded.shape[1], padded.shape[2]
    return jnp.concatenate(
        [padded[:, 0, :], padded[:, rows - 1, :], padded[:, 1 : rows - 1, 0], padded[:, 1 : rows - 1, cols - 1]],
        axis=1,
    )


def with_border(field, border):
    rows, cols = field.shape[1], field.shape[2]
    top = border[:, : cols + 2]
    bottom = border[:, cols + 2 : 2 * cols + 4]
    left = border[:, 2 * cols + 4 : 2 * cols + 4 + rows]
    right = border[:, 2 * cols + 4 + rows :]
    middle = jnp.concatenate([left[:, :, None], field, right[:, :, None]], axis=2)
    return jnp.concatenate([top[:, None, :], middle, bottom[:, None, :]], axis=1)


def local(inputs, cotangent, weight, bias_vector):
    own_channels, row_count, column_count = inputs.shape
    chan_count = lax.axis_size("chan")
    chan_index = lax.axis_index("chan")
    raw_blocks = []
    for shift in range(1, chan_count):
        pairs = [(i, (i - shift) % chan_count) for i in range(chan_count)]
        raw_blocks.append(lax.ppermute(inputs, "chan", pairs))
    input_pad = mask_rims(padded_2(inputs, (("lon", 2), ("lat", 1)), 1))
    own_border = border_of(input_pad)
    blocks = [input_pad]
    for shift in range(1, chan_count):
        pairs = [(i, (i - shift) % chan_count) for i in range(chan_count)]
        border = lax.ppermute(own_border, "chan", pairs)
        blocks.append(lax.optimization_barrier(with_border(raw_blocks[shift - 1], border)))
    kernel_cols = []
    for shift in range(chan_count):
        source = (chan_index + shift) % chan_count
        kernel_cols.append(
            lax.dynamic_slice_in_dim(weight, source * own_channels, own_channels, axis=3)
        )
    preact = None
    for shift in range(chan_count):
        part = conv_taps(kernel_cols[shift], blocks[shift], row_count, column_count, False)
        preact = part if preact is None else preact + part
    preact = preact + bias_vector[:, None]
    upstream = cotangent.reshape(own_channels, -1).astype(jnp.float32)
    grad_pre = (upstream * gelu_slope(preact)).astype(jnp.bfloat16)
    bias_part = jnp.sum(grad_pre.astype(jnp.float32), axis=1)
    input_local = jnp.concatenate(blocks, axis=0)
    taps = []
    for tap_row in range(3):
        row_taps = []
        for tap_col in range(3):
            window = window_of(input_local, tap_row, tap_col, row_count, column_count)
            row_taps.append(
                lax.dot_general(
                    grad_pre, window, (((1,), (1,)), ((), ())), preferred_element_type=jnp.float32
                )
            )
        taps.append(jnp.stack(row_taps))
    weight_part = jnp.stack(taps)
    flat = jnp.concatenate([weight_part.reshape(-1), bias_part])
    grad_field = grad_pre.reshape(own_channels, row_count, column_count)
    edges = (grad_field[:, :, column_count - 1 :], grad_field[:, :, :1])
    scattered, (before, after) = sum_start(flat, jnp.bfloat16, edges)
    grad_wide = jnp.concatenate([before, grad_field, after], axis=2)
    grad_pad = mask_rims(padded_2(grad_wide, (("lat", 1),), 1))
    outgoing = []
    for shift in range(1, chan_count):
        kernel_t = jnp.swapaxes(kernel_cols[shift], 2, 3)
        outgoing.append(conv_taps(kernel_t, grad_pad, row_count, column_count, True).astype(jnp.bfloat16))
    grad_pad, outgoing = lax.optimization_barrier((grad_pad, outgoing))
    received = []
    for shift in range(1, chan_count):
        pairs = [(i, (i + shift) % chan_count) for i in range(chan_count)]
        received.append(lax.ppermute(outgoing[shift - 1], "chan", pairs))
    own_part = conv_taps(jnp.swapaxes(kernel_cols[0], 2, 3), grad_pad, row_count, column_count, True)
    own_part, scattered = lax.optimization_barrier((own_part, scattered))
    flat = sum_finish(scattered, flat.size, jnp.bfloat16)
    weight_local = flat[: weight_part.size].reshape(weight_part.shape)
    bias_grad = flat[weight_part.size :]
    doubled = jnp.concatenate([weight_local, weight_local], axis=3)
    weight_grad = lax.dynamic_slice_in_dim(
        doubled, (chan_count - chan_index) % chan_count * own_channels, chan_count * own_channels, axis=3
    )
    own_part, weight_grad, bias_grad = lax.optimization_barrier((own_part, weight_grad, bias_grad))
    for piece in received:
        own_part = own_part + piece.astype(jnp.float32)
    input_grad = own_part.astype(jnp.bfloat16).reshape(own_channels, row_count, column_count)
    return (input_grad, weight_grad, bias_grad)


def solution(mesh):
    placed = (
        P("chan", ("groups", "lat"), "lon"),
        P("chan", ("groups", "lat"), "lon"),
        P(None, None, "chan", None),
        P("chan"),
    )
    return jax.shard_map(
        local,
        mesh=mesh,
        in_specs=placed,
        out_specs=(
            P("chan", ("groups", "lat"), "lon"),
            P("groups", None, "chan", None),
            P(("groups", "chan")),
        ),
        check_vma=False,
    )
```

```python
import jax
import jax.numpy as jnp
from jax import lax
from jax.sharding import PartitionSpec as P


def padded_2(shard, sides, width):
    for axis, dim in sides:
        devices, length = (lax.axis_size(axis), shard.shape[dim])
        up = [(i, (i + 1) % devices) for i in range(devices)]
        down = [(j, i) for i, j in up]
        last = lax.slice_in_dim(shard, length - width, length, axis=dim)
        initial = lax.slice_in_dim(shard, 0, width, axis=dim)
        before = lax.ppermute(last, axis, up)
        after = lax.ppermute(initial, axis, down)
        shard = jnp.concatenate([before, shard, after], axis=dim)
    return shard


def gelu_slope(preact):
    normal_cdf = 0.5 * (1.0 + jax.scipy.special.erf(preact * 0.7071067811865476))
    density = jnp.exp(-0.5 * preact * preact) * 0.3989422804014327
    return normal_cdf + preact * density


def mask_rims(padded):
    lat_index = lax.axis_index("lat")
    band_count = lax.axis_size("lat")
    row_ids = jnp.arange(padded.shape[1])
    outside = (row_ids == 0) & (lat_index == 0) | (row_ids == padded.shape[1] - 1) & (
        lat_index == band_count - 1
    )
    return jnp.where(outside[None, :, None], jnp.zeros((), padded.dtype), padded)


def window_of(field, first_row, first_col, row_count, column_count):
    return field[
        :, first_row : first_row + row_count, first_col : first_col + column_count
    ].reshape(field.shape[0], -1)


def conv_taps(kernel, field, row_count, column_count, flip):
    total = None
    for tap_row in range(3):
        for tap_col in range(3):
            if flip:
                window = window_of(field, 2 - tap_row, 2 - tap_col, row_count, column_count)
            else:
                window = window_of(field, tap_row, tap_col, row_count, column_count)
            part = jnp.dot(kernel[tap_row, tap_col], window, preferred_element_type=jnp.float32)
            total = part if total is None else total + part
    return total


def direct_reduce_scatter(rows, axis, send_dtype):
    count, index = lax.axis_size(axis), lax.axis_index(axis)
    if count == 1:
        return rows
    chunks = rows.reshape(count, -1, rows.shape[-1])
    acc = lax.dynamic_index_in_dim(chunks, index, keepdims=False)
    for step in range(1, count):
        pairs = [(j, (j + step) % count) for j in range(count)]
        piece = lax.dynamic_index_in_dim(chunks, (index + step) % count, keepdims=False)
        acc = acc + lax.ppermute(piece.astype(send_dtype), axis, pairs).astype(jnp.float32)
    return acc


def direct_all_gather(chunk, axis, send_dtype):
    count, index = lax.axis_size(axis), lax.axis_index(axis)
    if count == 1:
        return chunk
    pieces = [chunk]
    sent = chunk.astype(send_dtype)
    for step in range(1, count):
        pairs = [(j, (j + step) % count) for j in range(count)]
        pieces.append(lax.ppermute(sent, axis, pairs).astype(jnp.float32))
    stacked = jnp.stack(pieces[::-1])
    stacked = jnp.roll(stacked, (index + 1) % count, axis=0)
    return stacked.reshape(-1, chunk.shape[-1])


def sum_start(flat, send_dtype, columns):
    parts = lax.axis_size("lat") * lax.axis_size("lon")
    quantum = parts * 16 * 128
    padded = jnp.pad(flat, (0, (-flat.size) % quantum)).reshape(-1, 128)
    rows = direct_reduce_scatter(padded, "lat", send_dtype)
    count, index = lax.axis_size("lon"), lax.axis_index("lon")
    last, first = columns
    if count < 3:
        up = [(i, (i + 1) % count) for i in range(count)]
        down = [(j, i) for i, j in up]
        halo = (lax.ppermute(last, "lon", up), lax.ppermute(first, "lon", down))
        return direct_reduce_scatter(rows, "lon", send_dtype), halo
    chunks = rows.reshape(count, -1, rows.shape[-1])
    size = chunks.shape[1]
    acc = lax.dynamic_index_in_dim(chunks, index, keepdims=False)
    extra = {1: last, count - 1: first}
    got = {}
    for step in range(1, count):
        pairs = [(j, (j + step) % count) for j in range(count)]
        piece = lax.dynamic_index_in_dim(chunks, (index + step) % count, keepdims=False).astype(send_dtype)
        if step in extra:
            piece = jnp.concatenate([piece, extra[step].astype(send_dtype).reshape(-1, rows.shape[-1])], axis=0)
        moved = lax.ppermute(piece, "lon", pairs)
        acc = acc + moved[:size].astype(jnp.float32)
        if step in extra:
            got[step] = moved[size:].reshape(last.shape).astype(last.dtype)
    return acc, (got[1], got[count - 1])


def sum_finish(rows, size, send_dtype):
    rows = direct_all_gather(rows, "lon", send_dtype)
    rows = direct_all_gather(rows, "lat", send_dtype)
    return rows.reshape(-1)[:size]


def border_of(padded):
    rows, cols = padded.shape[1], padded.shape[2]
    return jnp.concatenate(
        [padded[:, 0, :], padded[:, rows - 1, :], padded[:, 1 : rows - 1, 0], padded[:, 1 : rows - 1, cols - 1]],
        axis=1,
    )


def with_border(field, border):
    rows, cols = field.shape[1], field.shape[2]
    top = border[:, : cols + 2]
    bottom = border[:, cols + 2 : 2 * cols + 4]
    left = border[:, 2 * cols + 4 : 2 * cols + 4 + rows]
    right = border[:, 2 * cols + 4 + rows :]
    middle = jnp.concatenate([left[:, :, None], field, right[:, :, None]], axis=2)
    return jnp.concatenate([top[:, None, :], middle, bottom[:, None, :]], axis=1)


def local(inputs, cotangent, weight, bias_vector):
    own_channels, row_count, column_count = inputs.shape
    chan_count = lax.axis_size("chan")
    chan_index = lax.axis_index("chan")
    raw_blocks = []
    for shift in range(1, chan_count):
        pairs = [(i, (i - shift) % chan_count) for i in range(chan_count)]
        raw_blocks.append(lax.ppermute(inputs, "chan", pairs))
    input_pad = mask_rims(padded_2(inputs, (("lon", 2), ("lat", 1)), 1))
    own_border = border_of(input_pad)
    blocks = [input_pad]
    for shift in range(1, chan_count):
        pairs = [(i, (i - shift) % chan_count) for i in range(chan_count)]
        border = lax.ppermute(own_border, "chan", pairs)
        blocks.append(lax.optimization_barrier(with_border(raw_blocks[shift - 1], border)))
    kernel_cols = []
    for shift in range(chan_count):
        source = (chan_index + shift) % chan_count
        kernel_cols.append(
            lax.dynamic_slice_in_dim(weight, source * own_channels, own_channels, axis=3)
        )
    preact = None
    for shift in range(chan_count):
        part = conv_taps(kernel_cols[shift], blocks[shift], row_count, column_count, False)
        preact = part if preact is None else preact + part
    preact = preact + bias_vector[:, None]
    upstream = cotangent.reshape(own_channels, -1).astype(jnp.float32)
    grad_pre = (upstream * gelu_slope(preact)).astype(jnp.bfloat16)
    bias_part = jnp.sum(grad_pre.astype(jnp.float32), axis=1)
    input_local = jnp.concatenate(blocks, axis=0)
    taps = []
    for tap_row in range(3):
        row_taps = []
        for tap_col in range(3):
            window = window_of(input_local, tap_row, tap_col, row_count, column_count)
            row_taps.append(
                lax.dot_general(
                    grad_pre, window, (((1,), (1,)), ((), ())), preferred_element_type=jnp.float32
                )
            )
        taps.append(jnp.stack(row_taps))
    weight_part = jnp.stack(taps)
    flat = jnp.concatenate([weight_part.reshape(-1), bias_part])
    grad_field = grad_pre.reshape(own_channels, row_count, column_count)
    edges = (grad_field[:, :, column_count - 1 :], grad_field[:, :, :1])
    scattered, (before, after) = sum_start(flat, jnp.bfloat16, edges)
    flat = sum_finish(scattered, flat.size, jnp.bfloat16)
    weight_local = flat[: weight_part.size].reshape(weight_part.shape)
    bias_grad = flat[weight_part.size :]
    doubled = jnp.concatenate([weight_local, weight_local], axis=3)
    weight_grad = lax.dynamic_slice_in_dim(
        doubled, (chan_count - chan_index) % chan_count * own_channels, chan_count * own_channels, axis=3
    )
    grad_wide = jnp.concatenate([before, grad_field, after], axis=2)
    grad_pad = mask_rims(padded_2(grad_wide, (("lat", 1),), 1))
    outgoing = []
    for shift in range(1, chan_count):
        kernel_t = jnp.swapaxes(kernel_cols[shift], 2, 3)
        outgoing.append(conv_taps(kernel_t, grad_pad, row_count, column_count, True).astype(jnp.bfloat16))
    grad_pad, outgoing = lax.optimization_barrier((grad_pad, outgoing))
    received = []
    for shift in range(1, chan_count):
        pairs = [(i, (i + shift) % chan_count) for i in range(chan_count)]
        received.append(lax.ppermute(outgoing[shift - 1], "chan", pairs))
    own_part = conv_taps(jnp.swapaxes(kernel_cols[0], 2, 3), grad_pad, row_count, column_count, True)
    own_part, weight_grad, bias_grad = lax.optimization_barrier((own_part, weight_grad, bias_grad))
    for piece in received:
        own_part = own_part + piece.astype(jnp.float32)
    input_grad = own_part.astype(jnp.bfloat16).reshape(own_channels, row_count, column_count)
    return (input_grad, weight_grad, bias_grad)


def solution(mesh):
    placed = (
        P("chan", ("groups", "lat"), "lon"),
        P("chan", ("groups", "lat"), "lon"),
        P(None, None, "chan", None),
        P("chan"),
    )
    return jax.shard_map(
        local,
        mesh=mesh,
        in_specs=placed,
        out_specs=(
            P("chan", ("groups", "lat"), "lon"),
            P("groups", None, "chan", None),
            P(("groups", "chan")),
        ),
        check_vma=False,
    )
```

```python
import jax
import jax.numpy as jnp
from jax import lax
from jax.sharding import PartitionSpec as P


def padded_2(shard, sides, width):
    for axis, dim in sides:
        devices, length = (lax.axis_size(axis), shard.shape[dim])
        up = [(i, (i + 1) % devices) for i in range(devices)]
        down = [(j, i) for i, j in up]
        last = lax.slice_in_dim(shard, length - width, length, axis=dim)
        initial = lax.slice_in_dim(shard, 0, width, axis=dim)
        before = lax.ppermute(last, axis, up)
        after = lax.ppermute(initial, axis, down)
        shard = jnp.concatenate([before, shard, after], axis=dim)
    return shard


def gelu_slope(preact):
    normal_cdf = 0.5 * (1.0 + jax.scipy.special.erf(preact * 0.7071067811865476))
    density = jnp.exp(-0.5 * preact * preact) * 0.3989422804014327
    return normal_cdf + preact * density


def mask_rims(padded):
    lat_index = lax.axis_index("lat")
    band_count = lax.axis_size("lat")
    row_ids = jnp.arange(padded.shape[1])
    outside = (row_ids == 0) & (lat_index == 0) | (row_ids == padded.shape[1] - 1) & (
        lat_index == band_count - 1
    )
    return jnp.where(outside[None, :, None], jnp.zeros((), padded.dtype), padded)


def window_of(field, first_row, first_col, row_count, column_count):
    return field[
        :, first_row : first_row + row_count, first_col : first_col + column_count
    ].reshape(field.shape[0], -1)


def conv_taps(kernel, field, row_count, column_count, flip):
    total = None
    for tap_row in range(3):
        for tap_col in range(3):
            if flip:
                window = window_of(field, 2 - tap_row, 2 - tap_col, row_count, column_count)
            else:
                window = window_of(field, tap_row, tap_col, row_count, column_count)
            part = jnp.dot(kernel[tap_row, tap_col], window, preferred_element_type=jnp.float32)
            total = part if total is None else total + part
    return total


def direct_reduce_scatter(rows, axis, send_dtype):
    count, index = lax.axis_size(axis), lax.axis_index(axis)
    if count == 1:
        return rows
    chunks = rows.reshape(count, -1, rows.shape[-1])
    acc = lax.dynamic_index_in_dim(chunks, index, keepdims=False)
    for step in range(1, count):
        pairs = [(j, (j + step) % count) for j in range(count)]
        piece = lax.dynamic_index_in_dim(chunks, (index + step) % count, keepdims=False)
        acc = acc + lax.ppermute(piece.astype(send_dtype), axis, pairs).astype(jnp.float32)
    return acc


def direct_all_gather(chunk, axis, send_dtype):
    count, index = lax.axis_size(axis), lax.axis_index(axis)
    if count == 1:
        return chunk
    pieces = [chunk]
    sent = chunk.astype(send_dtype)
    for step in range(1, count):
        pairs = [(j, (j + step) % count) for j in range(count)]
        pieces.append(lax.ppermute(sent, axis, pairs).astype(jnp.float32))
    stacked = jnp.stack(pieces[::-1])
    stacked = jnp.roll(stacked, (index + 1) % count, axis=0)
    return stacked.reshape(-1, chunk.shape[-1])


def sum_start(flat, send_dtype, columns):
    parts = lax.axis_size("lat") * lax.axis_size("lon")
    quantum = parts * 16 * 128
    padded = jnp.pad(flat, (0, (-flat.size) % quantum)).reshape(-1, 128)
    rows = direct_reduce_scatter(padded, "lat", jnp.float32)
    count, index = lax.axis_size("lon"), lax.axis_index("lon")
    last, first = columns
    if count < 3:
        up = [(i, (i + 1) % count) for i in range(count)]
        down = [(j, i) for i, j in up]
        halo = (lax.ppermute(last, "lon", up), lax.ppermute(first, "lon", down))
        return direct_reduce_scatter(rows, "lon", send_dtype), halo
    chunks = rows.reshape(count, -1, rows.shape[-1])
    size = chunks.shape[1]
    acc = lax.dynamic_index_in_dim(chunks, index, keepdims=False)
    extra = {1: last, count - 1: first}
    got = {}
    for step in range(1, count):
        pairs = [(j, (j + step) % count) for j in range(count)]
        piece = lax.dynamic_index_in_dim(chunks, (index + step) % count, keepdims=False).astype(send_dtype)
        if step in extra:
            piece = jnp.concatenate([piece, extra[step].astype(send_dtype).reshape(-1, rows.shape[-1])], axis=0)
        moved = lax.ppermute(piece, "lon", pairs)
        acc = acc + moved[:size].astype(jnp.float32)
        if step in extra:
            got[step] = moved[size:].reshape(last.shape).astype(last.dtype)
    return acc, (got[1], got[count - 1])


def sum_finish(rows, size, send_dtype):
    rows = direct_all_gather(rows, "lon", send_dtype)
    rows = direct_all_gather(rows, "lat", jnp.float32)
    return rows.reshape(-1)[:size]


def border_of(padded):
    rows, cols = padded.shape[1], padded.shape[2]
    return jnp.concatenate(
        [padded[:, 0, :], padded[:, rows - 1, :], padded[:, 1 : rows - 1, 0], padded[:, 1 : rows - 1, cols - 1]],
        axis=1,
    )


def with_border(field, border):
    rows, cols = field.shape[1], field.shape[2]
    top = border[:, : cols + 2]
    bottom = border[:, cols + 2 : 2 * cols + 4]
    left = border[:, 2 * cols + 4 : 2 * cols + 4 + rows]
    right = border[:, 2 * cols + 4 + rows :]
    middle = jnp.concatenate([left[:, :, None], field, right[:, :, None]], axis=2)
    return jnp.concatenate([top[:, None, :], middle, bottom[:, None, :]], axis=1)


def local(inputs, cotangent, weight, bias_vector):
    own_channels, row_count, column_count = inputs.shape
    chan_count = lax.axis_size("chan")
    chan_index = lax.axis_index("chan")
    raw_blocks = []
    for shift in range(1, chan_count):
        pairs = [(i, (i - shift) % chan_count) for i in range(chan_count)]
        raw_blocks.append(lax.ppermute(inputs, "chan", pairs))
    input_pad = mask_rims(padded_2(inputs, (("lon", 2), ("lat", 1)), 1))
    own_border = border_of(input_pad)
    blocks = [input_pad]
    for shift in range(1, chan_count):
        pairs = [(i, (i - shift) % chan_count) for i in range(chan_count)]
        border = lax.ppermute(own_border, "chan", pairs)
        blocks.append(lax.optimization_barrier(with_border(raw_blocks[shift - 1], border)))
    kernel_cols = []
    for shift in range(chan_count):
        source = (chan_index + shift) % chan_count
        kernel_cols.append(
            lax.dynamic_slice_in_dim(weight, source * own_channels, own_channels, axis=3)
        )
    preact = None
    for shift in range(chan_count):
        part = conv_taps(kernel_cols[shift], blocks[shift], row_count, column_count, False)
        preact = part if preact is None else preact + part
    preact = preact + bias_vector[:, None]
    upstream = cotangent.reshape(own_channels, -1).astype(jnp.float32)
    grad_pre = (upstream * gelu_slope(preact)).astype(jnp.bfloat16)
    bias_part = jnp.sum(grad_pre.astype(jnp.float32), axis=1)
    input_local = jnp.concatenate(blocks, axis=0)
    taps = []
    for tap_row in range(3):
        row_taps = []
        for tap_col in range(3):
            window = window_of(input_local, tap_row, tap_col, row_count, column_count)
            row_taps.append(
                lax.dot_general(
                    grad_pre, window, (((1,), (1,)), ((), ())), preferred_element_type=jnp.float32
                )
            )
        taps.append(jnp.stack(row_taps))
    weight_part = jnp.stack(taps)
    flat = jnp.concatenate([weight_part.reshape(-1), bias_part])
    grad_field = grad_pre.reshape(own_channels, row_count, column_count)
    edges = (grad_field[:, :, column_count - 1 :], grad_field[:, :, :1])
    scattered, (before, after) = sum_start(flat, jnp.float32, edges)
    flat = sum_finish(scattered, flat.size, jnp.bfloat16)
    weight_local = flat[: weight_part.size].reshape(weight_part.shape)
    bias_grad = flat[weight_part.size :]
    doubled = jnp.concatenate([weight_local, weight_local], axis=3)
    weight_grad = lax.dynamic_slice_in_dim(
        doubled, (chan_count - chan_index) % chan_count * own_channels, chan_count * own_channels, axis=3
    )
    grad_wide = jnp.concatenate([before, grad_field, after], axis=2)
    grad_pad = mask_rims(padded_2(grad_wide, (("lat", 1),), 1))
    outgoing = []
    for shift in range(1, chan_count):
        kernel_t = jnp.swapaxes(kernel_cols[shift], 2, 3)
        outgoing.append(conv_taps(kernel_t, grad_pad, row_count, column_count, True).astype(jnp.bfloat16))
    grad_pad, outgoing = lax.optimization_barrier((grad_pad, outgoing))
    received = []
    for shift in range(1, chan_count):
        pairs = [(i, (i + shift) % chan_count) for i in range(chan_count)]
        received.append(lax.ppermute(outgoing[shift - 1], "chan", pairs))
    own_part = conv_taps(jnp.swapaxes(kernel_cols[0], 2, 3), grad_pad, row_count, column_count, True)
    own_part, weight_grad, bias_grad = lax.optimization_barrier((own_part, weight_grad, bias_grad))
    for piece in received:
        own_part = own_part + piece.astype(jnp.float32)
    input_grad = own_part.astype(jnp.bfloat16).reshape(own_channels, row_count, column_count)
    return (input_grad, weight_grad, bias_grad)


def solution(mesh):
    placed = (
        P("chan", ("groups", "lat"), "lon"),
        P("chan", ("groups", "lat"), "lon"),
        P(None, None, "chan", None),
        P("chan"),
    )
    return jax.shard_map(
        local,
        mesh=mesh,
        in_specs=placed,
        out_specs=(
            P("chan", ("groups", "lat"), "lon"),
            P("groups", None, "chan", None),
            P(("groups", "chan")),
        ),
        check_vma=False,
    )
```

```python
import jax
import jax.numpy as jnp
from jax import lax
from jax.sharding import PartitionSpec as P


def padded_2(shard, sides, width):
    for axis, dim in sides:
        devices, length = (lax.axis_size(axis), shard.shape[dim])
        up = [(i, (i + 1) % devices) for i in range(devices)]
        down = [(j, i) for i, j in up]
        last = lax.slice_in_dim(shard, length - width, length, axis=dim)
        initial = lax.slice_in_dim(shard, 0, width, axis=dim)
        before = lax.ppermute(last, axis, up)
        after = lax.ppermute(initial, axis, down)
        shard = jnp.concatenate([before, shard, after], axis=dim)
    return shard


def gelu_slope(preact):
    normal_cdf = 0.5 * (1.0 + jax.scipy.special.erf(preact * 0.7071067811865476))
    density = jnp.exp(-0.5 * preact * preact) * 0.3989422804014327
    return normal_cdf + preact * density


def mask_rims(padded):
    lat_index = lax.axis_index("lat")
    band_count = lax.axis_size("lat")
    row_ids = jnp.arange(padded.shape[1])
    outside = (row_ids == 0) & (lat_index == 0) | (row_ids == padded.shape[1] - 1) & (
        lat_index == band_count - 1
    )
    return jnp.where(outside[None, :, None], jnp.zeros((), padded.dtype), padded)


def window_of(field, first_row, first_col, row_count, column_count):
    return field[
        :, first_row : first_row + row_count, first_col : first_col + column_count
    ].reshape(field.shape[0], -1)


def conv_taps(kernel, field, row_count, column_count, flip):
    total = None
    for tap_row in range(3):
        for tap_col in range(3):
            if flip:
                window = window_of(field, 2 - tap_row, 2 - tap_col, row_count, column_count)
            else:
                window = window_of(field, tap_row, tap_col, row_count, column_count)
            part = jnp.dot(kernel[tap_row, tap_col], window, preferred_element_type=jnp.float32)
            total = part if total is None else total + part
    return total


def direct_reduce_scatter(rows, axis, send_dtype):
    count, index = lax.axis_size(axis), lax.axis_index(axis)
    if count == 1:
        return rows
    chunks = rows.reshape(count, -1, rows.shape[-1])
    acc = lax.dynamic_index_in_dim(chunks, index, keepdims=False)
    for step in range(1, count):
        pairs = [(j, (j + step) % count) for j in range(count)]
        piece = lax.dynamic_index_in_dim(chunks, (index + step) % count, keepdims=False)
        acc = acc + lax.ppermute(piece.astype(send_dtype), axis, pairs).astype(jnp.float32)
    return acc


def direct_all_gather(chunk, axis, send_dtype):
    count, index = lax.axis_size(axis), lax.axis_index(axis)
    if count == 1:
        return chunk
    pieces = [chunk]
    sent = chunk.astype(send_dtype)
    for step in range(1, count):
        pairs = [(j, (j + step) % count) for j in range(count)]
        pieces.append(lax.ppermute(sent, axis, pairs).astype(jnp.float32))
    stacked = jnp.stack(pieces[::-1])
    stacked = jnp.roll(stacked, (index + 1) % count, axis=0)
    return stacked.reshape(-1, chunk.shape[-1])


def sum_start(flat, send_dtype, columns):
    parts = lax.axis_size("lat") * lax.axis_size("lon")
    quantum = parts * 16 * 128
    padded = jnp.pad(flat, (0, (-flat.size) % quantum)).reshape(-1, 128)
    rows = direct_reduce_scatter(padded, "lat", jnp.float32)
    count, index = lax.axis_size("lon"), lax.axis_index("lon")
    last, first = columns
    if count < 3:
        up = [(i, (i + 1) % count) for i in range(count)]
        down = [(j, i) for i, j in up]
        halo = (lax.ppermute(last, "lon", up), lax.ppermute(first, "lon", down))
        return direct_reduce_scatter(rows, "lon", send_dtype), halo
    chunks = rows.reshape(count, -1, rows.shape[-1])
    size = chunks.shape[1]
    acc = lax.dynamic_index_in_dim(chunks, index, keepdims=False)
    extra = {1: last, count - 1: first}
    got = {}
    for step in range(1, count):
        pairs = [(j, (j + step) % count) for j in range(count)]
        piece = lax.dynamic_index_in_dim(chunks, (index + step) % count, keepdims=False).astype(send_dtype)
        if step in extra:
            piece = jnp.concatenate([piece, extra[step].astype(send_dtype).reshape(-1, rows.shape[-1])], axis=0)
        moved = lax.ppermute(piece, "lon", pairs)
        acc = acc + moved[:size].astype(jnp.float32)
        if step in extra:
            got[step] = moved[size:].reshape(last.shape).astype(last.dtype)
    return acc, (got[1], got[count - 1])


def sum_finish(rows, size, send_dtype):
    rows = direct_all_gather(rows, "lon", send_dtype)
    rows = direct_all_gather(rows, "lat", jnp.float32)
    return rows.reshape(-1)[:size]


def border_of(padded):
    rows, cols = padded.shape[1], padded.shape[2]
    return jnp.concatenate(
        [padded[:, 0, :], padded[:, rows - 1, :], padded[:, 1 : rows - 1, 0], padded[:, 1 : rows - 1, cols - 1]],
        axis=1,
    )


def with_border(field, border):
    rows, cols = field.shape[1], field.shape[2]
    top = border[:, : cols + 2]
    bottom = border[:, cols + 2 : 2 * cols + 4]
    left = border[:, 2 * cols + 4 : 2 * cols + 4 + rows]
    right = border[:, 2 * cols + 4 + rows :]
    middle = jnp.concatenate([left[:, :, None], field, right[:, :, None]], axis=2)
    return jnp.concatenate([top[:, None, :], middle, bottom[:, None, :]], axis=1)


def local(inputs, cotangent, weight, bias_vector):
    own_channels, row_count, column_count = inputs.shape
    chan_count = lax.axis_size("chan")
    chan_index = lax.axis_index("chan")
    raw_blocks = []
    for shift in range(1, chan_count):
        pairs = [(i, (i - shift) % chan_count) for i in range(chan_count)]
        raw_blocks.append(lax.ppermute(inputs, "chan", pairs))
    input_pad = mask_rims(padded_2(inputs, (("lon", 2), ("lat", 1)), 1))
    own_border = border_of(input_pad)
    blocks = [input_pad]
    for shift in range(1, chan_count):
        pairs = [(i, (i - shift) % chan_count) for i in range(chan_count)]
        border = lax.ppermute(own_border, "chan", pairs)
        blocks.append(with_border(raw_blocks[shift - 1], border))
    kernel_cols = []
    for shift in range(chan_count):
        source = (chan_index + shift) % chan_count
        kernel_cols.append(
            lax.dynamic_slice_in_dim(weight, source * own_channels, own_channels, axis=3)
        )
    preact = None
    for shift in range(chan_count):
        part = conv_taps(kernel_cols[shift], blocks[shift], row_count, column_count, False)
        preact = part if preact is None else preact + part
    preact = preact + bias_vector[:, None]
    upstream = cotangent.reshape(own_channels, -1).astype(jnp.float32)
    grad_pre = (upstream * gelu_slope(preact)).astype(jnp.bfloat16)
    bias_part = jnp.sum(grad_pre.astype(jnp.float32), axis=1)
    input_local = jnp.concatenate(blocks, axis=0)
    taps = []
    for tap_row in range(3):
        row_taps = []
        for tap_col in range(3):
            window = window_of(input_local, tap_row, tap_col, row_count, column_count)
            row_taps.append(
                lax.dot_general(
                    grad_pre, window, (((1,), (1,)), ((), ())), preferred_element_type=jnp.float32
                )
            )
        taps.append(jnp.stack(row_taps))
    weight_part = jnp.stack(taps)
    flat = jnp.concatenate([weight_part.reshape(-1), bias_part])
    grad_field = grad_pre.reshape(own_channels, row_count, column_count)
    edges = (grad_field[:, :, column_count - 1 :], grad_field[:, :, :1])
    scattered, (before, after) = sum_start(flat, jnp.bfloat16, edges)
    flat = sum_finish(scattered, flat.size, jnp.bfloat16)
    weight_local = flat[: weight_part.size].reshape(weight_part.shape)
    bias_grad = flat[weight_part.size :]
    doubled = jnp.concatenate([weight_local, weight_local], axis=3)
    weight_grad = lax.dynamic_slice_in_dim(
        doubled, (chan_count - chan_index) % chan_count * own_channels, chan_count * own_channels, axis=3
    )
    grad_wide = jnp.concatenate([before, grad_field, after], axis=2)
    grad_pad = mask_rims(padded_2(grad_wide, (("lat", 1),), 1))
    outgoing = []
    for shift in range(1, chan_count):
        kernel_t = jnp.swapaxes(kernel_cols[shift], 2, 3)
        outgoing.append(conv_taps(kernel_t, grad_pad, row_count, column_count, True).astype(jnp.bfloat16))
    grad_pad, outgoing = lax.optimization_barrier((grad_pad, outgoing))
    received = []
    for shift in range(1, chan_count):
        pairs = [(i, (i + shift) % chan_count) for i in range(chan_count)]
        received.append(lax.ppermute(outgoing[shift - 1], "chan", pairs))
    own_part = conv_taps(jnp.swapaxes(kernel_cols[0], 2, 3), grad_pad, row_count, column_count, True)
    own_part, weight_grad, bias_grad = lax.optimization_barrier((own_part, weight_grad, bias_grad))
    for piece in received:
        own_part = own_part + piece.astype(jnp.float32)
    input_grad = own_part.astype(jnp.bfloat16).reshape(own_channels, row_count, column_count)
    return (input_grad, weight_grad, bias_grad)


def solution(mesh):
    placed = (
        P("chan", ("groups", "lat"), "lon"),
        P("chan", ("groups", "lat"), "lon"),
        P(None, None, "chan", None),
        P("chan"),
    )
    return jax.shard_map(
        local,
        mesh=mesh,
        in_specs=placed,
        out_specs=(
            P("chan", ("groups", "lat"), "lon"),
            P("groups", None, "chan", None),
            P(("groups", "chan")),
        ),
        check_vma=False,
    )
```

```python
import jax
import jax.numpy as jnp
from jax import lax
from jax.sharding import PartitionSpec as P


def padded_2(shard, sides, width):
    for axis, dim in sides:
        devices, length = (lax.axis_size(axis), shard.shape[dim])
        up = [(i, (i + 1) % devices) for i in range(devices)]
        down = [(j, i) for i, j in up]
        last = lax.slice_in_dim(shard, length - width, length, axis=dim)
        initial = lax.slice_in_dim(shard, 0, width, axis=dim)
        before = lax.ppermute(last, axis, up)
        after = lax.ppermute(initial, axis, down)
        shard = jnp.concatenate([before, shard, after], axis=dim)
    return shard


def gelu_slope(preact):
    normal_cdf = 0.5 * (1.0 + jax.scipy.special.erf(preact * 0.7071067811865476))
    density = jnp.exp(-0.5 * preact * preact) * 0.3989422804014327
    return normal_cdf + preact * density


def mask_rims(padded):
    lat_index = lax.axis_index("lat")
    band_count = lax.axis_size("lat")
    row_ids = jnp.arange(padded.shape[1])
    outside = (row_ids == 0) & (lat_index == 0) | (row_ids == padded.shape[1] - 1) & (
        lat_index == band_count - 1
    )
    return jnp.where(outside[None, :, None], jnp.zeros((), padded.dtype), padded)


def window_of(field, first_row, first_col, row_count, column_count):
    return field[
        :, first_row : first_row + row_count, first_col : first_col + column_count
    ].reshape(field.shape[0], -1)


def conv_taps(kernel, field, row_count, column_count, flip):
    total = None
    for tap_row in range(3):
        for tap_col in range(3):
            if flip:
                window = window_of(field, 2 - tap_row, 2 - tap_col, row_count, column_count)
            else:
                window = window_of(field, tap_row, tap_col, row_count, column_count)
            part = jnp.dot(kernel[tap_row, tap_col], window, preferred_element_type=jnp.float32)
            total = part if total is None else total + part
    return total


def direct_reduce_scatter(rows, axis, send_dtype):
    count, index = lax.axis_size(axis), lax.axis_index(axis)
    if count == 1:
        return rows
    chunks = rows.reshape(count, -1, rows.shape[-1])
    acc = lax.dynamic_index_in_dim(chunks, index, keepdims=False)
    for step in range(1, count):
        pairs = [(j, (j + step) % count) for j in range(count)]
        piece = lax.dynamic_index_in_dim(chunks, (index + step) % count, keepdims=False)
        acc = acc + lax.ppermute(piece.astype(send_dtype), axis, pairs).astype(jnp.float32)
    return acc


def direct_all_gather(chunk, axis, send_dtype):
    count, index = lax.axis_size(axis), lax.axis_index(axis)
    if count == 1:
        return chunk
    pieces = [chunk]
    sent = chunk.astype(send_dtype)
    for step in range(1, count):
        pairs = [(j, (j + step) % count) for j in range(count)]
        pieces.append(lax.ppermute(sent, axis, pairs).astype(jnp.float32))
    stacked = jnp.stack(pieces[::-1])
    stacked = jnp.roll(stacked, (index + 1) % count, axis=0)
    return stacked.reshape(-1, chunk.shape[-1])


def sum_start(flat, send_dtype, columns):
    parts = lax.axis_size("lat") * lax.axis_size("lon")
    quantum = parts * 16 * 128
    padded = jnp.pad(flat, (0, (-flat.size) % quantum)).reshape(-1, 128)
    rows = direct_reduce_scatter(padded, "lat", jnp.float32)
    count, index = lax.axis_size("lon"), lax.axis_index("lon")
    last, first = columns
    if count < 3:
        up = [(i, (i + 1) % count) for i in range(count)]
        down = [(j, i) for i, j in up]
        halo = (lax.ppermute(last, "lon", up), lax.ppermute(first, "lon", down))
        return direct_reduce_scatter(rows, "lon", send_dtype), halo
    chunks = rows.reshape(count, -1, rows.shape[-1])
    size = chunks.shape[1]
    acc = lax.dynamic_index_in_dim(chunks, index, keepdims=False)
    extra = {1: last, count - 1: first}
    got = {}
    for step in range(1, count):
        pairs = [(j, (j + step) % count) for j in range(count)]
        piece = lax.dynamic_index_in_dim(chunks, (index + step) % count, keepdims=False).astype(send_dtype)
        if step in extra:
            piece = jnp.concatenate([piece, extra[step].astype(send_dtype).reshape(-1, rows.shape[-1])], axis=0)
        moved = lax.ppermute(piece, "lon", pairs)
        acc = acc + moved[:size].astype(jnp.float32)
        if step in extra:
            got[step] = moved[size:].reshape(last.shape).astype(last.dtype)
    return acc, (got[1], got[count - 1])


def sum_finish(rows, size, send_dtype):
    rows = direct_all_gather(rows, "lon", send_dtype)
    rows = direct_all_gather(rows, "lat", jnp.float32)
    return rows.reshape(-1)[:size]


def border_of(padded):
    rows, cols = padded.shape[1], padded.shape[2]
    return jnp.concatenate(
        [padded[:, 0, :], padded[:, rows - 1, :], padded[:, 1 : rows - 1, 0], padded[:, 1 : rows - 1, cols - 1]],
        axis=1,
    )


def with_border(field, border):
    rows, cols = field.shape[1], field.shape[2]
    top = border[:, : cols + 2]
    bottom = border[:, cols + 2 : 2 * cols + 4]
    left = border[:, 2 * cols + 4 : 2 * cols + 4 + rows]
    right = border[:, 2 * cols + 4 + rows :]
    middle = jnp.concatenate([left[:, :, None], field, right[:, :, None]], axis=2)
    return jnp.concatenate([top[:, None, :], middle, bottom[:, None, :]], axis=1)


def local(inputs, cotangent, weight, bias_vector):
    own_channels, row_count, column_count = inputs.shape
    chan_count = lax.axis_size("chan")
    chan_index = lax.axis_index("chan")
    raw_blocks = []
    for shift in range(1, chan_count):
        pairs = [(i, (i - shift) % chan_count) for i in range(chan_count)]
        raw_blocks.append(lax.ppermute(inputs, "chan", pairs))
    input_pad = mask_rims(padded_2(inputs, (("lon", 2), ("lat", 1)), 1))
    own_border = border_of(input_pad)
    blocks = [input_pad]
    for shift in range(1, chan_count):
        pairs = [(i, (i - shift) % chan_count) for i in range(chan_count)]
        border = lax.ppermute(own_border, "chan", pairs)
        blocks.append(lax.optimization_barrier(with_border(raw_blocks[shift - 1], border)))
    kernel_cols = []
    for shift in range(chan_count):
        source = (chan_index + shift) % chan_count
        kernel_cols.append(
            lax.dynamic_slice_in_dim(weight, source * own_channels, own_channels, axis=3)
        )
    preact = None
    for shift in range(chan_count):
        part = conv_taps(kernel_cols[shift], blocks[shift], row_count, column_count, False)
        preact = part if preact is None else preact + part
    preact = preact + bias_vector[:, None]
    upstream = cotangent.reshape(own_channels, -1).astype(jnp.float32)
    grad_pre = (upstream * gelu_slope(preact)).astype(jnp.bfloat16)
    bias_part = jnp.sum(grad_pre.astype(jnp.float32), axis=1)
    input_local = lax.optimization_barrier(jnp.concatenate(blocks, axis=0))
    taps = []
    for tap_row in range(3):
        row_taps = []
        for tap_col in range(3):
            window = window_of(input_local, tap_row, tap_col, row_count, column_count)
            row_taps.append(
                lax.dot_general(
                    grad_pre, window, (((1,), (1,)), ((), ())), preferred_element_type=jnp.float32
                )
            )
        taps.append(jnp.stack(row_taps))
    weight_part = jnp.stack(taps)
    flat = jnp.concatenate([weight_part.reshape(-1), bias_part])
    grad_field = grad_pre.reshape(own_channels, row_count, column_count)
    edges = (grad_field[:, :, column_count - 1 :], grad_field[:, :, :1])
    scattered, (before, after) = sum_start(flat, jnp.bfloat16, edges)
    flat = sum_finish(scattered, flat.size, jnp.bfloat16)
    weight_local = flat[: weight_part.size].reshape(weight_part.shape)
    bias_grad = flat[weight_part.size :]
    doubled = jnp.concatenate([weight_local, weight_local], axis=3)
    weight_grad = lax.dynamic_slice_in_dim(
        doubled, (chan_count - chan_index) % chan_count * own_channels, chan_count * own_channels, axis=3
    )
    grad_wide = jnp.concatenate([before, grad_field, after], axis=2)
    grad_pad = mask_rims(padded_2(grad_wide, (("lat", 1),), 1))
    outgoing = []
    for shift in range(1, chan_count):
        kernel_t = jnp.swapaxes(kernel_cols[shift], 2, 3)
        outgoing.append(conv_taps(kernel_t, grad_pad, row_count, column_count, True).astype(jnp.bfloat16))
    grad_pad, outgoing = lax.optimization_barrier((grad_pad, outgoing))
    received = []
    for shift in range(1, chan_count):
        pairs = [(i, (i + shift) % chan_count) for i in range(chan_count)]
        received.append(lax.ppermute(outgoing[shift - 1], "chan", pairs))
    own_part = conv_taps(jnp.swapaxes(kernel_cols[0], 2, 3), grad_pad, row_count, column_count, True)
    own_part, weight_grad, bias_grad = lax.optimization_barrier((own_part, weight_grad, bias_grad))
    for piece in received:
        own_part = own_part + piece.astype(jnp.float32)
    input_grad = own_part.astype(jnp.bfloat16).reshape(own_channels, row_count, column_count)
    return (input_grad, weight_grad, bias_grad)


def solution(mesh):
    placed = (
        P("chan", ("groups", "lat"), "lon"),
        P("chan", ("groups", "lat"), "lon"),
        P(None, None, "chan", None),
        P("chan"),
    )
    return jax.shard_map(
        local,
        mesh=mesh,
        in_specs=placed,
        out_specs=(
            P("chan", ("groups", "lat"), "lon"),
            P("groups", None, "chan", None),
            P(("groups", "chan")),
        ),
        check_vma=False,
    )
```

```python
import jax
import jax.numpy as jnp
from jax import lax
from jax.sharding import PartitionSpec as P


def padded_2(shard, sides, width):
    for axis, dim in sides:
        devices, length = (lax.axis_size(axis), shard.shape[dim])
        up = [(i, (i + 1) % devices) for i in range(devices)]
        down = [(j, i) for i, j in up]
        last = lax.slice_in_dim(shard, length - width, length, axis=dim)
        initial = lax.slice_in_dim(shard, 0, width, axis=dim)
        before = lax.ppermute(last, axis, up)
        after = lax.ppermute(initial, axis, down)
        shard = jnp.concatenate([before, shard, after], axis=dim)
    return shard


def gelu_slope(preact):
    normal_cdf = 0.5 * (1.0 + jax.scipy.special.erf(preact * 0.7071067811865476))
    density = jnp.exp(-0.5 * preact * preact) * 0.3989422804014327
    return normal_cdf + preact * density


def mask_rims(padded):
    lat_index = lax.axis_index("lat")
    band_count = lax.axis_size("lat")
    row_ids = jnp.arange(padded.shape[1])
    outside = (row_ids == 0) & (lat_index == 0) | (row_ids == padded.shape[1] - 1) & (
        lat_index == band_count - 1
    )
    return jnp.where(outside[None, :, None], jnp.zeros((), padded.dtype), padded)


def window_of(field, first_row, first_col, row_count, column_count):
    return field[
        :, first_row : first_row + row_count, first_col : first_col + column_count
    ].reshape(field.shape[0], -1)


def conv_taps(kernel, field, row_count, column_count, flip):
    total = None
    for tap_row in range(3):
        for tap_col in range(3):
            if flip:
                window = window_of(field, 2 - tap_row, 2 - tap_col, row_count, column_count)
            else:
                window = window_of(field, tap_row, tap_col, row_count, column_count)
            part = jnp.dot(kernel[tap_row, tap_col], window, preferred_element_type=jnp.float32)
            total = part if total is None else total + part
    return total


def direct_reduce_scatter(rows, axis, send_dtype):
    count, index = lax.axis_size(axis), lax.axis_index(axis)
    if count == 1:
        return rows
    chunks = rows.reshape(count, -1, rows.shape[-1])
    acc = lax.dynamic_index_in_dim(chunks, index, keepdims=False)
    for step in range(1, count):
        pairs = [(j, (j + step) % count) for j in range(count)]
        piece = lax.dynamic_index_in_dim(chunks, (index + step) % count, keepdims=False)
        acc = acc + lax.ppermute(piece.astype(send_dtype), axis, pairs).astype(jnp.float32)
    return acc


def direct_all_gather(chunk, axis, send_dtype):
    count, index = lax.axis_size(axis), lax.axis_index(axis)
    if count == 1:
        return chunk
    pieces = [chunk]
    sent = chunk.astype(send_dtype)
    for step in range(1, count):
        pairs = [(j, (j + step) % count) for j in range(count)]
        pieces.append(lax.ppermute(sent, axis, pairs).astype(jnp.float32))
    stacked = jnp.stack(pieces[::-1])
    stacked = jnp.roll(stacked, (index + 1) % count, axis=0)
    return stacked.reshape(-1, chunk.shape[-1])


def sum_start(flat, send_dtype, columns):
    parts = lax.axis_size("lat") * lax.axis_size("lon")
    quantum = parts * 16 * 128
    padded = jnp.pad(flat, (0, (-flat.size) % quantum)).reshape(-1, 128)
    rows = direct_reduce_scatter(padded, "lat", jnp.float32)
    count, index = lax.axis_size("lon"), lax.axis_index("lon")
    last, first = columns
    if count < 3:
        up = [(i, (i + 1) % count) for i in range(count)]
        down = [(j, i) for i, j in up]
        halo = (lax.ppermute(last, "lon", up), lax.ppermute(first, "lon", down))
        return direct_reduce_scatter(rows, "lon", send_dtype), halo
    chunks = rows.reshape(count, -1, rows.shape[-1])
    size = chunks.shape[1]
    acc = lax.dynamic_index_in_dim(chunks, index, keepdims=False)
    extra = {1: last, count - 1: first}
    got = {}
    for step in sorted(range(1, count), key=lambda step: step in extra):
        pairs = [(j, (j + step) % count) for j in range(count)]
        piece = lax.dynamic_index_in_dim(chunks, (index + step) % count, keepdims=False).astype(send_dtype)
        if step in extra:
            piece = jnp.concatenate([piece, extra[step].astype(send_dtype).reshape(-1, rows.shape[-1])], axis=0)
        moved = lax.ppermute(piece, "lon", pairs)
        acc = acc + moved[:size].astype(jnp.float32)
        if step in extra:
            got[step] = moved[size:].reshape(last.shape).astype(last.dtype)
    return acc, (got[1], got[count - 1])


def sum_finish(rows, size, send_dtype):
    rows = direct_all_gather(rows, "lon", send_dtype)
    rows = direct_all_gather(rows, "lat", jnp.float32)
    return rows.reshape(-1)[:size]


def border_of(padded):
    rows, cols = padded.shape[1], padded.shape[2]
    return jnp.concatenate(
        [padded[:, 0, :], padded[:, rows - 1, :], padded[:, 1 : rows - 1, 0], padded[:, 1 : rows - 1, cols - 1]],
        axis=1,
    )


def with_border(field, border):
    rows, cols = field.shape[1], field.shape[2]
    top = border[:, : cols + 2]
    bottom = border[:, cols + 2 : 2 * cols + 4]
    left = border[:, 2 * cols + 4 : 2 * cols + 4 + rows]
    right = border[:, 2 * cols + 4 + rows :]
    middle = jnp.concatenate([left[:, :, None], field, right[:, :, None]], axis=2)
    return jnp.concatenate([top[:, None, :], middle, bottom[:, None, :]], axis=1)


def local(inputs, cotangent, weight, bias_vector):
    own_channels, row_count, column_count = inputs.shape
    chan_count = lax.axis_size("chan")
    chan_index = lax.axis_index("chan")
    raw_blocks = []
    for shift in range(1, chan_count):
        pairs = [(i, (i - shift) % chan_count) for i in range(chan_count)]
        raw_blocks.append(lax.ppermute(inputs, "chan", pairs))
    input_pad = mask_rims(padded_2(inputs, (("lon", 2), ("lat", 1)), 1))
    own_border = border_of(input_pad)
    blocks = [input_pad]
    for shift in range(1, chan_count):
        pairs = [(i, (i - shift) % chan_count) for i in range(chan_count)]
        border = lax.ppermute(own_border, "chan", pairs)
        blocks.append(lax.optimization_barrier(with_border(raw_blocks[shift - 1], border)))
    kernel_cols = []
    for shift in range(chan_count):
        source = (chan_index + shift) % chan_count
        kernel_cols.append(
            lax.dynamic_slice_in_dim(weight, source * own_channels, own_channels, axis=3)
        )
    preact = None
    for shift in range(chan_count):
        part = conv_taps(kernel_cols[shift], blocks[shift], row_count, column_count, False)
        preact = part if preact is None else preact + part
    preact = preact + bias_vector[:, None]
    upstream = cotangent.reshape(own_channels, -1).astype(jnp.float32)
    grad_pre = (upstream * gelu_slope(preact)).astype(jnp.bfloat16)
    bias_part = jnp.sum(grad_pre.astype(jnp.float32), axis=1)
    input_local = jnp.concatenate(blocks, axis=0)
    taps = []
    for tap_row in range(3):
        row_taps = []
        for tap_col in range(3):
            window = window_of(input_local, tap_row, tap_col, row_count, column_count)
            row_taps.append(
                lax.dot_general(
                    grad_pre, window, (((1,), (1,)), ((), ())), preferred_element_type=jnp.float32
                )
            )
        taps.append(jnp.stack(row_taps))
    weight_part = jnp.stack(taps)
    flat = jnp.concatenate([weight_part.reshape(-1), bias_part])
    grad_field = grad_pre.reshape(own_channels, row_count, column_count)
    edges = (grad_field[:, :, column_count - 1 :], grad_field[:, :, :1])
    scattered, (before, after) = sum_start(flat, jnp.bfloat16, edges)
    flat = sum_finish(scattered, flat.size, jnp.bfloat16)
    weight_local = flat[: weight_part.size].reshape(weight_part.shape)
    bias_grad = flat[weight_part.size :]
    doubled = jnp.concatenate([weight_local, weight_local], axis=3)
    weight_grad = lax.dynamic_slice_in_dim(
        doubled, (chan_count - chan_index) % chan_count * own_channels, chan_count * own_channels, axis=3
    )
    grad_wide = jnp.concatenate([before, grad_field, after], axis=2)
    grad_pad = mask_rims(padded_2(grad_wide, (("lat", 1),), 1))
    outgoing = []
    for shift in range(1, chan_count):
        kernel_t = jnp.swapaxes(kernel_cols[shift], 2, 3)
        outgoing.append(conv_taps(kernel_t, grad_pad, row_count, column_count, True).astype(jnp.bfloat16))
    grad_pad, outgoing = lax.optimization_barrier((grad_pad, outgoing))
    received = []
    for shift in range(1, chan_count):
        pairs = [(i, (i + shift) % chan_count) for i in range(chan_count)]
        received.append(lax.ppermute(outgoing[shift - 1], "chan", pairs))
    own_part = conv_taps(jnp.swapaxes(kernel_cols[0], 2, 3), grad_pad, row_count, column_count, True)
    own_part, weight_grad, bias_grad = lax.optimization_barrier((own_part, weight_grad, bias_grad))
    for piece in received:
        own_part = own_part + piece.astype(jnp.float32)
    input_grad = own_part.astype(jnp.bfloat16).reshape(own_channels, row_count, column_count)
    return (input_grad, weight_grad, bias_grad)


def solution(mesh):
    placed = (
        P("chan", ("groups", "lat"), "lon"),
        P("chan", ("groups", "lat"), "lon"),
        P(None, None, "chan", None),
        P("chan"),
    )
    return jax.shard_map(
        local,
        mesh=mesh,
        in_specs=placed,
        out_specs=(
            P("chan", ("groups", "lat"), "lon"),
            P("groups", None, "chan", None),
            P(("groups", "chan")),
        ),
        check_vma=False,
    )
```

```python
import jax
import jax.numpy as jnp
from jax import lax
from jax.sharding import PartitionSpec as P


def padded_2(shard, sides, width):
    for axis, dim in sides:
        devices, length = (lax.axis_size(axis), shard.shape[dim])
        up = [(i, (i + 1) % devices) for i in range(devices)]
        down = [(j, i) for i, j in up]
        last = lax.slice_in_dim(shard, length - width, length, axis=dim)
        initial = lax.slice_in_dim(shard, 0, width, axis=dim)
        before = lax.ppermute(last, axis, up)
        after = lax.ppermute(initial, axis, down)
        shard = jnp.concatenate([before, shard, after], axis=dim)
    return shard


def gelu_slope(preact):
    normal_cdf = 0.5 * (1.0 + jax.scipy.special.erf(preact * 0.7071067811865476))
    density = jnp.exp(-0.5 * preact * preact) * 0.3989422804014327
    return normal_cdf + preact * density


def mask_rims(padded):
    lat_index = lax.axis_index("lat")
    band_count = lax.axis_size("lat")
    row_ids = jnp.arange(padded.shape[1])
    outside = (row_ids == 0) & (lat_index == 0) | (row_ids == padded.shape[1] - 1) & (
        lat_index == band_count - 1
    )
    return jnp.where(outside[None, :, None], jnp.zeros((), padded.dtype), padded)


def window_of(field, first_row, first_col, row_count, column_count):
    return field[
        :, first_row : first_row + row_count, first_col : first_col + column_count
    ].reshape(field.shape[0], -1)


def conv_taps(kernel, field, row_count, column_count, flip):
    total = None
    for tap_row in range(3):
        for tap_col in range(3):
            if flip:
                window = window_of(field, 2 - tap_row, 2 - tap_col, row_count, column_count)
            else:
                window = window_of(field, tap_row, tap_col, row_count, column_count)
            part = jnp.dot(kernel[tap_row, tap_col], window, preferred_element_type=jnp.float32)
            total = part if total is None else total + part
    return total


def direct_reduce_scatter(rows, axis, send_dtype):
    count, index = lax.axis_size(axis), lax.axis_index(axis)
    if count == 1:
        return rows
    chunks = rows.reshape(count, -1, rows.shape[-1])
    acc = lax.dynamic_index_in_dim(chunks, index, keepdims=False)
    for step in range(1, count):
        pairs = [(j, (j + step) % count) for j in range(count)]
        piece = lax.dynamic_index_in_dim(chunks, (index + step) % count, keepdims=False)
        acc = acc + lax.ppermute(piece.astype(send_dtype), axis, pairs).astype(jnp.float32)
    return acc


def direct_all_gather(chunk, axis, send_dtype):
    count, index = lax.axis_size(axis), lax.axis_index(axis)
    if count == 1:
        return chunk
    pieces = [chunk]
    sent = chunk.astype(send_dtype)
    for step in range(1, count):
        pairs = [(j, (j + step) % count) for j in range(count)]
        pieces.append(lax.ppermute(sent, axis, pairs).astype(jnp.float32))
    stacked = jnp.stack(pieces[::-1])
    stacked = jnp.roll(stacked, (index + 1) % count, axis=0)
    return stacked.reshape(-1, chunk.shape[-1])


def sum_start(flat, send_dtype, columns):
    parts = lax.axis_size("lat") * lax.axis_size("lon")
    quantum = parts * 16 * 128
    padded = jnp.pad(flat, (0, (-flat.size) % quantum)).reshape(-1, 128)
    rows = direct_reduce_scatter(padded, "lat", send_dtype)
    count, index = lax.axis_size("lon"), lax.axis_index("lon")
    last, first = columns
    if count < 3:
        up = [(i, (i + 1) % count) for i in range(count)]
        down = [(j, i) for i, j in up]
        halo = (lax.ppermute(last, "lon", up), lax.ppermute(first, "lon", down))
        return direct_reduce_scatter(rows, "lon", send_dtype), halo
    chunks = rows.reshape(count, -1, rows.shape[-1])
    size = chunks.shape[1]
    acc = lax.dynamic_index_in_dim(chunks, index, keepdims=False)
    extra = {1: last, count - 1: first}
    got = {}
    for step in range(1, count):
        pairs = [(j, (j + step) % count) for j in range(count)]
        piece = lax.dynamic_index_in_dim(chunks, (index + step) % count, keepdims=False).astype(send_dtype)
        if step in extra:
            piece = jnp.concatenate([piece, extra[step].astype(send_dtype).reshape(-1, rows.shape[-1])], axis=0)
        moved = lax.ppermute(piece, "lon", pairs)
        acc = acc + moved[:size].astype(jnp.float32)
        if step in extra:
            got[step] = moved[size:].reshape(last.shape).astype(last.dtype)
    return acc, (got[1], got[count - 1])


def sum_finish(rows, size, send_dtype):
    rows = direct_all_gather(rows, "lon", send_dtype)
    rows = direct_all_gather(rows, "lat", jnp.float32)
    return rows.reshape(-1)[:size]


def border_of(padded):
    rows, cols = padded.shape[1], padded.shape[2]
    return jnp.concatenate(
        [padded[:, 0, :], padded[:, rows - 1, :], padded[:, 1 : rows - 1, 0], padded[:, 1 : rows - 1, cols - 1]],
        axis=1,
    )


def with_border(field, border):
    rows, cols = field.shape[1], field.shape[2]
    top = border[:, : cols + 2]
    bottom = border[:, cols + 2 : 2 * cols + 4]
    left = border[:, 2 * cols + 4 : 2 * cols + 4 + rows]
    right = border[:, 2 * cols + 4 + rows :]
    middle = jnp.concatenate([left[:, :, None], field, right[:, :, None]], axis=2)
    return jnp.concatenate([top[:, None, :], middle, bottom[:, None, :]], axis=1)


def local(inputs, cotangent, weight, bias_vector):
    own_channels, row_count, column_count = inputs.shape
    chan_count = lax.axis_size("chan")
    chan_index = lax.axis_index("chan")
    raw_blocks = []
    for shift in range(1, chan_count):
        pairs = [(i, (i - shift) % chan_count) for i in range(chan_count)]
        raw_blocks.append(lax.ppermute(inputs, "chan", pairs))
    input_pad = mask_rims(padded_2(inputs, (("lon", 2), ("lat", 1)), 1))
    own_border = border_of(input_pad)
    blocks = [input_pad]
    for shift in range(1, chan_count):
        pairs = [(i, (i - shift) % chan_count) for i in range(chan_count)]
        border = lax.ppermute(own_border, "chan", pairs)
        blocks.append(lax.optimization_barrier(with_border(raw_blocks[shift - 1], border)))
    kernel_cols = []
    for shift in range(chan_count):
        source = (chan_index + shift) % chan_count
        kernel_cols.append(
            lax.dynamic_slice_in_dim(weight, source * own_channels, own_channels, axis=3)
        )
    preact = None
    for shift in range(chan_count):
        part = conv_taps(kernel_cols[shift], blocks[shift], row_count, column_count, False)
        preact = part if preact is None else preact + part
    preact = preact + bias_vector[:, None]
    upstream = cotangent.reshape(own_channels, -1).astype(jnp.float32)
    grad_pre = (upstream * gelu_slope(preact)).astype(jnp.bfloat16)
    bias_part = jnp.sum(grad_pre.astype(jnp.float32), axis=1)
    input_local = jnp.concatenate(blocks, axis=0)
    taps = []
    for tap_row in range(3):
        row_taps = []
        for tap_col in range(3):
            window = window_of(input_local, tap_row, tap_col, row_count, column_count)
            row_taps.append(
                lax.dot_general(
                    grad_pre, window, (((1,), (1,)), ((), ())), preferred_element_type=jnp.float32
                )
            )
        taps.append(jnp.stack(row_taps))
    weight_part = jnp.stack(taps)
    flat = jnp.concatenate([weight_part.reshape(-1), bias_part])
    grad_field = grad_pre.reshape(own_channels, row_count, column_count)
    edges = (grad_field[:, :, column_count - 1 :], grad_field[:, :, :1])
    scattered, (before, after) = sum_start(flat, jnp.bfloat16, edges)
    flat = sum_finish(scattered, flat.size, jnp.bfloat16)
    weight_local = flat[: weight_part.size].reshape(weight_part.shape)
    bias_grad = flat[weight_part.size :]
    doubled = jnp.concatenate([weight_local, weight_local], axis=3)
    weight_grad = lax.dynamic_slice_in_dim(
        doubled, (chan_count - chan_index) % chan_count * own_channels, chan_count * own_channels, axis=3
    )
    grad_wide = jnp.concatenate([before, grad_field, after], axis=2)
    grad_pad = mask_rims(padded_2(grad_wide, (("lat", 1),), 1))
    outgoing = []
    for shift in range(1, chan_count):
        kernel_t = jnp.swapaxes(kernel_cols[shift], 2, 3)
        outgoing.append(conv_taps(kernel_t, grad_pad, row_count, column_count, True).astype(jnp.bfloat16))
    grad_pad, outgoing = lax.optimization_barrier((grad_pad, outgoing))
    received = []
    for shift in range(1, chan_count):
        pairs = [(i, (i + shift) % chan_count) for i in range(chan_count)]
        received.append(lax.ppermute(outgoing[shift - 1], "chan", pairs))
    own_part = conv_taps(jnp.swapaxes(kernel_cols[0], 2, 3), grad_pad, row_count, column_count, True)
    own_part, weight_grad, bias_grad = lax.optimization_barrier((own_part, weight_grad, bias_grad))
    for piece in received:
        own_part = own_part + piece.astype(jnp.float32)
    input_grad = own_part.astype(jnp.bfloat16).reshape(own_channels, row_count, column_count)
    return (input_grad, weight_grad, bias_grad)


def solution(mesh):
    placed = (
        P("chan", ("groups", "lat"), "lon"),
        P("chan", ("groups", "lat"), "lon"),
        P(None, None, "chan", None),
        P("chan"),
    )
    return jax.shard_map(
        local,
        mesh=mesh,
        in_specs=placed,
        out_specs=(
            P("chan", ("groups", "lat"), "lon"),
            P("groups", None, "chan", None),
            P(("groups", "chan")),
        ),
        check_vma=False,
    )
```
